32 devices in a mesh: dp: 8 (over z, core), tensor: 4 (over y, x).
Axes of the slice: x: 2, y: 2, z: 4, core: 2. Of those that a mesh axis runs over, the one named last changes fastest.
Arguments:
- t_index: int32 [8], P('dp'), may hold values from 0 to 999
- cond_slot: int32 [8], P('dp'), may hold values from 0 to 1
- positions: int32 [8, 3, 512], P('dp'), may hold values from 0 to 63, as said below
- latent: bfloat16 [8, 512, 5120], P('dp', 'tensor'), may hold values from -6 to 6
- teacher_query: bfloat16 [2, 8, 512, 4096], P(None, 'dp', None, 'tensor'), may hold values from -6 to 6
- teacher_key: bfloat16 [2, 8, 512, 4096], P(None, 'dp', None, 'tensor'), may hold values from -6 to 6
- teacher_value: bfloat16 [2, 8, 512, 4096], P(None, 'dp', None, 'tensor'), may hold values from -6 to 6
- student_query: bfloat16 [8, 512, 4096], P('dp', 'tensor'), may hold values from -6 to 6
- student_key: bfloat16 [8, 512, 4096], P('dp', 'tensor'), may hold values from -6 to 6
- student_value: bfloat16 [8, 512, 4096], P('dp', 'tensor'), may hold values from -6 to 6
- query_tangent: bfloat16 [8, 512, 4096], P('dp', 'tensor'), may hold values from -6 to 6
- key_tangent: bfloat16 [8, 512, 4096], P('dp', 'tensor'), may hold values from -6 to 6
- value_tangent: bfloat16 [8, 512, 4096], P('dp', 'tensor'), may hold values from -6 to 6
- teacher_out: bfloat16 [4096, 5120], P('tensor', 'dp'), may hold values from -0.375 to 0.375
- student_out: bfloat16 [4096, 5120], P('tensor', 'dp'), may hold values from -0.375 to 0.375
Outputs:
- target: bfloat16 [8, 512, 5120], P('dp', 'tensor')
- gradient: float32 [4096, 5120], P('tensor', 'dp')
The draws below stay inside these ranges and needn't reach their ends.
Inputs may be any that keep to these rules, and one draw needn't show every extreme that they name: `positions`: within each clip, tokens 64 m and 64 m + 1 have equal coordinates on all three axes.
All inputs are finite; a program needn't handle non-finite values.
Results may differ from the reference program's by a relative error of at most 0.015.
Values may be sent and summed in bfloat16 or wider, within the bound.
No kernel may reach another device: no remote copies, remote signals or barrier semaphores. Data moves between devices by JAX's collectives and lax.ppermute only.
A program may use at most 192 MiB of HBM per device.

```python
import math
import jax
import jax.numpy as jnp
from jax import lax

D = 5120
HD = 128
HEADS = 32
STEPS = 1000
SEQ = 512
CLIPS = 8
INNER = 4096
N_TENSOR = 4


def drawn_pair(key, leading):
    shape = leading + (SEQ, HEADS * HD)
    query_key = jax.random.fold_in(key, 1)
    keys_key = jax.random.fold_in(key, 2)
    queries = 1.4 * jax.random.truncated_normal(query_key, -4.0, 4.0, shape, jnp.float32)
    key_rows = 1.4 * jax.random.truncated_normal(keys_key, -4.0, 4.0, shape, jnp.float32)
    return (queries, key_rows)


def draw_teacher_query(key, part):
    return drawn_pair(jax.random.fold_in(key, 7), (2, CLIPS))[0].astype(jnp.bfloat16)


def draw_teacher_key(key, part):
    return drawn_pair(jax.random.fold_in(key, 7), (2, CLIPS))[1].astype(jnp.bfloat16)


def draw_student_query(key, part):
    return drawn_pair(jax.random.fold_in(key, 11), (CLIPS,))[0].astype(jnp.bfloat16)


def draw_student_key(key, part):
    return drawn_pair(jax.random.fold_in(key, 11), (CLIPS,))[1].astype(jnp.bfloat16)


def draw_positions(key, part):
    coords = jax.random.randint(jax.random.fold_in(key, 5), (CLIPS, 3, SEQ), 0, 64)
    token = jnp.arange(SEQ)
    coords = jnp.where((token % 64 == 1)[None, None, :], jnp.roll(coords, 1, axis=2), coords)
    coords = jnp.where((token == SEQ - 1)[None, None, :], 63, coords)
    return coords.astype(jnp.int32)


def touch_ends(drawn, own_key, low, top_value):
    shape = drawn.shape
    spot = [jax.random.randint(jax.random.fold_in(own_key, axis), (), 0, shape[axis]) for axis in range(len(shape))]
    drawn = drawn.at[tuple(spot)].set(low)
    longest = shape.index(max(shape))
    spot[longest] = (spot[longest] + 1) % shape[longest]
    return drawn.at[tuple(spot)].set(top_value)


def with_spikes(values, stream_key, source, target, blocks, factor):
    def block_of(dim):
        return (jnp.arange(values.shape[dim]) // (values.shape[dim] // blocks)).reshape((-1,) + (1,) * (values.ndim - 1 - dim))

    first = jax.random.permutation(stream_key, blocks)[block_of(target)]
    other_side = (block_of(target) + blocks // 2) % blocks
    return jnp.where((block_of(source) == first) | (block_of(source) == other_side), factor * values, values)


def block_scale(rng, extent, split, least, top_value):
    level = 1.0
    for axis_at, blocks in split:
        heights = jax.random.uniform(jax.random.fold_in(jax.random.fold_in(rng, 6), axis_at), (blocks,), jnp.float32, least / len(split), top_value / len(split))
        level = level * jnp.repeat(jnp.exp(heights), extent[axis_at] // blocks).reshape((-1,) + (1,) * (len(extent) - 1 - axis_at))
    return level


def scatter_about(rng, extent, deviation, bound, pieces=(), dtype=jnp.bfloat16):
    drawn = jax.random.normal(rng, extent, jnp.float32) * deviation
    if len(pieces) > 0:
        drawn = block_scale(rng, extent, pieces, -0.22, 0.18) * drawn
    return jnp.clip(drawn, min=-bound, max=bound).astype(dtype)


def heavy_noise(stream_key, dims, deviation, reach, pieces, heavy, kind=jnp.bfloat16):
    result = deviation * jax.random.normal(stream_key, dims, jnp.float32)
    if pieces:
        result = result * block_scale(stream_key, dims, pieces, -0.22, 0.18)
    return jnp.clip(with_spikes(result, jax.random.fold_in(stream_key, 3), *heavy), -reach, reach).astype(kind)


def setup_inputs(seed: int = 0) -> dict:
    keys = jax.random.split(jax.random.key(seed), 16)
    t_index = touch_ends(jax.random.randint(keys[0], (CLIPS,), 0, STEPS), jax.random.fold_in(keys[0], 1), 0, STEPS - 1).astype(jnp.int32)
    cond_slot = touch_ends(jax.random.randint(keys[1], (CLIPS,), 0, 2), jax.random.fold_in(keys[1], 1), 0, 1).astype(jnp.int32)
    positions = draw_positions(jax.random.fold_in(keys[15], 71), 0)
    latent = heavy_noise(keys[3], (CLIPS, SEQ, D), 1.0, 6.0, ((0, 8), (1, 4)), (0, 2, 8, 2.0))
    teacher_query = draw_teacher_query(jax.random.fold_in(keys[15], 71), 0)
    teacher_key = draw_teacher_key(jax.random.fold_in(keys[15], 71), 0)
    teacher_value = scatter_about(keys[6], (2, CLIPS, SEQ, INNER), 1.0, 6.0, ((1, 8), (3, 4)))
    student_query = draw_student_query(jax.random.fold_in(keys[15], 71), 0)
    student_key = draw_student_key(jax.random.fold_in(keys[15], 71), 0)
    student_value = scatter_about(keys[9], (CLIPS, SEQ, INNER), 1.0, 6.0, ((0, 8), (1, 4)))
    query_tangent = scatter_about(keys[10], (CLIPS, SEQ, INNER), 1.0, 6.0, ((0, 8), (1, 4)))
    key_tangent = scatter_about(keys[11], (CLIPS, SEQ, INNER), 1.0, 6.0, ((0, 8), (1, 4)))
    value_tangent = scatter_about(keys[12], (CLIPS, SEQ, INNER), 1.0, 6.0, ((0, 8), (1, 4)))
    teacher_out = scatter_about(keys[13], (INNER, D), 0.0625, 0.375, ((0, 4), (1, 8)))
    student_out = scatter_about(keys[14], (INNER, D), 0.0625, 0.375, ((0, 4), (1, 8)))
    return dict(t_index=t_index, cond_slot=cond_slot, positions=positions, latent=latent, teacher_query=teacher_query, teacher_key=teacher_key, teacher_value=teacher_value, student_query=student_query, student_key=student_key, student_value=student_value, query_tangent=query_tangent, key_tangent=key_tangent, value_tangent=value_tangent, teacher_out=teacher_out, student_out=student_out)


sigma_data = 0.5
guidance = 5.0

def rope_angles(coords):
    half_size = HD // 2
    sixth = HD // 6
    first_pairs = half_size - 2 * sixth
    pair_index = jnp.arange(half_size)
    axis_id = (pair_index >= first_pairs).astype(jnp.int32) + (pair_index >= first_pairs + sixth).astype(jnp.int32)
    offset = jnp.where(axis_id == 0, 0, jnp.where(axis_id == 1, first_pairs, first_pairs + sixth))
    axis_width = jnp.where(axis_id == 0, 2 * first_pairs, 2 * sixth)
    exponent = 2.0 * (pair_index - offset).astype(jnp.float32) / axis_width.astype(jnp.float32)
    frequency = jnp.exp(-exponent * math.log(10000.0))
    angles = jnp.zeros((coords.shape[1], half_size), jnp.float32)
    for which_axis in range(3):
        chosen = jnp.where(axis_id == which_axis, frequency, 0.0)
        angles = angles + coords[which_axis].astype(jnp.float32)[:, None] * chosen[None, :]
    return angles

def rotate_heads(source, angles):
    half_size = source.shape[-1] // 2
    cos_angle = jnp.cos(angles)[:, None, :]
    sin_angle = jnp.sin(angles)[:, None, :]
    front_half = source[..., :half_size]
    back_half = source[..., half_size:]
    return jnp.concatenate([front_half * cos_angle - back_half * sin_angle, back_half * cos_angle + front_half * sin_angle], axis=-1)

def softmax_rows(scores):
    row_peak = lax.optimization_barrier(jnp.max(scores, axis=-1, keepdims=True))
    exponent = jnp.exp(scores - row_peak)
    return exponent / lax.optimization_barrier(jnp.sum(exponent, axis=-1, keepdims=True))

def attend_plain(queries, key_rows, value_rows):
    scores = jnp.einsum('qhd,khd->hqk', queries.astype(jnp.float32), key_rows.astype(jnp.float32)) * HD ** (-0.5)
    weights = softmax_rows(scores)
    rounded = weights.astype(jnp.bfloat16)
    return jnp.einsum('hqk,khd->qhd', rounded.astype(jnp.float32), value_rows.astype(jnp.float32))

def attend_tangent(queries, key_rows, value_rows, query_dir, key_dir, value_dir):
    score_scale = HD ** (-0.5)
    scores = jnp.einsum('qhd,khd->hqk', queries.astype(jnp.float32), key_rows.astype(jnp.float32)) * score_scale
    weights = softmax_rows(scores)
    rounded = weights.astype(jnp.bfloat16)
    primal = jnp.einsum('hqk,khd->qhd', rounded.astype(jnp.float32), value_rows.astype(jnp.float32))
    score_dir = (jnp.einsum('qhd,khd->hqk', query_dir.astype(jnp.float32), key_rows.astype(jnp.float32)) + jnp.einsum('qhd,khd->hqk', queries.astype(jnp.float32), key_dir.astype(jnp.float32))) * score_scale
    weight_dir = weights * (score_dir - lax.optimization_barrier(jnp.sum(weights * score_dir, axis=-1, keepdims=True)))
    rounded_dir = weight_dir.astype(jnp.bfloat16)
    tangent = jnp.einsum('hqk,khd->qhd', rounded_dir.astype(jnp.float32), value_rows.astype(jnp.float32)) + jnp.einsum('hqk,khd->qhd', rounded.astype(jnp.float32), value_dir.astype(jnp.float32))
    return (primal, tangent)

def reference(t_index, cond_slot, positions, latent, teacher_query, teacher_key, teacher_value, student_query, student_key, student_value, query_tangent, key_tangent, value_tangent, teacher_out, student_out):
    grad_scale = -2.0 / math.sqrt(CLIPS * SEQ)
    groups = N_TENSOR
    group_width = INNER // groups
    student_groups = student_out.reshape(groups, group_width, D).astype(jnp.float32)
    teacher_groups = teacher_out.reshape(groups, group_width, D).astype(jnp.float32)

    def split_heads(source):
        return source.reshape(SEQ, HEADS, HD)

    def rotated(source, angles):
        return rotate_heads(split_heads(source).astype(jnp.float32), angles).astype(jnp.bfloat16)

    def clip_step(running, inputs):
        time_index, cond_index, coords, latent_rows, t_query, t_key, t_value, s_query, s_key, s_value, q_dir, k_dir, v_dir = inputs
        time_value = 0.2 + 1.2 * (time_index.astype(jnp.float32) + 0.5) / STEPS
        cos_time = jnp.cos(time_value)
        sin_time = jnp.sin(time_value)
        angles = rope_angles(coords)
        outputs = []
        for stream in range(2):
            outputs.append(attend_plain(rotated(t_query[stream], angles), rotated(t_key[stream], angles), split_heads(t_value[stream])))
        cond_out = jnp.where(cond_index == 0, outputs[0], outputs[1])
        uncond_out = jnp.where(cond_index == 0, outputs[1], outputs[0])
        teacher_term = (cos_time * cos_time * sigma_data * (uncond_out + guidance * (cond_out - uncond_out))).astype(jnp.bfloat16).reshape(SEQ, INNER)
        primal, tangent = attend_tangent(rotated(s_query, angles), rotated(s_key, angles), split_heads(s_value), rotated(q_dir, angles), rotated(k_dir, angles), split_heads(v_dir))
        student_term = (-(cos_time * cos_time) * sigma_data * primal - cos_time * sin_time * sigma_data * tangent).astype(jnp.bfloat16).reshape(SEQ, INNER)
        attended = primal.astype(jnp.bfloat16).reshape(SEQ, INNER)
        split_student = student_term.reshape(SEQ, groups, group_width).astype(jnp.float32)
        split_teacher = teacher_term.reshape(SEQ, groups, group_width).astype(jnp.float32)
        partial_value = jnp.einsum('sgi,gid->gsd', split_student, student_groups) + jnp.einsum('sgi,gid->gsd', split_teacher, teacher_groups)
        partial_value = lax.optimization_barrier(partial_value.astype(jnp.bfloat16))
        velocity = lax.optimization_barrier(jnp.sum(partial_value.astype(jnp.float32), axis=0))
        target = (velocity - cos_time * sin_time * latent_rows.astype(jnp.float32)).astype(jnp.bfloat16)
        term = (grad_scale * jnp.dot(attended.T, target, preferred_element_type=jnp.float32)).astype(jnp.bfloat16)
        term = lax.optimization_barrier(term)
        return (running + term.astype(jnp.float32), target)
    start_grad = jnp.zeros((INNER, D), jnp.float32)
    inputs = (t_index, cond_slot, positions, latent, jnp.moveaxis(teacher_query, 1, 0), jnp.moveaxis(teacher_key, 1, 0), jnp.moveaxis(teacher_value, 1, 0), student_query, student_key, student_value, query_tangent, key_tangent, value_tangent)
    gradient, target = lax.scan(clip_step, start_grad, inputs)
    return (target, gradient)
```

```python
import math

import jax
import jax.numpy as jnp
from jax import lax
from jax.sharding import PartitionSpec as P

HD = 128
STEPS = 1000


sigma_data = 0.5
guidance = 5.0


def rope_angles(coords):
    half_size = HD // 2
    sixth = HD // 6
    first_pairs = half_size - 2 * sixth
    pair_index = jnp.arange(half_size)
    axis_id = (pair_index >= first_pairs).astype(jnp.int32) + (
        pair_index >= first_pairs + sixth
    ).astype(jnp.int32)
    offset = jnp.where(axis_id == 0, 0, jnp.where(axis_id == 1, first_pairs, first_pairs + sixth))
    axis_width = jnp.where(axis_id == 0, 2 * first_pairs, 2 * sixth)
    exponent = 2.0 * (pair_index - offset).astype(jnp.float32) / axis_width.astype(jnp.float32)
    frequency = jnp.exp(-exponent * math.log(10000.0))
    angles = jnp.zeros((coords.shape[1], half_size), jnp.float32)
    for which_axis in range(3):
        chosen = jnp.where(axis_id == which_axis, frequency, 0.0)
        angles = angles + coords[which_axis].astype(jnp.float32)[:, None] * chosen[None, :]
    return angles


def rotate_heads(source, angles):
    half_size = source.shape[-1] // 2
    cos_angle = jnp.cos(angles)[:, None, :]
    sin_angle = jnp.sin(angles)[:, None, :]
    front_half = source[..., :half_size]
    back_half = source[..., half_size:]
    return jnp.concatenate(
        [
            front_half * cos_angle - back_half * sin_angle,
            back_half * cos_angle + front_half * sin_angle,
        ],
        axis=-1,
    )


def split_heads(source):
    return source.reshape(source.shape[0], -1, HD)


def rotated(source, angles):
    row_count = source.shape[0]
    return (
        rotate_heads(split_heads(source).astype(jnp.float32), angles)
        .astype(jnp.bfloat16)
        .reshape(row_count, -1)
    )


def softmax_rows(scores):
    row_peak = jnp.max(scores, axis=-1, keepdims=True)
    exponent = jnp.exp(scores - row_peak)
    return exponent / jnp.sum(exponent, axis=-1, keepdims=True)


def attend_plain(queries, key_rows, value_rows):
    scores = jnp.einsum(
        "qhd,khd->hqk", queries, key_rows, preferred_element_type=jnp.float32
    ) * HD ** (-0.5)
    rounded = softmax_rows(scores).astype(jnp.bfloat16)
    return jnp.einsum("hqk,khd->qhd", rounded, value_rows, preferred_element_type=jnp.float32)


def attend_tangent(queries, key_rows, value_rows, query_dir, key_dir, value_dir):
    score_scale = HD ** (-0.5)
    scores = (
        jnp.einsum("qhd,khd->hqk", queries, key_rows, preferred_element_type=jnp.float32)
        * score_scale
    )
    weights = softmax_rows(scores)
    rounded = weights.astype(jnp.bfloat16)
    primal = jnp.einsum("hqk,khd->qhd", rounded, value_rows, preferred_element_type=jnp.float32)
    score_dir = (
        jnp.einsum("qhd,khd->hqk", query_dir, key_rows, preferred_element_type=jnp.float32)
        + jnp.einsum("qhd,khd->hqk", queries, key_dir, preferred_element_type=jnp.float32)
    ) * score_scale
    weight_dir = weights * (score_dir - jnp.sum(weights * score_dir, axis=-1, keepdims=True))
    rounded_dir = weight_dir.astype(jnp.bfloat16)
    tangent = jnp.einsum(
        "hqk,khd->qhd", rounded_dir, value_rows, preferred_element_type=jnp.float32
    ) + jnp.einsum("hqk,khd->qhd", rounded, value_dir, preferred_element_type=jnp.float32)
    return (primal, tangent)


def local(
    t_index,
    cond_slot,
    positions,
    latent,
    teacher_query,
    teacher_key,
    teacher_value,
    student_query,
    student_key,
    student_value,
    query_tangent,
    key_tangent,
    value_tangent,
    teacher_out,
    student_out,
):
    groups = lax.axis_size("tensor")
    seq_local = latent.shape[1]
    seq_whole = seq_local * groups
    row_start = lax.axis_index("tensor") * seq_local
    time_value = 0.2 + 1.2 * (t_index[0].astype(jnp.float32) + 0.5) / STEPS
    cos_time = jnp.cos(time_value)
    sin_time = jnp.sin(time_value)
    angles_whole = rope_angles(positions[0])
    angles_local = lax.dynamic_slice_in_dim(angles_whole, row_start, seq_local, 0)
    outgoing = (
        rotated(student_query[0], angles_local),
        rotated(student_key[0], angles_local),
        student_value[0],
        rotated(query_tangent[0], angles_local),
        rotated(key_tangent[0], angles_local),
        value_tangent[0],
    )
    arrived = (
        lax.all_to_all(outgoing[0], "tensor", split_axis=1, concat_axis=0, tiled=True),
        lax.all_to_all(outgoing[1], "tensor", split_axis=1, concat_axis=0, tiled=True),
        lax.all_to_all(outgoing[2], "tensor", split_axis=1, concat_axis=0, tiled=True),
        lax.all_to_all(outgoing[3], "tensor", split_axis=1, concat_axis=0, tiled=True),
        lax.all_to_all(outgoing[4], "tensor", split_axis=1, concat_axis=0, tiled=True),
        lax.all_to_all(outgoing[5], "tensor", split_axis=1, concat_axis=0, tiled=True),
    )
    outputs = []
    for stream in range(2):
        outputs.append(
            attend_plain(
                split_heads(rotated(teacher_query[stream, 0], angles_whole)),
                split_heads(rotated(teacher_key[stream, 0], angles_whole)),
                split_heads(teacher_value[stream, 0]),
            )
        )
    cond_index = cond_slot[0]
    cond_out = jnp.where(cond_index == 0, outputs[0], outputs[1])
    uncond_out = jnp.where(cond_index == 0, outputs[1], outputs[0])
    teacher_term = (
        (cos_time * cos_time * sigma_data * (uncond_out + guidance * (cond_out - uncond_out)))
        .astype(jnp.bfloat16)
        .reshape(seq_whole, -1)
    )
    primal, tangent = attend_tangent(
        split_heads(arrived[0]),
        split_heads(arrived[1]),
        split_heads(arrived[2]),
        split_heads(arrived[3]),
        split_heads(arrived[4]),
        split_heads(arrived[5]),
    )
    student_term = (
        (-(cos_time * cos_time) * sigma_data * primal - cos_time * sin_time * sigma_data * tangent)
        .astype(jnp.bfloat16)
        .reshape(seq_whole, -1)
    )
    attended = primal.astype(jnp.bfloat16).reshape(seq_whole, -1)
    stacked = jnp.stack([student_out, teacher_out])
    pieces = lax.all_gather(stacked, "dp", axis=2, tiled=True)
    partial_value = jnp.dot(student_term, pieces[0], preferred_element_type=jnp.float32) + jnp.dot(
        teacher_term, pieces[1], preferred_element_type=jnp.float32
    )
    latent_weight = cos_time * sin_time
    clips = lax.axis_size("dp")
    copies = jnp.broadcast_to(attended[None], (clips,) + attended.shape)
    attended_all = lax.all_to_all(copies, "dp", split_axis=0, concat_axis=0, tiled=True)
    velocity = lax.psum_scatter(
        partial_value.astype(jnp.bfloat16), "tensor", scatter_dimension=0, tiled=True
    )
    velocity, attended_all = lax.optimization_barrier((velocity, attended_all))
    target = (
        velocity.astype(jnp.float32) - latent_weight * latent[0].astype(jnp.float32)
    ).astype(jnp.bfloat16)
    width = target.shape[1] // clips
    columns = lax.all_to_all(
        target.reshape(seq_local, clips, width), "dp", split_axis=1, concat_axis=1, tiled=True
    )
    columns = lax.all_gather(columns, "tensor", axis=0, tiled=True)
    grad_scale = -2.0 / math.sqrt(clips * seq_whole)
    terms = jnp.einsum(
        "csi,scd->cid", attended_all, columns, preferred_element_type=jnp.float32
    )
    gradient = jnp.sum((grad_scale * terms).astype(jnp.bfloat16).astype(jnp.float32), axis=0)
    return (target[None], gradient)


def solution(mesh):
    placed = (
        P("dp"),
        P("dp"),
        P("dp", None, None),
        P("dp", "tensor", None),
        P(None, "dp", None, "tensor"),
        P(None, "dp", None, "tensor"),
        P(None, "dp", None, "tensor"),
        P("dp", "tensor", None),
        P("dp", "tensor", None),
        P("dp", "tensor", None),
        P("dp", "tensor", None),
        P("dp", "tensor", None),
        P("dp", "tensor", None),
        P("tensor", "dp"),
        P("tensor", "dp"),
    )
    return jax.shard_map(
        local,
        mesh=mesh,
        in_specs=placed,
        out_specs=(P("dp", "tensor", None), P("tensor", "dp")),
        check_vma=False,
    )
```

```python
import math

import jax
import jax.numpy as jnp
from jax import lax
from jax.sharding import PartitionSpec as P

HD = 128
STEPS = 1000


sigma_data = 0.5
guidance = 5.0


def rope_angles(coords):
    half_size = HD // 2
    sixth = HD // 6
    first_pairs = half_size - 2 * sixth
    pair_index = jnp.arange(half_size)
    axis_id = (pair_index >= first_pairs).astype(jnp.int32) + (
        pair_index >= first_pairs + sixth
    ).astype(jnp.int32)
    offset = jnp.where(axis_id == 0, 0, jnp.where(axis_id == 1, first_pairs, first_pairs + sixth))
    axis_width = jnp.where(axis_id == 0, 2 * first_pairs, 2 * sixth)
    exponent = 2.0 * (pair_index - offset).astype(jnp.float32) / axis_width.astype(jnp.float32)
    frequency = jnp.exp(-exponent * math.log(10000.0))
    angles = jnp.zeros((coords.shape[1], half_size), jnp.float32)
    for which_axis in range(3):
        chosen = jnp.where(axis_id == which_axis, frequency, 0.0)
        angles = angles + coords[which_axis].astype(jnp.float32)[:, None] * chosen[None, :]
    return angles


def rotate_heads(source, angles):
    half_size = source.shape[-1] // 2
    cos_angle = jnp.cos(angles)[:, None, :]
    sin_angle = jnp.sin(angles)[:, None, :]
    front_half = source[..., :half_size]
    back_half = source[..., half_size:]
    return jnp.concatenate(
        [
            front_half * cos_angle - back_half * sin_angle,
            back_half * cos_angle + front_half * sin_angle,
        ],
        axis=-1,
    )


def split_heads(source):
    return source.reshape(source.shape[0], -1, HD)


def rotated(source, angles):
    row_count = source.shape[0]
    return (
        rotate_heads(split_heads(source).astype(jnp.float32), angles)
        .astype(jnp.bfloat16)
        .reshape(row_count, -1)
    )


def softmax_rows(scores):
    row_peak = jnp.max(scores, axis=-1, keepdims=True)
    exponent = jnp.exp(scores - row_peak)
    return exponent / jnp.sum(exponent, axis=-1, keepdims=True)


def attend_plain(queries, key_rows, value_rows):
    scores = jnp.einsum(
        "qhd,khd->hqk", queries, key_rows, preferred_element_type=jnp.float32
    ) * HD ** (-0.5)
    rounded = softmax_rows(scores).astype(jnp.bfloat16)
    return jnp.einsum("hqk,khd->qhd", rounded, value_rows, preferred_element_type=jnp.float32)


def attend_tangent(queries, key_rows, value_rows, query_dir, key_dir, value_dir):
    score_scale = HD ** (-0.5)
    scores = (
        jnp.einsum("qhd,khd->hqk", queries, key_rows, preferred_element_type=jnp.float32)
        * score_scale
    )
    weights = softmax_rows(scores)
    rounded = weights.astype(jnp.bfloat16)
    primal = jnp.einsum("hqk,khd->qhd", rounded, value_rows, preferred_element_type=jnp.float32)
    score_dir = (
        jnp.einsum("qhd,khd->hqk", query_dir, key_rows, preferred_element_type=jnp.float32)
        + jnp.einsum("qhd,khd->hqk", queries, key_dir, preferred_element_type=jnp.float32)
    ) * score_scale
    weight_dir = weights * (score_dir - jnp.sum(weights * score_dir, axis=-1, keepdims=True))
    rounded_dir = weight_dir.astype(jnp.bfloat16)
    tangent = jnp.einsum(
        "hqk,khd->qhd", rounded_dir, value_rows, preferred_element_type=jnp.float32
    ) + jnp.einsum("hqk,khd->qhd", rounded, value_dir, preferred_element_type=jnp.float32)
    return (primal, tangent)


def local(
    t_index,
    cond_slot,
    positions,
    latent,
    teacher_query,
    teacher_key,
    teacher_value,
    student_query,
    student_key,
    student_value,
    query_tangent,
    key_tangent,
    value_tangent,
    teacher_out,
    student_out,
):
    groups = lax.axis_size("tensor")
    seq_local = latent.shape[1]
    seq_whole = seq_local * groups
    row_start = lax.axis_index("tensor") * seq_local
    time_value = 0.2 + 1.2 * (t_index[0].astype(jnp.float32) + 0.5) / STEPS
    cos_time = jnp.cos(time_value)
    sin_time = jnp.sin(time_value)
    angles_whole = rope_angles(positions[0])
    angles_local = lax.dynamic_slice_in_dim(angles_whole, row_start, seq_local, 0)
    outgoing = (
        rotated(student_query[0], angles_local),
        rotated(student_key[0], angles_local),
        student_value[0],
        rotated(query_tangent[0], angles_local),
        rotated(key_tangent[0], angles_local),
        value_tangent[0],
    )
    arrived = (
        lax.all_to_all(outgoing[0], "tensor", split_axis=1, concat_axis=0, tiled=True),
        lax.all_to_all(outgoing[1], "tensor", split_axis=1, concat_axis=0, tiled=True),
        lax.all_to_all(outgoing[2], "tensor", split_axis=1, concat_axis=0, tiled=True),
        lax.all_to_all(outgoing[3], "tensor", split_axis=1, concat_axis=0, tiled=True),
        lax.all_to_all(outgoing[4], "tensor", split_axis=1, concat_axis=0, tiled=True),
        lax.all_to_all(outgoing[5], "tensor", split_axis=1, concat_axis=0, tiled=True),
    )
    outputs = []
    for stream in range(2):
        outputs.append(
            attend_plain(
                split_heads(rotated(teacher_query[stream, 0], angles_whole)),
                split_heads(rotated(teacher_key[stream, 0], angles_whole)),
                split_heads(teacher_value[stream, 0]),
            )
        )
    cond_index = cond_slot[0]
    cond_out = jnp.where(cond_index == 0, outputs[0], outputs[1])
    uncond_out = jnp.where(cond_index == 0, outputs[1], outputs[0])
    teacher_term = (
        (cos_time * cos_time * sigma_data * (uncond_out + guidance * (cond_out - uncond_out)))
        .astype(jnp.bfloat16)
        .reshape(seq_whole, -1)
    )
    primal, tangent = attend_tangent(
        split_heads(arrived[0]),
        split_heads(arrived[1]),
        split_heads(arrived[2]),
        split_heads(arrived[3]),
        split_heads(arrived[4]),
        split_heads(arrived[5]),
    )
    student_term = (
        (-(cos_time * cos_time) * sigma_data * primal - cos_time * sin_time * sigma_data * tangent)
        .astype(jnp.bfloat16)
        .reshape(seq_whole, -1)
    )
    attended = primal.astype(jnp.bfloat16).reshape(seq_whole, -1)
    stacked = jnp.stack([student_out, teacher_out])
    pieces = lax.all_gather(stacked, "dp", axis=2, tiled=True)
    partial_value = jnp.dot(student_term, pieces[0], preferred_element_type=jnp.float32) + jnp.dot(
        teacher_term, pieces[1], preferred_element_type=jnp.float32
    )
    latent_weight = cos_time * sin_time
    pieces_in = lax.all_to_all(
        partial_value.astype(jnp.bfloat16).reshape(groups, seq_local, -1),
        "tensor",
        split_axis=0,
        concat_axis=0,
        tiled=True,
    )
    velocity = jnp.sum(pieces_in.astype(jnp.float32), axis=0)
    target = (velocity - latent_weight * latent[0].astype(jnp.float32)).astype(jnp.bfloat16)
    clips = lax.axis_size("dp")
    width = target.shape[1] // clips
    attended_all = lax.all_gather(attended, "dp", axis=0, tiled=False)
    columns = lax.all_to_all(
        target.reshape(seq_local, clips, width), "dp", split_axis=1, concat_axis=1, tiled=True
    )
    columns = lax.all_gather(columns, "tensor", axis=0, tiled=True)
    grad_scale = -2.0 / math.sqrt(clips * seq_whole)
    terms = jnp.einsum(
        "csi,scd->cid", attended_all, columns, preferred_element_type=jnp.float32
    )
    gradient = jnp.sum((grad_scale * terms).astype(jnp.bfloat16).astype(jnp.float32), axis=0)
    return (target[None], gradient)


def solution(mesh):
    placed = (
        P("dp"),
        P("dp"),
        P("dp", None, None),
        P("dp", "tensor", None),
        P(None, "dp", None, "tensor"),
        P(None, "dp", None, "tensor"),
        P(None, "dp", None, "tensor"),
        P("dp", "tensor", None),
        P("dp", "tensor", None),
        P("dp", "tensor", None),
        P("dp", "tensor", None),
        P("dp", "tensor", None),
        P("dp", "tensor", None),
        P("tensor", "dp"),
        P("tensor", "dp"),
    )
    return jax.shard_map(
        local,
        mesh=mesh,
        in_specs=placed,
        out_specs=(P("dp", "tensor", None), P("tensor", "dp")),
        check_vma=False,
    )
```

```python
import math

import jax
import jax.numpy as jnp
from jax import lax
from jax.experimental import pallas as pl
from jax.experimental.pallas import tpu as pltpu
from jax.sharding import PartitionSpec as P

HD = 128
STEPS = 1000


sigma_data = 0.5
guidance = 5.0


def rope_angles(coords):
    half_size = HD // 2
    sixth = HD // 6
    first_pairs = half_size - 2 * sixth
    pair_index = jnp.arange(half_size)
    axis_id = (pair_index >= first_pairs).astype(jnp.int32) + (
        pair_index >= first_pairs + sixth
    ).astype(jnp.int32)
    offset = jnp.where(axis_id == 0, 0, jnp.where(axis_id == 1, first_pairs, first_pairs + sixth))
    axis_width = jnp.where(axis_id == 0, 2 * first_pairs, 2 * sixth)
    exponent = 2.0 * (pair_index - offset).astype(jnp.float32) / axis_width.astype(jnp.float32)
    frequency = jnp.exp(-exponent * math.log(10000.0))
    angles = jnp.zeros((coords.shape[1], half_size), jnp.float32)
    for which_axis in range(3):
        chosen = jnp.where(axis_id == which_axis, frequency, 0.0)
        angles = angles + coords[which_axis].astype(jnp.float32)[:, None] * chosen[None, :]
    return angles


def rotate_heads(source, angles):
    half_size = source.shape[-1] // 2
    cos_angle = jnp.cos(angles)[:, None, :]
    sin_angle = jnp.sin(angles)[:, None, :]
    front_half = source[..., :half_size]
    back_half = source[..., half_size:]
    return jnp.concatenate(
        [
            front_half * cos_angle - back_half * sin_angle,
            back_half * cos_angle + front_half * sin_angle,
        ],
        axis=-1,
    )


def split_heads(source):
    return source.reshape(source.shape[0], -1, HD)


def rotated(source, angles):
    row_count = source.shape[0]
    return (
        rotate_heads(split_heads(source).astype(jnp.float32), angles)
        .astype(jnp.bfloat16)
        .reshape(row_count, -1)
    )


def softmax_rows(scores):
    row_peak = jnp.max(scores, axis=-1, keepdims=True)
    exponent = jnp.exp(scores - row_peak)
    return exponent / jnp.sum(exponent, axis=-1, keepdims=True)


def attend_plain(queries, key_rows, value_rows):
    scores = jnp.einsum(
        "qhd,khd->hqk", queries, key_rows, preferred_element_type=jnp.float32
    ) * HD ** (-0.5)
    rounded = softmax_rows(scores).astype(jnp.bfloat16)
    return jnp.einsum("hqk,khd->qhd", rounded, value_rows, preferred_element_type=jnp.float32)


def attend_tangent(queries, key_rows, value_rows, query_dir, key_dir, value_dir):
    score_scale = HD ** (-0.5)
    scores = (
        jnp.einsum("qhd,khd->hqk", queries, key_rows, preferred_element_type=jnp.float32)
        * score_scale
    )
    weights = softmax_rows(scores)
    rounded = weights.astype(jnp.bfloat16)
    primal = jnp.einsum("hqk,khd->qhd", rounded, value_rows, preferred_element_type=jnp.float32)
    score_dir = (
        jnp.einsum("qhd,khd->hqk", query_dir, key_rows, preferred_element_type=jnp.float32)
        + jnp.einsum("qhd,khd->hqk", queries, key_dir, preferred_element_type=jnp.float32)
    ) * score_scale
    weight_dir = weights * (score_dir - jnp.sum(weights * score_dir, axis=-1, keepdims=True))
    rounded_dir = weight_dir.astype(jnp.bfloat16)
    tangent = jnp.einsum(
        "hqk,khd->qhd", rounded_dir, value_rows, preferred_element_type=jnp.float32
    ) + jnp.einsum("hqk,khd->qhd", rounded, value_dir, preferred_element_type=jnp.float32)
    return (primal, tangent)


SCORE_SCALE = HD ** (-0.5)


def rope_tables(angles):
    cos_angle = jnp.cos(angles)
    sin_angle = jnp.sin(angles)
    return (
        jnp.concatenate([cos_angle, cos_angle], axis=-1),
        jnp.concatenate([-sin_angle, sin_angle], axis=-1),
    )


def rotate_block(block, cos_ref, sin_ref):
    source = block.astype(jnp.float32)
    swapped = pltpu.roll(source, HD // 2, 1)
    return (source * cos_ref[...] + swapped * sin_ref[...]).astype(jnp.bfloat16)


def scores_of(queries, key_rows):
    return (
        lax.dot_general(
            queries, key_rows, (((1,), (1,)), ((), ())), preferred_element_type=jnp.float32
        )
        * SCORE_SCALE
    )


def softmax_block(scores):
    exponent = jnp.exp(scores - jnp.max(scores, axis=-1, keepdims=True))
    return exponent / jnp.sum(exponent, axis=-1, keepdims=True)


def teacher_kernel(scal, cos_ref, sin_ref, q0, k0, v0, q1, k1, v1, out_ref):
    def attend(q_ref, k_ref, v_ref):
        weights = softmax_block(
            scores_of(rotate_block(q_ref[...], cos_ref, sin_ref), rotate_block(k_ref[...], cos_ref, sin_ref))
        )
        return jnp.dot(weights.astype(jnp.bfloat16), v_ref[...], preferred_element_type=jnp.float32)

    first = attend(q0, k0, v0)
    second = attend(q1, k1, v1)
    pick_first = scal[1] == 0.0
    cond_out = jnp.where(pick_first, first, second)
    uncond_out = jnp.where(pick_first, second, first)
    out_ref[...] = (scal[0] * (uncond_out + guidance * (cond_out - uncond_out))).astype(jnp.bfloat16)


def student_kernel(scal, cos_ref, sin_ref, q, k, v, qt, kt, vt, term_ref, att_ref):
    queries = rotate_block(q[...], cos_ref, sin_ref)
    key_rows = rotate_block(k[...], cos_ref, sin_ref)
    query_dir = rotate_block(qt[...], cos_ref, sin_ref)
    key_dir = rotate_block(kt[...], cos_ref, sin_ref)
    weights = softmax_block(scores_of(queries, key_rows))
    rounded = weights.astype(jnp.bfloat16)
    primal = jnp.dot(rounded, v[...], preferred_element_type=jnp.float32)
    score_dir = (
        lax.dot_general(query_dir, key_rows, (((1,), (1,)), ((), ())), preferred_element_type=jnp.float32)
        + lax.dot_general(queries, key_dir, (((1,), (1,)), ((), ())), preferred_element_type=jnp.float32)
    ) * SCORE_SCALE
    weight_dir = weights * (score_dir - jnp.sum(weights * score_dir, axis=-1, keepdims=True))
    tangent = jnp.dot(weight_dir.astype(jnp.bfloat16), v[...], preferred_element_type=jnp.float32) + jnp.dot(
        rounded, vt[...], preferred_element_type=jnp.float32
    )
    term_ref[...] = (scal[0] * primal - scal[1] * tangent).astype(jnp.bfloat16)
    att_ref[...] = primal.astype(jnp.bfloat16)


def head_call(kernel, scal, tables, operands, outputs):
    seq, cols = outputs[0].shape
    heads = cols // HD
    head_block = pl.BlockSpec((seq, HD), lambda h: (0, h))
    table_block = pl.BlockSpec((seq, HD), lambda h: (0, 0))
    in_specs = [pl.BlockSpec(memory_space=pltpu.SMEM), table_block, table_block]
    for operand in operands:
        if operand.ndim == 2:
            in_specs.append(head_block)
        else:
            in_specs.append(pl.BlockSpec((None, seq, HD), lambda h, s=operand.index: (s, 0, h)))
    return pl.pallas_call(
        kernel,
        grid=(heads,),
        in_specs=in_specs,
        out_specs=[head_block] * len(outputs),
        out_shape=outputs,
        compiler_params=pltpu.CompilerParams(dimension_semantics=("arbitrary",)),
    )(scal, *tables, *[o.array for o in operands])


class Operand:
    def __init__(self, array, index=None):
        self.array = array
        self.index = index
        self.ndim = 2 if index is None else 3


def local(
    t_index,
    cond_slot,
    positions,
    latent,
    teacher_query,
    teacher_key,
    teacher_value,
    student_query,
    student_key,
    student_value,
    query_tangent,
    key_tangent,
    value_tangent,
    teacher_out,
    student_out,
):
    groups = lax.axis_size("tensor")
    seq_local = latent.shape[1]
    seq_whole = seq_local * groups
    row_start = lax.axis_index("tensor") * seq_local
    time_value = 0.2 + 1.2 * (t_index[0].astype(jnp.float32) + 0.5) / STEPS
    cos_time = jnp.cos(time_value)
    sin_time = jnp.sin(time_value)
    angles_whole = rope_angles(positions[0])
    tables = rope_tables(angles_whole)
    arrived = [
        lax.all_to_all(source[0], "tensor", split_axis=1, concat_axis=0, tiled=True)
        for source in (student_query, student_key, student_value, query_tangent, key_tangent, value_tangent)
    ]
    cols = arrived[0].shape[1]
    teacher_scal = jnp.stack(
        [cos_time * cos_time * sigma_data, cond_slot[0].astype(jnp.float32)]
    )
    t_q = teacher_query.reshape((2,) + teacher_query.shape[2:])
    t_k = teacher_key.reshape((2,) + teacher_key.shape[2:])
    t_v = teacher_value.reshape((2,) + teacher_value.shape[2:])
    (teacher_term,) = head_call(
        teacher_kernel,
        teacher_scal,
        tables,
        [Operand(t_q, 0), Operand(t_k, 0), Operand(t_v, 0), Operand(t_q, 1), Operand(t_k, 1), Operand(t_v, 1)],
        [jax.ShapeDtypeStruct((seq_whole, cols), jnp.bfloat16)],
    )
    student_scal = jnp.stack(
        [-(cos_time * cos_time) * sigma_data, cos_time * sin_time * sigma_data]
    )
    student_term, attended = head_call(
        student_kernel,
        student_scal,
        tables,
        [Operand(a) for a in arrived],
        [jax.ShapeDtypeStruct((seq_whole, cols), jnp.bfloat16)] * 2,
    )
    stacked = jnp.stack([student_out, teacher_out])
    pieces = lax.all_gather(stacked, "dp", axis=2, tiled=True)
    partial_value = jnp.dot(student_term, pieces[0], preferred_element_type=jnp.float32) + jnp.dot(
        teacher_term, pieces[1], preferred_element_type=jnp.float32
    )
    latent_weight = cos_time * sin_time
    pieces_in = lax.all_to_all(
        partial_value.astype(jnp.bfloat16).reshape(groups, seq_local, -1),
        "tensor",
        split_axis=0,
        concat_axis=0,
        tiled=True,
    )
    velocity = jnp.sum(pieces_in.astype(jnp.float32), axis=0)
    target = (velocity - latent_weight * latent[0].astype(jnp.float32)).astype(jnp.bfloat16)
    clips = lax.axis_size("dp")
    width = target.shape[1] // clips
    attended_all = lax.all_gather(attended, "dp", axis=0, tiled=False)
    columns = lax.all_to_all(
        target.reshape(seq_local, clips, width), "dp", split_axis=1, concat_axis=1, tiled=True
    )
    columns = lax.all_gather(columns, "tensor", axis=0, tiled=True)
    grad_scale = -2.0 / math.sqrt(clips * seq_whole)
    terms = jnp.einsum(
        "csi,scd->cid", attended_all, columns, preferred_element_type=jnp.float32
    )
    gradient = jnp.sum((grad_scale * terms).astype(jnp.bfloat16).astype(jnp.float32), axis=0)
    return (target[None], gradient)


def solution(mesh):
    placed = (
        P("dp"),
        P("dp"),
        P("dp", None, None),
        P("dp", "tensor", None),
        P(None, "dp", None, "tensor"),
        P(None, "dp", None, "tensor"),
        P(None, "dp", None, "tensor"),
        P("dp", "tensor", None),
        P("dp", "tensor", None),
        P("dp", "tensor", None),
        P("dp", "tensor", None),
        P("dp", "tensor", None),
        P("dp", "tensor", None),
        P("tensor", "dp"),
        P("tensor", "dp"),
    )
    return jax.shard_map(
        local,
        mesh=mesh,
        in_specs=placed,
        out_specs=(P("dp", "tensor", None), P("tensor", "dp")),
        check_vma=False,
    )
```

```python
import math

import jax
import jax.numpy as jnp
from jax import lax
from jax.experimental import pallas as pl
from jax.experimental.pallas import tpu as pltpu
from jax.sharding import PartitionSpec as P

HD = 128
STEPS = 1000


sigma_data = 0.5
guidance = 5.0


def rope_angles(coords):
    half_size = HD // 2
    sixth = HD // 6
    first_pairs = half_size - 2 * sixth
    pair_index = jnp.arange(half_size)
    axis_id = (pair_index >= first_pairs).astype(jnp.int32) + (
        pair_index >= first_pairs + sixth
    ).astype(jnp.int32)
    offset = jnp.where(axis_id == 0, 0, jnp.where(axis_id == 1, first_pairs, first_pairs + sixth))
    axis_width = jnp.where(axis_id == 0, 2 * first_pairs, 2 * sixth)
    exponent = 2.0 * (pair_index - offset).astype(jnp.float32) / axis_width.astype(jnp.float32)
    frequency = jnp.exp(-exponent * math.log(10000.0))
    angles = jnp.zeros((coords.shape[1], half_size), jnp.float32)
    for which_axis in range(3):
        chosen = jnp.where(axis_id == which_axis, frequency, 0.0)
        angles = angles + coords[which_axis].astype(jnp.float32)[:, None] * chosen[None, :]
    return angles


def rotate_heads(source, angles):
    half_size = source.shape[-1] // 2
    cos_angle = jnp.cos(angles)[:, None, :]
    sin_angle = jnp.sin(angles)[:, None, :]
    front_half = source[..., :half_size]
    back_half = source[..., half_size:]
    return jnp.concatenate(
        [
            front_half * cos_angle - back_half * sin_angle,
            back_half * cos_angle + front_half * sin_angle,
        ],
        axis=-1,
    )


def split_heads(source):
    return source.reshape(source.shape[0], -1, HD)


def rotated(source, angles):
    row_count = source.shape[0]
    return (
        rotate_heads(split_heads(source).astype(jnp.float32), angles)
        .astype(jnp.bfloat16)
        .reshape(row_count, -1)
    )


def softmax_rows(scores):
    row_peak = jnp.max(scores, axis=-1, keepdims=True)
    exponent = jnp.exp(scores - row_peak)
    return exponent / jnp.sum(exponent, axis=-1, keepdims=True)


def attend_plain(queries, key_rows, value_rows):
    scores = jnp.einsum(
        "qhd,khd->hqk", queries, key_rows, preferred_element_type=jnp.float32
    ) * HD ** (-0.5)
    rounded = softmax_rows(scores).astype(jnp.bfloat16)
    return jnp.einsum("hqk,khd->qhd", rounded, value_rows, preferred_element_type=jnp.float32)


def attend_tangent(queries, key_rows, value_rows, query_dir, key_dir, value_dir):
    score_scale = HD ** (-0.5)
    scores = (
        jnp.einsum("qhd,khd->hqk", queries, key_rows, preferred_element_type=jnp.float32)
        * score_scale
    )
    weights = softmax_rows(scores)
    rounded = weights.astype(jnp.bfloat16)
    primal = jnp.einsum("hqk,khd->qhd", rounded, value_rows, preferred_element_type=jnp.float32)
    score_dir = (
        jnp.einsum("qhd,khd->hqk", query_dir, key_rows, preferred_element_type=jnp.float32)
        + jnp.einsum("qhd,khd->hqk", queries, key_dir, preferred_element_type=jnp.float32)
    ) * score_scale
    weight_dir = weights * (score_dir - jnp.sum(weights * score_dir, axis=-1, keepdims=True))
    rounded_dir = weight_dir.astype(jnp.bfloat16)
    tangent = jnp.einsum(
        "hqk,khd->qhd", rounded_dir, value_rows, preferred_element_type=jnp.float32
    ) + jnp.einsum("hqk,khd->qhd", rounded, value_dir, preferred_element_type=jnp.float32)
    return (primal, tangent)


SCORE_SCALE = HD ** (-0.5)


def rope_tables(angles):
    cos_angle = jnp.cos(angles)
    sin_angle = jnp.sin(angles)
    return (
        jnp.concatenate([cos_angle, cos_angle], axis=-1),
        jnp.concatenate([-sin_angle, sin_angle], axis=-1),
    )


def rotate_block(block, cos_ref, sin_ref):
    source = block.astype(jnp.float32)
    swapped = pltpu.roll(source, HD // 2, 1)
    return (source * cos_ref[...] + swapped * sin_ref[...]).astype(jnp.bfloat16)


def scores_of(queries, key_rows):
    return (
        lax.dot_general(
            queries, key_rows, (((1,), (1,)), ((), ())), preferred_element_type=jnp.float32
        )
        * SCORE_SCALE
    )


def softmax_block(scores):
    exponent = jnp.exp(scores - jnp.max(scores, axis=-1, keepdims=True))
    return exponent / jnp.sum(exponent, axis=-1, keepdims=True)


def teacher_kernel(scal, cos_ref, sin_ref, q0, k0, v0, q1, k1, v1, out_ref):
    def attend(q_ref, k_ref, v_ref):
        weights = softmax_block(
            scores_of(rotate_block(q_ref[...], cos_ref, sin_ref), rotate_block(k_ref[...], cos_ref, sin_ref))
        )
        return jnp.dot(weights.astype(jnp.bfloat16), v_ref[...], preferred_element_type=jnp.float32)

    first = attend(q0, k0, v0)
    second = attend(q1, k1, v1)
    pick_first = scal[1] == 0.0
    cond_out = jnp.where(pick_first, first, second)
    uncond_out = jnp.where(pick_first, second, first)
    out_ref[...] = (scal[0] * (uncond_out + guidance * (cond_out - uncond_out))).astype(jnp.bfloat16)


def student_kernel(scal, cos_ref, sin_ref, q, k, v, qt, kt, vt, term_ref, att_ref):
    queries = rotate_block(q[...], cos_ref, sin_ref)
    key_rows = rotate_block(k[...], cos_ref, sin_ref)
    query_dir = rotate_block(qt[...], cos_ref, sin_ref)
    key_dir = rotate_block(kt[...], cos_ref, sin_ref)
    weights = softmax_block(scores_of(queries, key_rows))
    rounded = weights.astype(jnp.bfloat16)
    primal = jnp.dot(rounded, v[...], preferred_element_type=jnp.float32)
    score_dir = (
        lax.dot_general(query_dir, key_rows, (((1,), (1,)), ((), ())), preferred_element_type=jnp.float32)
        + lax.dot_general(queries, key_dir, (((1,), (1,)), ((), ())), preferred_element_type=jnp.float32)
    ) * SCORE_SCALE
    weight_dir = weights * (score_dir - jnp.sum(weights * score_dir, axis=-1, keepdims=True))
    tangent = jnp.dot(weight_dir.astype(jnp.bfloat16), v[...], preferred_element_type=jnp.float32) + jnp.dot(
        rounded, vt[...], preferred_element_type=jnp.float32
    )
    term_ref[...] = (scal[0] * primal - scal[1] * tangent).astype(jnp.bfloat16)
    att_ref[...] = primal.astype(jnp.bfloat16)


def head_call(kernel, scal, tables, operands, outputs):
    seq, cols = outputs[0].shape
    heads = cols // HD
    head_block = pl.BlockSpec((seq, HD), lambda h: (0, h))
    table_block = pl.BlockSpec((seq, HD), lambda h: (0, 0))
    in_specs = [pl.BlockSpec(memory_space=pltpu.SMEM), table_block, table_block]
    for operand in operands:
        if operand.ndim == 2:
            in_specs.append(head_block)
        else:
            in_specs.append(pl.BlockSpec((None, seq, HD), lambda h, s=operand.index: (s, 0, h)))
    return pl.pallas_call(
        kernel,
        grid=(heads,),
        in_specs=in_specs,
        out_specs=[head_block] * len(outputs),
        out_shape=outputs,
        compiler_params=pltpu.CompilerParams(dimension_semantics=("arbitrary",)),
    )(scal, *tables, *[o.array for o in operands])


class Operand:
    def __init__(self, array, index=None):
        self.array = array
        self.index = index
        self.ndim = 2 if index is None else 3


def local(
    t_index,
    cond_slot,
    positions,
    latent,
    teacher_query,
    teacher_key,
    teacher_value,
    student_query,
    student_key,
    student_value,
    query_tangent,
    key_tangent,
    value_tangent,
    teacher_out,
    student_out,
):
    groups = lax.axis_size("tensor")
    seq_local = latent.shape[1]
    seq_whole = seq_local * groups
    row_start = lax.axis_index("tensor") * seq_local
    time_value = 0.2 + 1.2 * (t_index[0].astype(jnp.float32) + 0.5) / STEPS
    cos_time = jnp.cos(time_value)
    sin_time = jnp.sin(time_value)
    angles_whole = rope_angles(positions[0])
    tables = rope_tables(angles_whole)
    cols = teacher_query.shape[3]
    teacher_scal = jnp.stack(
        [cos_time * cos_time * sigma_data, cond_slot[0].astype(jnp.float32)]
    )
    t_q = teacher_query.reshape((2,) + teacher_query.shape[2:])
    t_k = teacher_key.reshape((2,) + teacher_key.shape[2:])
    t_v = teacher_value.reshape((2,) + teacher_value.shape[2:])
    (teacher_term,) = head_call(
        teacher_kernel,
        teacher_scal,
        tables,
        [Operand(t_q, 0), Operand(t_k, 0), Operand(t_v, 0), Operand(t_q, 1), Operand(t_k, 1), Operand(t_v, 1)],
        [jax.ShapeDtypeStruct((seq_whole, cols), jnp.bfloat16)],
    )
    teacher_term, sources = lax.optimization_barrier(
        (teacher_term, (student_query, student_key, student_value, query_tangent, key_tangent, value_tangent))
    )
    teacher_all = lax.all_gather(teacher_term, "dp", axis=0, tiled=False)
    arrived = [
        lax.all_to_all(source[0], "tensor", split_axis=1, concat_axis=0, tiled=True)
        for source in sources[:-1]
    ]
    teacher_all, last = lax.optimization_barrier((teacher_all, sources[-1]))
    arrived.append(lax.all_to_all(last[0], "tensor", split_axis=1, concat_axis=0, tiled=True))
    student_scal = jnp.stack(
        [-(cos_time * cos_time) * sigma_data, cos_time * sin_time * sigma_data]
    )
    student_term, attended = head_call(
        student_kernel,
        student_scal,
        tables,
        [Operand(a) for a in arrived],
        [jax.ShapeDtypeStruct((seq_whole, cols), jnp.bfloat16)] * 2,
    )
    clips = lax.axis_size("dp")
    width = latent.shape[2] // clips
    times_all = lax.all_gather(t_index, "dp", axis=0, tiled=True)
    time_all = 0.2 + 1.2 * (times_all.astype(jnp.float32) + 0.5) / STEPS
    latent_weight = (jnp.cos(time_all) * jnp.sin(time_all))[:, None, None]
    latent_cols = lax.all_to_all(
        latent[0].reshape(seq_local, clips, width), "dp", split_axis=1, concat_axis=1, tiled=True
    )
    student_all = lax.all_gather(student_term, "dp", axis=0, tiled=False)
    attended, student_all = lax.optimization_barrier((attended, student_all))
    attended_all = lax.all_gather(attended, "dp", axis=0, tiled=False)
    partial_value = jnp.einsum(
        "csi,id->csd", student_all, student_out, preferred_element_type=jnp.float32
    ) + jnp.einsum("csi,id->csd", teacher_all, teacher_out, preferred_element_type=jnp.float32)
    pieces_in = lax.all_to_all(
        partial_value.astype(jnp.bfloat16).reshape(clips, groups, seq_local, width),
        "tensor",
        split_axis=1,
        concat_axis=1,
        tiled=True,
    )
    velocity = jnp.sum(pieces_in.astype(jnp.float32), axis=1)
    columns = (
        velocity - latent_weight * jnp.transpose(latent_cols, (1, 0, 2)).astype(jnp.float32)
    ).astype(jnp.bfloat16)
    target = lax.all_to_all(columns, "dp", split_axis=0, concat_axis=0, tiled=True)
    target = jnp.transpose(target, (1, 0, 2)).reshape(seq_local, clips * width)
    columns, attended_all = lax.optimization_barrier((columns, attended_all))
    columns = lax.all_gather(columns, "tensor", axis=1, tiled=True)
    grad_scale = -2.0 / math.sqrt(clips * seq_whole)
    terms = jnp.einsum(
        "csi,csd->cid", attended_all, columns, preferred_element_type=jnp.float32
    )
    gradient = jnp.sum((grad_scale * terms).astype(jnp.bfloat16).astype(jnp.float32), axis=0)
    return (target[None], gradient)


def solution(mesh):
    placed = (
        P("dp"),
        P("dp"),
        P("dp", None, None),
        P("dp", "tensor", None),
        P(None, "dp", None, "tensor"),
        P(None, "dp", None, "tensor"),
        P(None, "dp", None, "tensor"),
        P("dp", "tensor", None),
        P("dp", "tensor", None),
        P("dp", "tensor", None),
        P("dp", "tensor", None),
        P("dp", "tensor", None),
        P("dp", "tensor", None),
        P("tensor", "dp"),
        P("tensor", "dp"),
    )
    return jax.shard_map(
        local,
        mesh=mesh,
        in_specs=placed,
        out_specs=(P("dp", "tensor", None), P("tensor", "dp")),
        check_vma=False,
    )
```

```python
import math

import jax
import jax.numpy as jnp
from jax import lax
from jax.experimental import pallas as pl
from jax.experimental.pallas import tpu as pltpu
from jax.sharding import PartitionSpec as P

HD = 128
STEPS = 1000


sigma_data = 0.5
guidance = 5.0


def rope_angles(coords):
    half_size = HD // 2
    sixth = HD // 6
    first_pairs = half_size - 2 * sixth
    pair_index = jnp.arange(half_size)
    axis_id = (pair_index >= first_pairs).astype(jnp.int32) + (
        pair_index >= first_pairs + sixth
    ).astype(jnp.int32)
    offset = jnp.where(axis_id == 0, 0, jnp.where(axis_id == 1, first_pairs, first_pairs + sixth))
    axis_width = jnp.where(axis_id == 0, 2 * first_pairs, 2 * sixth)
    exponent = 2.0 * (pair_index - offset).astype(jnp.float32) / axis_width.astype(jnp.float32)
    frequency = jnp.exp(-exponent * math.log(10000.0))
    angles = jnp.zeros((coords.shape[1], half_size), jnp.float32)
    for which_axis in range(3):
        chosen = jnp.where(axis_id == which_axis, frequency, 0.0)
        angles = angles + coords[which_axis].astype(jnp.float32)[:, None] * chosen[None, :]
    return angles


def rotate_heads(source, angles):
    half_size = source.shape[-1] // 2
    cos_angle = jnp.cos(angles)[:, None, :]
    sin_angle = jnp.sin(angles)[:, None, :]
    front_half = source[..., :half_size]
    back_half = source[..., half_size:]
    return jnp.concatenate(
        [
            front_half * cos_angle - back_half * sin_angle,
            back_half * cos_angle + front_half * sin_angle,
        ],
        axis=-1,
    )


def split_heads(source):
    return source.reshape(source.shape[0], -1, HD)


def rotated(source, angles):
    row_count = source.shape[0]
    return (
        rotate_heads(split_heads(source).astype(jnp.float32), angles)
        .astype(jnp.bfloat16)
        .reshape(row_count, -1)
    )


def softmax_rows(scores):
    row_peak = jnp.max(scores, axis=-1, keepdims=True)
    exponent = jnp.exp(scores - row_peak)
    return exponent / jnp.sum(exponent, axis=-1, keepdims=True)


def attend_plain(queries, key_rows, value_rows):
    scores = jnp.einsum(
        "qhd,khd->hqk", queries, key_rows, preferred_element_type=jnp.float32
    ) * HD ** (-0.5)
    rounded = softmax_rows(scores).astype(jnp.bfloat16)
    return jnp.einsum("hqk,khd->qhd", rounded, value_rows, preferred_element_type=jnp.float32)


def attend_tangent(queries, key_rows, value_rows, query_dir, key_dir, value_dir):
    score_scale = HD ** (-0.5)
    scores = (
        jnp.einsum("qhd,khd->hqk", queries, key_rows, preferred_element_type=jnp.float32)
        * score_scale
    )
    weights = softmax_rows(scores)
    rounded = weights.astype(jnp.bfloat16)
    primal = jnp.einsum("hqk,khd->qhd", rounded, value_rows, preferred_element_type=jnp.float32)
    score_dir = (
        jnp.einsum("qhd,khd->hqk", query_dir, key_rows, preferred_element_type=jnp.float32)
        + jnp.einsum("qhd,khd->hqk", queries, key_dir, preferred_element_type=jnp.float32)
    ) * score_scale
    weight_dir = weights * (score_dir - jnp.sum(weights * score_dir, axis=-1, keepdims=True))
    rounded_dir = weight_dir.astype(jnp.bfloat16)
    tangent = jnp.einsum(
        "hqk,khd->qhd", rounded_dir, value_rows, preferred_element_type=jnp.float32
    ) + jnp.einsum("hqk,khd->qhd", rounded, value_dir, preferred_element_type=jnp.float32)
    return (primal, tangent)


SCORE_SCALE = HD ** (-0.5)


def rope_tables(angles):
    cos_angle = jnp.cos(angles)
    sin_angle = jnp.sin(angles)
    return (
        jnp.concatenate([cos_angle, cos_angle], axis=-1),
        jnp.concatenate([-sin_angle, sin_angle], axis=-1),
    )


def rotate_block(block, cos_ref, sin_ref):
    source = block.astype(jnp.float32)
    swapped = pltpu.roll(source, HD // 2, 1)
    return (source * cos_ref[...] + swapped * sin_ref[...]).astype(jnp.bfloat16)


def scores_of(queries, key_rows):
    return (
        lax.dot_general(
            queries, key_rows, (((1,), (1,)), ((), ())), preferred_element_type=jnp.float32
        )
        * SCORE_SCALE
    )


def softmax_block(scores):
    exponent = jnp.exp(scores - jnp.max(scores, axis=-1, keepdims=True))
    return exponent / jnp.sum(exponent, axis=-1, keepdims=True)


def teacher_kernel(scal, cos_ref, sin_ref, q0, k0, v0, q1, k1, v1, out_ref):
    def attend(q_ref, k_ref, v_ref):
        weights = softmax_block(
            scores_of(rotate_block(q_ref[...], cos_ref, sin_ref), rotate_block(k_ref[...], cos_ref, sin_ref))
        )
        return jnp.dot(weights.astype(jnp.bfloat16), v_ref[...], preferred_element_type=jnp.float32)

    first = attend(q0, k0, v0)
    second = attend(q1, k1, v1)
    pick_first = scal[1] == 0.0
    cond_out = jnp.where(pick_first, first, second)
    uncond_out = jnp.where(pick_first, second, first)
    out_ref[...] = (scal[0] * (uncond_out + guidance * (cond_out - uncond_out))).astype(jnp.bfloat16)


def student_kernel(scal, cos_ref, sin_ref, q, k, v, qt, kt, vt, term_ref, att_ref):
    queries = rotate_block(q[...], cos_ref, sin_ref)
    key_rows = rotate_block(k[...], cos_ref, sin_ref)
    query_dir = rotate_block(qt[...], cos_ref, sin_ref)
    key_dir = rotate_block(kt[...], cos_ref, sin_ref)
    weights = softmax_block(scores_of(queries, key_rows))
    rounded = weights.astype(jnp.bfloat16)
    primal = jnp.dot(rounded, v[...], preferred_element_type=jnp.float32)
    score_dir = (
        lax.dot_general(query_dir, key_rows, (((1,), (1,)), ((), ())), preferred_element_type=jnp.float32)
        + lax.dot_general(queries, key_dir, (((1,), (1,)), ((), ())), preferred_element_type=jnp.float32)
    ) * SCORE_SCALE
    weight_dir = weights * (score_dir - jnp.sum(weights * score_dir, axis=-1, keepdims=True))
    tangent = jnp.dot(weight_dir.astype(jnp.bfloat16), v[...], preferred_element_type=jnp.float32) + jnp.dot(
        rounded, vt[...], preferred_element_type=jnp.float32
    )
    term_ref[...] = (scal[0] * primal - scal[1] * tangent).astype(jnp.bfloat16)
    att_ref[...] = primal.astype(jnp.bfloat16)


def head_call(kernel, scal, tables, operands, outputs):
    seq, cols = outputs[0].shape
    heads = cols // HD
    head_block = pl.BlockSpec((seq, HD), lambda h: (0, h))
    table_block = pl.BlockSpec((seq, HD), lambda h: (0, 0))
    in_specs = [pl.BlockSpec(memory_space=pltpu.SMEM), table_block, table_block]
    for operand in operands:
        if operand.ndim == 2:
            in_specs.append(head_block)
        else:
            in_specs.append(pl.BlockSpec((None, seq, HD), lambda h, s=operand.index: (s, 0, h)))
    return pl.pallas_call(
        kernel,
        grid=(heads,),
        in_specs=in_specs,
        out_specs=[head_block] * len(outputs),
        out_shape=outputs,
        compiler_params=pltpu.CompilerParams(dimension_semantics=("arbitrary",)),
    )(scal, *tables, *[o.array for o in operands])


class Operand:
    def __init__(self, array, index=None):
        self.array = array
        self.index = index
        self.ndim = 2 if index is None else 3


def local(
    t_index,
    cond_slot,
    positions,
    latent,
    teacher_query,
    teacher_key,
    teacher_value,
    student_query,
    student_key,
    student_value,
    query_tangent,
    key_tangent,
    value_tangent,
    teacher_out,
    student_out,
):
    groups = lax.axis_size("tensor")
    seq_local = latent.shape[1]
    seq_whole = seq_local * groups
    row_start = lax.axis_index("tensor") * seq_local
    time_value = 0.2 + 1.2 * (t_index[0].astype(jnp.float32) + 0.5) / STEPS
    cos_time = jnp.cos(time_value)
    sin_time = jnp.sin(time_value)
    angles_whole = rope_angles(positions[0])
    tables = rope_tables(angles_whole)
    cols = teacher_query.shape[3]
    teacher_scal = jnp.stack(
        [cos_time * cos_time * sigma_data, cond_slot[0].astype(jnp.float32)]
    )
    t_q = teacher_query.reshape((2,) + teacher_query.shape[2:])
    t_k = teacher_key.reshape((2,) + teacher_key.shape[2:])
    t_v = teacher_value.reshape((2,) + teacher_value.shape[2:])
    (teacher_term,) = head_call(
        teacher_kernel,
        teacher_scal,
        tables,
        [Operand(t_q, 0), Operand(t_k, 0), Operand(t_v, 0), Operand(t_q, 1), Operand(t_k, 1), Operand(t_v, 1)],
        [jax.ShapeDtypeStruct((seq_whole, cols), jnp.bfloat16)],
    )
    clips = lax.axis_size("dp")
    width = latent.shape[2] // clips
    times_all = lax.all_gather(t_index, "dp", axis=0, tiled=True)
    teacher_term, sources, times_all = lax.optimization_barrier(
        (teacher_term, (student_query, student_key, student_value, query_tangent, key_tangent, value_tangent), times_all)
    )
    teacher_all = lax.all_gather(teacher_term, "dp", axis=0, tiled=False)
    latent_cols = lax.all_to_all(
        latent[0].reshape(seq_local, clips, width), "dp", split_axis=1, concat_axis=1, tiled=True
    )
    arrived = [
        lax.all_to_all(source[0], "tensor", split_axis=1, concat_axis=0, tiled=True)
        for source in sources[:-1]
    ]
    teacher_all, last, latent_cols = lax.optimization_barrier((teacher_all, sources[-1], latent_cols))
    arrived.append(lax.all_to_all(last[0], "tensor", split_axis=1, concat_axis=0, tiled=True))
    student_scal = jnp.stack(
        [-(cos_time * cos_time) * sigma_data, cos_time * sin_time * sigma_data]
    )
    student_term, attended = head_call(
        student_kernel,
        student_scal,
        tables,
        [Operand(a) for a in arrived],
        [jax.ShapeDtypeStruct((seq_whole, cols), jnp.bfloat16)] * 2,
    )
    time_all = 0.2 + 1.2 * (times_all.astype(jnp.float32) + 0.5) / STEPS
    latent_weight = (jnp.cos(time_all) * jnp.sin(time_all))[:, None, None]
    teacher_partial = jnp.einsum(
        "csi,id->csd", teacher_all, teacher_out, preferred_element_type=jnp.float32
    )
    student_all = lax.all_gather(student_term, "dp", axis=0, tiled=False)
    attended, student_all, teacher_partial = lax.optimization_barrier((attended, student_all, teacher_partial))
    attended_all = lax.all_gather(attended, "dp", axis=0, tiled=False)
    partial_value = jnp.einsum(
        "csi,id->csd", student_all, student_out, preferred_element_type=jnp.float32
    ) + teacher_partial
    pieces_in = lax.all_to_all(
        partial_value.astype(jnp.bfloat16).reshape(clips, groups, seq_local, width),
        "tensor",
        split_axis=1,
        concat_axis=1,
        tiled=True,
    )
    velocity = jnp.sum(pieces_in.astype(jnp.float32), axis=1)
    columns = (
        velocity - latent_weight * jnp.transpose(latent_cols, (1, 0, 2)).astype(jnp.float32)
    ).astype(jnp.bfloat16)
    target = lax.all_to_all(columns, "dp", split_axis=0, concat_axis=0, tiled=True)
    target = jnp.transpose(target, (1, 0, 2)).reshape(seq_local, clips * width)
    columns, attended_all = lax.optimization_barrier((columns, attended_all))
    columns = lax.all_gather(columns, "tensor", axis=1, tiled=True)
    grad_scale = -2.0 / math.sqrt(clips * seq_whole)
    terms = jnp.einsum(
        "csi,csd->cid", attended_all, columns, preferred_element_type=jnp.float32
    )
    gradient = jnp.sum((grad_scale * terms).astype(jnp.bfloat16).astype(jnp.float32), axis=0)
    return (target[None], gradient)


def solution(mesh):
    placed = (
        P("dp"),
        P("dp"),
        P("dp", None, None),
        P("dp", "tensor", None),
        P(None, "dp", None, "tensor"),
        P(None, "dp", None, "tensor"),
        P(None, "dp", None, "tensor"),
        P("dp", "tensor", None),
        P("dp", "tensor", None),
        P("dp", "tensor", None),
        P("dp", "tensor", None),
        P("dp", "tensor", None),
        P("dp", "tensor", None),
        P("tensor", "dp"),
        P("tensor", "dp"),
    )
    return jax.shard_map(
        local,
        mesh=mesh,
        in_specs=placed,
        out_specs=(P("dp", "tensor", None), P("tensor", "dp")),
        check_vma=False,
    )
```

```python
import math

import jax
import jax.numpy as jnp
from jax import lax
from jax.experimental import pallas as pl
from jax.experimental.pallas import tpu as pltpu
from jax.sharding import PartitionSpec as P

HD = 128
STEPS = 1000


sigma_data = 0.5
guidance = 5.0


def rope_angles(coords):
    half_size = HD // 2
    sixth = HD // 6
    first_pairs = half_size - 2 * sixth
    pair_index = jnp.arange(half_size)
    axis_id = (pair_index >= first_pairs).astype(jnp.int32) + (
        pair_index >= first_pairs + sixth
    ).astype(jnp.int32)
    offset = jnp.where(axis_id == 0, 0, jnp.where(axis_id == 1, first_pairs, first_pairs + sixth))
    axis_width = jnp.where(axis_id == 0, 2 * first_pairs, 2 * sixth)
    exponent = 2.0 * (pair_index - offset).astype(jnp.float32) / axis_width.astype(jnp.float32)
    frequency = jnp.exp(-exponent * math.log(10000.0))
    angles = jnp.zeros((coords.shape[1], half_size), jnp.float32)
    for which_axis in range(3):
        chosen = jnp.where(axis_id == which_axis, frequency, 0.0)
        angles = angles + coords[which_axis].astype(jnp.float32)[:, None] * chosen[None, :]
    return angles


def rotate_heads(source, angles):
    half_size = source.shape[-1] // 2
    cos_angle = jnp.cos(angles)[:, None, :]
    sin_angle = jnp.sin(angles)[:, None, :]
    front_half = source[..., :half_size]
    back_half = source[..., half_size:]
    return jnp.concatenate(
        [
            front_half * cos_angle - back_half * sin_angle,
            back_half * cos_angle + front_half * sin_angle,
        ],
        axis=-1,
    )


def split_heads(source):
    return source.reshape(source.shape[0], -1, HD)


def rotated(source, angles):
    row_count = source.shape[0]
    return (
        rotate_heads(split_heads(source).astype(jnp.float32), angles)
        .astype(jnp.bfloat16)
        .reshape(row_count, -1)
    )


def softmax_rows(scores):
    row_peak = jnp.max(scores, axis=-1, keepdims=True)
    exponent = jnp.exp(scores - row_peak)
    return exponent / jnp.sum(exponent, axis=-1, keepdims=True)


def attend_plain(queries, key_rows, value_rows):
    scores = jnp.einsum(
        "qhd,khd->hqk", queries, key_rows, preferred_element_type=jnp.float32
    ) * HD ** (-0.5)
    rounded = softmax_rows(scores).astype(jnp.bfloat16)
    return jnp.einsum("hqk,khd->qhd", rounded, value_rows, preferred_element_type=jnp.float32)


def attend_tangent(queries, key_rows, value_rows, query_dir, key_dir, value_dir):
    score_scale = HD ** (-0.5)
    scores = (
        jnp.einsum("qhd,khd->hqk", queries, key_rows, preferred_element_type=jnp.float32)
        * score_scale
    )
    weights = softmax_rows(scores)
    rounded = weights.astype(jnp.bfloat16)
    primal = jnp.einsum("hqk,khd->qhd", rounded, value_rows, preferred_element_type=jnp.float32)
    score_dir = (
        jnp.einsum("qhd,khd->hqk", query_dir, key_rows, preferred_element_type=jnp.float32)
        + jnp.einsum("qhd,khd->hqk", queries, key_dir, preferred_element_type=jnp.float32)
    ) * score_scale
    weight_dir = weights * (score_dir - jnp.sum(weights * score_dir, axis=-1, keepdims=True))
    rounded_dir = weight_dir.astype(jnp.bfloat16)
    tangent = jnp.einsum(
        "hqk,khd->qhd", rounded_dir, value_rows, preferred_element_type=jnp.float32
    ) + jnp.einsum("hqk,khd->qhd", rounded, value_dir, preferred_element_type=jnp.float32)
    return (primal, tangent)


SCORE_SCALE = HD ** (-0.5)


def rope_tables(angles):
    cos_angle = jnp.cos(angles)
    sin_angle = jnp.sin(angles)
    return (
        jnp.concatenate([cos_angle, cos_angle], axis=-1),
        jnp.concatenate([-sin_angle, sin_angle], axis=-1),
    )


def rotate_block(block, cos_ref, sin_ref):
    source = block.astype(jnp.float32)
    swapped = pltpu.roll(source, HD // 2, 1)
    return (source * cos_ref[...] + swapped * sin_ref[...]).astype(jnp.bfloat16)


def scores_of(queries, key_rows):
    return (
        lax.dot_general(
            queries, key_rows, (((1,), (1,)), ((), ())), preferred_element_type=jnp.float32
        )
        * SCORE_SCALE
    )


def softmax_block(scores):
    exponent = jnp.exp(scores - jnp.max(scores, axis=-1, keepdims=True))
    return exponent / jnp.sum(exponent, axis=-1, keepdims=True)


def teacher_kernel(scal, cos_ref, sin_ref, q0, k0, v0, q1, k1, v1, out_ref):
    def attend(q_ref, k_ref, v_ref):
        weights = softmax_block(
            scores_of(rotate_block(q_ref[...], cos_ref, sin_ref), rotate_block(k_ref[...], cos_ref, sin_ref))
        )
        return jnp.dot(weights.astype(jnp.bfloat16), v_ref[...], preferred_element_type=jnp.float32)

    first = attend(q0, k0, v0)
    second = attend(q1, k1, v1)
    pick_first = scal[1] == 0.0
    cond_out = jnp.where(pick_first, first, second)
    uncond_out = jnp.where(pick_first, second, first)
    out_ref[...] = (scal[0] * (uncond_out + guidance * (cond_out - uncond_out))).astype(jnp.bfloat16)


def student_kernel(scal, cos_ref, sin_ref, q, k, v, qt, kt, vt, term_ref, att_ref):
    queries = rotate_block(q[...], cos_ref, sin_ref)
    key_rows = rotate_block(k[...], cos_ref, sin_ref)
    query_dir = rotate_block(qt[...], cos_ref, sin_ref)
    key_dir = rotate_block(kt[...], cos_ref, sin_ref)
    weights = softmax_block(scores_of(queries, key_rows))
    rounded = weights.astype(jnp.bfloat16)
    primal = jnp.dot(rounded, v[...], preferred_element_type=jnp.float32)
    score_dir = (
        lax.dot_general(query_dir, key_rows, (((1,), (1,)), ((), ())), preferred_element_type=jnp.float32)
        + lax.dot_general(queries, key_dir, (((1,), (1,)), ((), ())), preferred_element_type=jnp.float32)
    ) * SCORE_SCALE
    weight_dir = weights * (score_dir - jnp.sum(weights * score_dir, axis=-1, keepdims=True))
    tangent = jnp.dot(weight_dir.astype(jnp.bfloat16), v[...], preferred_element_type=jnp.float32) + jnp.dot(
        rounded, vt[...], preferred_element_type=jnp.float32
    )
    term_ref[...] = (scal[0] * primal - scal[1] * tangent).astype(jnp.bfloat16)
    att_ref[...] = primal.astype(jnp.bfloat16)


def head_call(kernel, scal, tables, operands, outputs):
    seq, cols = outputs[0].shape
    heads = cols // HD
    head_block = pl.BlockSpec((seq, HD), lambda h: (0, h))
    table_block = pl.BlockSpec((seq, HD), lambda h: (0, 0))
    in_specs = [pl.BlockSpec(memory_space=pltpu.SMEM), table_block, table_block]
    for operand in operands:
        if operand.ndim == 2:
            in_specs.append(head_block)
        else:
            in_specs.append(pl.BlockSpec((None, seq, HD), lambda h, s=operand.index: (s, 0, h)))
    return pl.pallas_call(
        kernel,
        grid=(heads,),
        in_specs=in_specs,
        out_specs=[head_block] * len(outputs),
        out_shape=outputs,
        compiler_params=pltpu.CompilerParams(dimension_semantics=("arbitrary",)),
    )(scal, *tables, *[o.array for o in operands])


class Operand:
    def __init__(self, array, index=None):
        self.array = array
        self.index = index
        self.ndim = 2 if index is None else 3


def local(
    t_index,
    cond_slot,
    positions,
    latent,
    teacher_query,
    teacher_key,
    teacher_value,
    student_query,
    student_key,
    student_value,
    query_tangent,
    key_tangent,
    value_tangent,
    teacher_out,
    student_out,
):
    groups = lax.axis_size("tensor")
    seq_local = latent.shape[1]
    seq_whole = seq_local * groups
    row_start = lax.axis_index("tensor") * seq_local
    time_value = 0.2 + 1.2 * (t_index[0].astype(jnp.float32) + 0.5) / STEPS
    cos_time = jnp.cos(time_value)
    sin_time = jnp.sin(time_value)
    angles_whole = rope_angles(positions[0])
    tables = rope_tables(angles_whole)
    arrived = [
        lax.all_to_all(source[0], "tensor", split_axis=1, concat_axis=0, tiled=True)
        for source in (student_query, student_key, student_value, query_tangent, key_tangent, value_tangent)
    ]
    cols = arrived[0].shape[1]
    teacher_scal = jnp.stack(
        [cos_time * cos_time * sigma_data, cond_slot[0].astype(jnp.float32)]
    )
    t_q = teacher_query.reshape((2,) + teacher_query.shape[2:])
    t_k = teacher_key.reshape((2,) + teacher_key.shape[2:])
    t_v = teacher_value.reshape((2,) + teacher_value.shape[2:])
    (teacher_term,) = head_call(
        teacher_kernel,
        teacher_scal,
        tables,
        [Operand(t_q, 0), Operand(t_k, 0), Operand(t_v, 0), Operand(t_q, 1), Operand(t_k, 1), Operand(t_v, 1)],
        [jax.ShapeDtypeStruct((seq_whole, cols), jnp.bfloat16)],
    )
    student_scal = jnp.stack(
        [-(cos_time * cos_time) * sigma_data, cos_time * sin_time * sigma_data]
    )
    student_term, attended = head_call(
        student_kernel,
        student_scal,
        tables,
        [Operand(a) for a in arrived],
        [jax.ShapeDtypeStruct((seq_whole, cols), jnp.bfloat16)] * 2,
    )
    stacked = jnp.stack([student_out, teacher_out])
    pieces = lax.all_gather(stacked, "dp", axis=2, tiled=True)
    partial_value = jnp.dot(student_term, pieces[0], preferred_element_type=jnp.float32) + jnp.dot(
        teacher_term, pieces[1], preferred_element_type=jnp.float32
    )
    latent_weight = cos_time * sin_time
    pieces_in = lax.all_to_all(
        partial_value.astype(jnp.bfloat16).reshape(groups, seq_local, -1),
        "tensor",
        split_axis=0,
        concat_axis=0,
        tiled=True,
    )
    velocity = jnp.sum(pieces_in.astype(jnp.float32), axis=0)
    target = (velocity - latent_weight * latent[0].astype(jnp.float32)).astype(jnp.bfloat16)
    clips = lax.axis_size("dp")
    width = target.shape[1] // clips
    attended_all = lax.all_gather(attended, "dp", axis=0, tiled=False)
    grad_scale = -2.0 / math.sqrt(clips * seq_whole)
    half = width // 2
    split_target = target.reshape(seq_local, clips, width)
    pieces = []
    for part in range(2):
        columns = lax.all_to_all(
            split_target[:, :, part * half : (part + 1) * half], "dp", split_axis=1, concat_axis=1, tiled=True
        )
        columns = lax.all_gather(columns, "tensor", axis=0, tiled=True)
        terms = jnp.einsum(
            "csi,scd->cid", attended_all, columns, preferred_element_type=jnp.float32
        )
        pieces.append(jnp.sum((grad_scale * terms).astype(jnp.bfloat16).astype(jnp.float32), axis=0))
    gradient = jnp.concatenate(pieces, axis=1)
    return (target[None], gradient)


def solution(mesh):
    placed = (
        P("dp"),
        P("dp"),
        P("dp", None, None),
        P("dp", "tensor", None),
        P(None, "dp", None, "tensor"),
        P(None, "dp", None, "tensor"),
        P(None, "dp", None, "tensor"),
        P("dp", "tensor", None),
        P("dp", "tensor", None),
        P("dp", "tensor", None),
        P("dp", "tensor", None),
        P("dp", "tensor", None),
        P("dp", "tensor", None),
        P("tensor", "dp"),
        P("tensor", "dp"),
    )
    return jax.shard_map(
        local,
        mesh=mesh,
        in_specs=placed,
        out_specs=(P("dp", "tensor", None), P("tensor", "dp")),
        check_vma=False,
    )
```

```python
import math

import jax
import jax.numpy as jnp
from jax import lax
from jax.experimental import pallas as pl
from jax.experimental.pallas import tpu as pltpu
from jax.sharding import PartitionSpec as P

HD = 128
STEPS = 1000


sigma_data = 0.5
guidance = 5.0


def rope_angles(coords):
    half_size = HD // 2
    sixth = HD // 6
    first_pairs = half_size - 2 * sixth
    pair_index = jnp.arange(half_size)
    axis_id = (pair_index >= first_pairs).astype(jnp.int32) + (
        pair_index >= first_pairs + sixth
    ).astype(jnp.int32)
    offset = jnp.where(axis_id == 0, 0, jnp.where(axis_id == 1, first_pairs, first_pairs + sixth))
    axis_width = jnp.where(axis_id == 0, 2 * first_pairs, 2 * sixth)
    exponent = 2.0 * (pair_index - offset).astype(jnp.float32) / axis_width.astype(jnp.float32)
    frequency = jnp.exp(-exponent * math.log(10000.0))
    angles = jnp.zeros((coords.shape[1], half_size), jnp.float32)
    for which_axis in range(3):
        chosen = jnp.where(axis_id == which_axis, frequency, 0.0)
        angles = angles + coords[which_axis].astype(jnp.float32)[:, None] * chosen[None, :]
    return angles


def rotate_heads(source, angles):
    half_size = source.shape[-1] // 2
    cos_angle = jnp.cos(angles)[:, None, :]
    sin_angle = jnp.sin(angles)[:, None, :]
    front_half = source[..., :half_size]
    back_half = source[..., half_size:]
    return jnp.concatenate(
        [
            front_half * cos_angle - back_half * sin_angle,
            back_half * cos_angle + front_half * sin_angle,
        ],
        axis=-1,
    )


def split_heads(source):
    return source.reshape(source.shape[0], -1, HD)


def rotated(source, angles):
    row_count = source.shape[0]
    return (
        rotate_heads(split_heads(source).astype(jnp.float32), angles)
        .astype(jnp.bfloat16)
        .reshape(row_count, -1)
    )


def softmax_rows(scores):
    row_peak = jnp.max(scores, axis=-1, keepdims=True)
    exponent = jnp.exp(scores - row_peak)
    return exponent / jnp.sum(exponent, axis=-1, keepdims=True)


def attend_plain(queries, key_rows, value_rows):
    scores = jnp.einsum(
        "qhd,khd->hqk", queries, key_rows, preferred_element_type=jnp.float32
    ) * HD ** (-0.5)
    rounded = softmax_rows(scores).astype(jnp.bfloat16)
    return jnp.einsum("hqk,khd->qhd", rounded, value_rows, preferred_element_type=jnp.float32)


def attend_tangent(queries, key_rows, value_rows, query_dir, key_dir, value_dir):
    score_scale = HD ** (-0.5)
    scores = (
        jnp.einsum("qhd,khd->hqk", queries, key_rows, preferred_element_type=jnp.float32)
        * score_scale
    )
    weights = softmax_rows(scores)
    rounded = weights.astype(jnp.bfloat16)
    primal = jnp.einsum("hqk,khd->qhd", rounded, value_rows, preferred_element_type=jnp.float32)
    score_dir = (
        jnp.einsum("qhd,khd->hqk", query_dir, key_rows, preferred_element_type=jnp.float32)
        + jnp.einsum("qhd,khd->hqk", queries, key_dir, preferred_element_type=jnp.float32)
    ) * score_scale
    weight_dir = weights * (score_dir - jnp.sum(weights * score_dir, axis=-1, keepdims=True))
    rounded_dir = weight_dir.astype(jnp.bfloat16)
    tangent = jnp.einsum(
        "hqk,khd->qhd", rounded_dir, value_rows, preferred_element_type=jnp.float32
    ) + jnp.einsum("hqk,khd->qhd", rounded, value_dir, preferred_element_type=jnp.float32)
    return (primal, tangent)


SCORE_SCALE = HD ** (-0.5)


def rope_tables(angles):
    cos_angle = jnp.cos(angles)
    sin_angle = jnp.sin(angles)
    return (
        jnp.concatenate([cos_angle, cos_angle], axis=-1),
        jnp.concatenate([-sin_angle, sin_angle], axis=-1),
    )


def rotate_block(block, cos_ref, sin_ref):
    source = block.astype(jnp.float32)
    swapped = pltpu.roll(source, HD // 2, 1)
    return (source * cos_ref[...] + swapped * sin_ref[...]).astype(jnp.bfloat16)


def scores_of(queries, key_rows):
    return (
        lax.dot_general(
            queries, key_rows, (((1,), (1,)), ((), ())), preferred_element_type=jnp.float32
        )
        * SCORE_SCALE
    )


def softmax_block(scores):
    exponent = jnp.exp(scores - jnp.max(scores, axis=-1, keepdims=True))
    return exponent / jnp.sum(exponent, axis=-1, keepdims=True)


def teacher_kernel(scal, cos_ref, sin_ref, q0, k0, v0, q1, k1, v1, out_ref):
    def attend(q_ref, k_ref, v_ref):
        weights = softmax_block(
            scores_of(rotate_block(q_ref[...], cos_ref, sin_ref), rotate_block(k_ref[...], cos_ref, sin_ref))
        )
        return jnp.dot(weights.astype(jnp.bfloat16), v_ref[...], preferred_element_type=jnp.float32)

    first = attend(q0, k0, v0)
    second = attend(q1, k1, v1)
    pick_first = scal[1] == 0.0
    cond_out = jnp.where(pick_first, first, second)
    uncond_out = jnp.where(pick_first, second, first)
    out_ref[...] = (scal[0] * (uncond_out + guidance * (cond_out - uncond_out))).astype(jnp.bfloat16)


def student_kernel(scal, cos_ref, sin_ref, q, k, v, qt, kt, vt, term_ref, att_ref):
    queries = rotate_block(q[...], cos_ref, sin_ref)
    key_rows = rotate_block(k[...], cos_ref, sin_ref)
    query_dir = rotate_block(qt[...], cos_ref, sin_ref)
    key_dir = rotate_block(kt[...], cos_ref, sin_ref)
    weights = softmax_block(scores_of(queries, key_rows))
    rounded = weights.astype(jnp.bfloat16)
    primal = jnp.dot(rounded, v[...], preferred_element_type=jnp.float32)
    score_dir = (
        lax.dot_general(query_dir, key_rows, (((1,), (1,)), ((), ())), preferred_element_type=jnp.float32)
        + lax.dot_general(queries, key_dir, (((1,), (1,)), ((), ())), preferred_element_type=jnp.float32)
    ) * SCORE_SCALE
    weight_dir = weights * (score_dir - jnp.sum(weights * score_dir, axis=-1, keepdims=True))
    tangent = jnp.dot(weight_dir.astype(jnp.bfloat16), v[...], preferred_element_type=jnp.float32) + jnp.dot(
        rounded, vt[...], preferred_element_type=jnp.float32
    )
    term_ref[...] = (scal[0] * primal - scal[1] * tangent).astype(jnp.bfloat16)
    att_ref[...] = primal.astype(jnp.bfloat16)


def head_call(kernel, scal, tables, operands, outputs):
    seq, cols = outputs[0].shape
    heads = cols // HD
    head_block = pl.BlockSpec((seq, HD), lambda h: (0, h))
    table_block = pl.BlockSpec((seq, HD), lambda h: (0, 0))
    in_specs = [pl.BlockSpec(memory_space=pltpu.SMEM), table_block, table_block]
    for operand in operands:
        if operand.ndim == 2:
            in_specs.append(head_block)
        else:
            in_specs.append(pl.BlockSpec((None, seq, HD), lambda h, s=operand.index: (s, 0, h)))
    return pl.pallas_call(
        kernel,
        grid=(heads,),
        in_specs=in_specs,
        out_specs=[head_block] * len(outputs),
        out_shape=outputs,
        compiler_params=pltpu.CompilerParams(dimension_semantics=("arbitrary",)),
    )(scal, *tables, *[o.array for o in operands])


class Operand:
    def __init__(self, array, index=None):
        self.array = array
        self.index = index
        self.ndim = 2 if index is None else 3


def local(
    t_index,
    cond_slot,
    positions,
    latent,
    teacher_query,
    teacher_key,
    teacher_value,
    student_query,
    student_key,
    student_value,
    query_tangent,
    key_tangent,
    value_tangent,
    teacher_out,
    student_out,
):
    groups = lax.axis_size("tensor")
    seq_local = latent.shape[1]
    seq_whole = seq_local * groups
    row_start = lax.axis_index("tensor") * seq_local
    time_value = 0.2 + 1.2 * (t_index[0].astype(jnp.float32) + 0.5) / STEPS
    cos_time = jnp.cos(time_value)
    sin_time = jnp.sin(time_value)
    angles_whole = rope_angles(positions[0])
    tables = rope_tables(angles_whole)
    arrived = [
        lax.all_to_all(source[0], "tensor", split_axis=1, concat_axis=0, tiled=True)
        for source in (student_query, student_key, student_value, query_tangent, key_tangent, value_tangent)
    ]
    cols = arrived[0].shape[1]
    teacher_scal = jnp.stack(
        [cos_time * cos_time * sigma_data, cond_slot[0].astype(jnp.float32)]
    )
    t_q = teacher_query.reshape((2,) + teacher_query.shape[2:])
    t_k = teacher_key.reshape((2,) + teacher_key.shape[2:])
    t_v = teacher_value.reshape((2,) + teacher_value.shape[2:])
    (teacher_term,) = head_call(
        teacher_kernel,
        teacher_scal,
        tables,
        [Operand(t_q, 0), Operand(t_k, 0), Operand(t_v, 0), Operand(t_q, 1), Operand(t_k, 1), Operand(t_v, 1)],
        [jax.ShapeDtypeStruct((seq_whole, cols), jnp.bfloat16)],
    )
    student_scal = jnp.stack(
        [-(cos_time * cos_time) * sigma_data, cos_time * sin_time * sigma_data]
    )
    student_term, attended = head_call(
        student_kernel,
        student_scal,
        tables,
        [Operand(a) for a in arrived],
        [jax.ShapeDtypeStruct((seq_whole, cols), jnp.bfloat16)] * 2,
    )
    teacher_whole = lax.all_gather(teacher_out, "dp", axis=1, tiled=True)
    student_whole = lax.all_gather(student_out, "dp", axis=1, tiled=True)
    teacher_partial = jnp.dot(teacher_term, teacher_whole, preferred_element_type=jnp.float32)
    teacher_partial, student_whole = lax.optimization_barrier((teacher_partial, student_whole))
    partial_value = jnp.dot(student_term, student_whole, preferred_element_type=jnp.float32) + teacher_partial
    latent_weight = cos_time * sin_time
    pieces_in = lax.all_to_all(
        partial_value.astype(jnp.bfloat16).reshape(groups, seq_local, -1),
        "tensor",
        split_axis=0,
        concat_axis=0,
        tiled=True,
    )
    velocity = jnp.sum(pieces_in.astype(jnp.float32), axis=0)
    target = (velocity - latent_weight * latent[0].astype(jnp.float32)).astype(jnp.bfloat16)
    clips = lax.axis_size("dp")
    width = target.shape[1] // clips
    attended_all = lax.all_gather(attended, "dp", axis=0, tiled=False)
    grad_scale = -2.0 / math.sqrt(clips * seq_whole)
    half = width // 2
    split_target = target.reshape(seq_local, clips, width)
    pieces = []
    for part in range(2):
        columns = lax.all_to_all(
            split_target[:, :, part * half : (part + 1) * half], "dp", split_axis=1, concat_axis=1, tiled=True
        )
        columns = lax.all_gather(columns, "tensor", axis=0, tiled=True)
        terms = jnp.einsum(
            "csi,scd->cid", attended_all, columns, preferred_element_type=jnp.float32
        )
        pieces.append(jnp.sum((grad_scale * terms).astype(jnp.bfloat16).astype(jnp.float32), axis=0))
    gradient = jnp.concatenate(pieces, axis=1)
    return (target[None], gradient)


def solution(mesh):
    placed = (
        P("dp"),
        P("dp"),
        P("dp", None, None),
        P("dp", "tensor", None),
        P(None, "dp", None, "tensor"),
        P(None, "dp", None, "tensor"),
        P(None, "dp", None, "tensor"),
        P("dp", "tensor", None),
        P("dp", "tensor", None),
        P("dp", "tensor", None),
        P("dp", "tensor", None),
        P("dp", "tensor", None),
        P("dp", "tensor", None),
        P("tensor", "dp"),
        P("tensor", "dp"),
    )
    return jax.shard_map(
        local,
        mesh=mesh,
        in_specs=placed,
        out_specs=(P("dp", "tensor", None), P("tensor", "dp")),
        check_vma=False,
    )
```

```python
import math

import jax
import jax.numpy as jnp
from jax import lax
from jax.experimental import pallas as pl
from jax.experimental.pallas import tpu as pltpu
from jax.sharding import PartitionSpec as P

HD = 128
STEPS = 1000


sigma_data = 0.5
guidance = 5.0


def rope_angles(coords):
    half_size = HD // 2
    sixth = HD // 6
    first_pairs = half_size - 2 * sixth
    pair_index = jnp.arange(half_size)
    axis_id = (pair_index >= first_pairs).astype(jnp.int32) + (
        pair_index >= first_pairs + sixth
    ).astype(jnp.int32)
    offset = jnp.where(axis_id == 0, 0, jnp.where(axis_id == 1, first_pairs, first_pairs + sixth))
    axis_width = jnp.where(axis_id == 0, 2 * first_pairs, 2 * sixth)
    exponent = 2.0 * (pair_index - offset).astype(jnp.float32) / axis_width.astype(jnp.float32)
    frequency = jnp.exp(-exponent * math.log(10000.0))
    angles = jnp.zeros((coords.shape[1], half_size), jnp.float32)
    for which_axis in range(3):
        chosen = jnp.where(axis_id == which_axis, frequency, 0.0)
        angles = angles + coords[which_axis].astype(jnp.float32)[:, None] * chosen[None, :]
    return angles


def rotate_heads(source, angles):
    half_size = source.shape[-1] // 2
    cos_angle = jnp.cos(angles)[:, None, :]
    sin_angle = jnp.sin(angles)[:, None, :]
    front_half = source[..., :half_size]
    back_half = source[..., half_size:]
    return jnp.concatenate(
        [
            front_half * cos_angle - back_half * sin_angle,
            back_half * cos_angle + front_half * sin_angle,
        ],
        axis=-1,
    )


def split_heads(source):
    return source.reshape(source.shape[0], -1, HD)


def rotated(source, angles):
    row_count = source.shape[0]
    return (
        rotate_heads(split_heads(source).astype(jnp.float32), angles)
        .astype(jnp.bfloat16)
        .reshape(row_count, -1)
    )


def softmax_rows(scores):
    row_peak = jnp.max(scores, axis=-1, keepdims=True)
    exponent = jnp.exp(scores - row_peak)
    return exponent / jnp.sum(exponent, axis=-1, keepdims=True)


def attend_plain(queries, key_rows, value_rows):
    scores = jnp.einsum(
        "qhd,khd->hqk", queries, key_rows, preferred_element_type=jnp.float32
    ) * HD ** (-0.5)
    rounded = softmax_rows(scores).astype(jnp.bfloat16)
    return jnp.einsum("hqk,khd->qhd", rounded, value_rows, preferred_element_type=jnp.float32)


def attend_tangent(queries, key_rows, value_rows, query_dir, key_dir, value_dir):
    score_scale = HD ** (-0.5)
    scores = (
        jnp.einsum("qhd,khd->hqk", queries, key_rows, preferred_element_type=jnp.float32)
        * score_scale
    )
    weights = softmax_rows(scores)
    rounded = weights.astype(jnp.bfloat16)
    primal = jnp.einsum("hqk,khd->qhd", rounded, value_rows, preferred_element_type=jnp.float32)
    score_dir = (
        jnp.einsum("qhd,khd->hqk", query_dir, key_rows, preferred_element_type=jnp.float32)
        + jnp.einsum("qhd,khd->hqk", queries, key_dir, preferred_element_type=jnp.float32)
    ) * score_scale
    weight_dir = weights * (score_dir - jnp.sum(weights * score_dir, axis=-1, keepdims=True))
    rounded_dir = weight_dir.astype(jnp.bfloat16)
    tangent = jnp.einsum(
        "hqk,khd->qhd", rounded_dir, value_rows, preferred_element_type=jnp.float32
    ) + jnp.einsum("hqk,khd->qhd", rounded, value_dir, preferred_element_type=jnp.float32)
    return (primal, tangent)


SCORE_SCALE = HD ** (-0.5)


def rope_tables(angles):
    cos_angle = jnp.cos(angles)
    sin_angle = jnp.sin(angles)
    return (
        jnp.concatenate([cos_angle, cos_angle], axis=-1),
        jnp.concatenate([-sin_angle, sin_angle], axis=-1),
    )


def rotate_block(block, cos_ref, sin_ref):
    source = block.astype(jnp.float32)
    swapped = pltpu.roll(source, HD // 2, 1)
    return (source * cos_ref[...] + swapped * sin_ref[...]).astype(jnp.bfloat16)


def scores_of(queries, key_rows):
    return (
        lax.dot_general(
            queries, key_rows, (((1,), (1,)), ((), ())), preferred_element_type=jnp.float32
        )
        * SCORE_SCALE
    )


def softmax_block(scores):
    exponent = jnp.exp(scores - jnp.max(scores, axis=-1, keepdims=True))
    return exponent / jnp.sum(exponent, axis=-1, keepdims=True)


def teacher_kernel(scal, cos_ref, sin_ref, q0, k0, v0, q1, k1, v1, out_ref):
    def attend(q_ref, k_ref, v_ref):
        weights = softmax_block(
            scores_of(rotate_block(q_ref[...], cos_ref, sin_ref), rotate_block(k_ref[...], cos_ref, sin_ref))
        )
        return jnp.dot(weights.astype(jnp.bfloat16), v_ref[...], preferred_element_type=jnp.float32)

    first = attend(q0, k0, v0)
    second = attend(q1, k1, v1)
    pick_first = scal[1] == 0.0
    cond_out = jnp.where(pick_first, first, second)
    uncond_out = jnp.where(pick_first, second, first)
    out_ref[...] = (scal[0] * (uncond_out + guidance * (cond_out - uncond_out))).astype(jnp.bfloat16)


def student_kernel(scal, cos_ref, sin_ref, q, k, v, qt, kt, vt, term_ref, att_ref):
    queries = rotate_block(q[...], cos_ref, sin_ref)
    key_rows = rotate_block(k[...], cos_ref, sin_ref)
    query_dir = rotate_block(qt[...], cos_ref, sin_ref)
    key_dir = rotate_block(kt[...], cos_ref, sin_ref)
    weights = softmax_block(scores_of(queries, key_rows))
    rounded = weights.astype(jnp.bfloat16)
    primal = jnp.dot(rounded, v[...], preferred_element_type=jnp.float32)
    score_dir = (
        lax.dot_general(query_dir, key_rows, (((1,), (1,)), ((), ())), preferred_element_type=jnp.float32)
        + lax.dot_general(queries, key_dir, (((1,), (1,)), ((), ())), preferred_element_type=jnp.float32)
    ) * SCORE_SCALE
    weight_dir = weights * (score_dir - jnp.sum(weights * score_dir, axis=-1, keepdims=True))
    tangent = jnp.dot(weight_dir.astype(jnp.bfloat16), v[...], preferred_element_type=jnp.float32) + jnp.dot(
        rounded, vt[...], preferred_element_type=jnp.float32
    )
    term_ref[...] = (scal[0] * primal - scal[1] * tangent).astype(jnp.bfloat16)
    att_ref[...] = primal.astype(jnp.bfloat16)


def head_call(kernel, scal, tables, operands, outputs):
    seq, cols = outputs[0].shape
    heads = cols // HD
    head_block = pl.BlockSpec((seq, HD), lambda h: (0, h))
    table_block = pl.BlockSpec((seq, HD), lambda h: (0, 0))
    in_specs = [pl.BlockSpec(memory_space=pltpu.SMEM), table_block, table_block]
    for operand in operands:
        if operand.ndim == 2:
            in_specs.append(head_block)
        else:
            in_specs.append(pl.BlockSpec((None, seq, HD), lambda h, s=operand.index: (s, 0, h)))
    return pl.pallas_call(
        kernel,
        grid=(heads,),
        in_specs=in_specs,
        out_specs=[head_block] * len(outputs),
        out_shape=outputs,
        compiler_params=pltpu.CompilerParams(dimension_semantics=("arbitrary",)),
    )(scal, *tables, *[o.array for o in operands])


class Operand:
    def __init__(self, array, index=None):
        self.array = array
        self.index = index
        self.ndim = 2 if index is None else 3


def local(
    t_index,
    cond_slot,
    positions,
    latent,
    teacher_query,
    teacher_key,
    teacher_value,
    student_query,
    student_key,
    student_value,
    query_tangent,
    key_tangent,
    value_tangent,
    teacher_out,
    student_out,
):
    groups = lax.axis_size("tensor")
    seq_local = latent.shape[1]
    seq_whole = seq_local * groups
    row_start = lax.axis_index("tensor") * seq_local
    time_value = 0.2 + 1.2 * (t_index[0].astype(jnp.float32) + 0.5) / STEPS
    cos_time = jnp.cos(time_value)
    sin_time = jnp.sin(time_value)
    angles_whole = rope_angles(positions[0])
    tables = rope_tables(angles_whole)
    arrived = [
        lax.all_to_all(source[0], "tensor", split_axis=1, concat_axis=0, tiled=True)
        for source in (student_query, student_key, student_value, query_tangent, key_tangent, value_tangent)
    ]
    cols = arrived[0].shape[1]
    teacher_scal = jnp.stack(
        [cos_time * cos_time * sigma_data, cond_slot[0].astype(jnp.float32)]
    )
    t_q = teacher_query.reshape((2,) + teacher_query.shape[2:])
    t_k = teacher_key.reshape((2,) + teacher_key.shape[2:])
    t_v = teacher_value.reshape((2,) + teacher_value.shape[2:])
    (teacher_term,) = head_call(
        teacher_kernel,
        teacher_scal,
        tables,
        [Operand(t_q, 0), Operand(t_k, 0), Operand(t_v, 0), Operand(t_q, 1), Operand(t_k, 1), Operand(t_v, 1)],
        [jax.ShapeDtypeStruct((seq_whole, cols), jnp.bfloat16)],
    )
    student_scal = jnp.stack(
        [-(cos_time * cos_time) * sigma_data, cos_time * sin_time * sigma_data]
    )
    student_term, attended = head_call(
        student_kernel,
        student_scal,
        tables,
        [Operand(a) for a in arrived],
        [jax.ShapeDtypeStruct((seq_whole, cols), jnp.bfloat16)] * 2,
    )
    stacked = jnp.stack([student_out, teacher_out])
    pieces = lax.all_gather(stacked, "dp", axis=2, tiled=True)
    partial_value = jnp.dot(student_term, pieces[0], preferred_element_type=jnp.float32) + jnp.dot(
        teacher_term, pieces[1], preferred_element_type=jnp.float32
    )
    latent_weight = cos_time * sin_time
    pieces_in = lax.all_to_all(
        partial_value.astype(jnp.bfloat16).reshape(groups, seq_local, -1),
        "tensor",
        split_axis=0,
        concat_axis=0,
        tiled=True,
    )
    velocity = jnp.sum(pieces_in.astype(jnp.float32), axis=0)
    target = (velocity - latent_weight * latent[0].astype(jnp.float32)).astype(jnp.bfloat16)
    clips = lax.axis_size("dp")
    width = target.shape[1] // clips
    attended_all = lax.all_gather(attended, "dp", axis=0, tiled=False)
    grad_scale = -2.0 / math.sqrt(clips * seq_whole)
    half = width // 2
    split_target = target.reshape(seq_local, clips, width)
    pieces = []
    me = lax.axis_index("dp")
    by_block = jnp.transpose(split_target, (1, 0, 2))
    for part in range(2):
        blocks = by_block[:, :, part * half : (part + 1) * half]
        received = [lax.dynamic_index_in_dim(blocks, me, 0, keepdims=False)]
        for shift in range(1, clips):
            outgoing = lax.dynamic_index_in_dim(blocks, (me + shift) % clips, 0, keepdims=False)
            received.append(
                lax.ppermute(outgoing, "dp", [(i, (i + shift) % clips) for i in range(clips)])
            )
        order = (me - jnp.arange(clips)) % clips
        columns = jnp.take(jnp.stack(received), order, axis=0)
        columns = lax.all_gather(columns, "tensor", axis=1, tiled=True)
        terms = jnp.einsum(
            "csi,csd->cid", attended_all, columns, preferred_element_type=jnp.float32
        )
        pieces.append(jnp.sum((grad_scale * terms).astype(jnp.bfloat16).astype(jnp.float32), axis=0))
    gradient = jnp.concatenate(pieces, axis=1)
    return (target[None], gradient)


def solution(mesh):
    placed = (
        P("dp"),
        P("dp"),
        P("dp", None, None),
        P("dp", "tensor", None),
        P(None, "dp", None, "tensor"),
        P(None, "dp", None, "tensor"),
        P(None, "dp", None, "tensor"),
        P("dp", "tensor", None),
        P("dp", "tensor", None),
        P("dp", "tensor", None),
        P("dp", "tensor", None),
        P("dp", "tensor", None),
        P("dp", "tensor", None),
        P("tensor", "dp"),
        P("tensor", "dp"),
    )
    return jax.shard_map(
        local,
        mesh=mesh,
        in_specs=placed,
        out_specs=(P("dp", "tensor", None), P("tensor", "dp")),
        check_vma=False,
    )
```

```python
import math

import jax
import jax.numpy as jnp
from jax import lax
from jax.experimental import pallas as pl
from jax.experimental.pallas import tpu as pltpu
from jax.sharding import PartitionSpec as P

HD = 128
STEPS = 1000


sigma_data = 0.5
guidance = 5.0


def rope_angles(coords):
    half_size = HD // 2
    sixth = HD // 6
    first_pairs = half_size - 2 * sixth
    pair_index = jnp.arange(half_size)
    axis_id = (pair_index >= first_pairs).astype(jnp.int32) + (
        pair_index >= first_pairs + sixth
    ).astype(jnp.int32)
    offset = jnp.where(axis_id == 0, 0, jnp.where(axis_id == 1, first_pairs, first_pairs + sixth))
    axis_width = jnp.where(axis_id == 0, 2 * first_pairs, 2 * sixth)
    exponent = 2.0 * (pair_index - offset).astype(jnp.float32) / axis_width.astype(jnp.float32)
    frequency = jnp.exp(-exponent * math.log(10000.0))
    angles = jnp.zeros((coords.shape[1], half_size), jnp.float32)
    for which_axis in range(3):
        chosen = jnp.where(axis_id == which_axis, frequency, 0.0)
        angles = angles + coords[which_axis].astype(jnp.float32)[:, None] * chosen[None, :]
    return angles


def rotate_heads(source, angles):
    half_size = source.shape[-1] // 2
    cos_angle = jnp.cos(angles)[:, None, :]
    sin_angle = jnp.sin(angles)[:, None, :]
    front_half = source[..., :half_size]
    back_half = source[..., half_size:]
    return jnp.concatenate(
        [
            front_half * cos_angle - back_half * sin_angle,
            back_half * cos_angle + front_half * sin_angle,
        ],
        axis=-1,
    )


def split_heads(source):
    return source.reshape(source.shape[0], -1, HD)


def rotated(source, angles):
    row_count = source.shape[0]
    return (
        rotate_heads(split_heads(source).astype(jnp.float32), angles)
        .astype(jnp.bfloat16)
        .reshape(row_count, -1)
    )


def softmax_rows(scores):
    row_peak = jnp.max(scores, axis=-1, keepdims=True)
    exponent = jnp.exp(scores - row_peak)
    return exponent / jnp.sum(exponent, axis=-1, keepdims=True)


def attend_plain(queries, key_rows, value_rows):
    scores = jnp.einsum(
        "qhd,khd->hqk", queries, key_rows, preferred_element_type=jnp.float32
    ) * HD ** (-0.5)
    rounded = softmax_rows(scores).astype(jnp.bfloat16)
    return jnp.einsum("hqk,khd->qhd", rounded, value_rows, preferred_element_type=jnp.float32)


def attend_tangent(queries, key_rows, value_rows, query_dir, key_dir, value_dir):
    score_scale = HD ** (-0.5)
    scores = (
        jnp.einsum("qhd,khd->hqk", queries, key_rows, preferred_element_type=jnp.float32)
        * score_scale
    )
    weights = softmax_rows(scores)
    rounded = weights.astype(jnp.bfloat16)
    primal = jnp.einsum("hqk,khd->qhd", rounded, value_rows, preferred_element_type=jnp.float32)
    score_dir = (
        jnp.einsum("qhd,khd->hqk", query_dir, key_rows, preferred_element_type=jnp.float32)
        + jnp.einsum("qhd,khd->hqk", queries, key_dir, preferred_element_type=jnp.float32)
    ) * score_scale
    weight_dir = weights * (score_dir - jnp.sum(weights * score_dir, axis=-1, keepdims=True))
    rounded_dir = weight_dir.astype(jnp.bfloat16)
    tangent = jnp.einsum(
        "hqk,khd->qhd", rounded_dir, value_rows, preferred_element_type=jnp.float32
    ) + jnp.einsum("hqk,khd->qhd", rounded, value_dir, preferred_element_type=jnp.float32)
    return (primal, tangent)


SCORE_SCALE = HD ** (-0.5)


def rope_tables(angles):
    cos_angle = jnp.cos(angles)
    sin_angle = jnp.sin(angles)
    return (
        jnp.concatenate([cos_angle, cos_angle], axis=-1),
        jnp.concatenate([-sin_angle, sin_angle], axis=-1),
    )


def rotate_block(block, cos_ref, sin_ref):
    source = block.astype(jnp.float32)
    swapped = pltpu.roll(source, HD // 2, 1)
    return (source * cos_ref[...] + swapped * sin_ref[...]).astype(jnp.bfloat16)


def scores_of(queries, key_rows):
    return (
        lax.dot_general(
            queries, key_rows, (((1,), (1,)), ((), ())), preferred_element_type=jnp.float32
        )
        * SCORE_SCALE
    )


def softmax_block(scores):
    exponent = jnp.exp(scores - jnp.max(scores, axis=-1, keepdims=True))
    return exponent / jnp.sum(exponent, axis=-1, keepdims=True)


def teacher_kernel(scal, cos_ref, sin_ref, q0, k0, v0, q1, k1, v1, out_ref):
    def attend(q_ref, k_ref, v_ref):
        weights = softmax_block(
            scores_of(rotate_block(q_ref[...], cos_ref, sin_ref), rotate_block(k_ref[...], cos_ref, sin_ref))
        )
        return jnp.dot(weights.astype(jnp.bfloat16), v_ref[...], preferred_element_type=jnp.float32)

    first = attend(q0, k0, v0)
    second = attend(q1, k1, v1)
    pick_first = scal[1] == 0.0
    cond_out = jnp.where(pick_first, first, second)
    uncond_out = jnp.where(pick_first, second, first)
    out_ref[...] = (scal[0] * (uncond_out + guidance * (cond_out - uncond_out))).astype(jnp.bfloat16)


def student_kernel(scal, cos_ref, sin_ref, q, k, v, qt, kt, vt, term_ref, att_ref):
    queries = rotate_block(q[...], cos_ref, sin_ref)
    key_rows = rotate_block(k[...], cos_ref, sin_ref)
    query_dir = rotate_block(qt[...], cos_ref, sin_ref)
    key_dir = rotate_block(kt[...], cos_ref, sin_ref)
    weights = softmax_block(scores_of(queries, key_rows))
    rounded = weights.astype(jnp.bfloat16)
    primal = jnp.dot(rounded, v[...], preferred_element_type=jnp.float32)
    score_dir = (
        lax.dot_general(query_dir, key_rows, (((1,), (1,)), ((), ())), preferred_element_type=jnp.float32)
        + lax.dot_general(queries, key_dir, (((1,), (1,)), ((), ())), preferred_element_type=jnp.float32)
    ) * SCORE_SCALE
    weight_dir = weights * (score_dir - jnp.sum(weights * score_dir, axis=-1, keepdims=True))
    tangent = jnp.dot(weight_dir.astype(jnp.bfloat16), v[...], preferred_element_type=jnp.float32) + jnp.dot(
        rounded, vt[...], preferred_element_type=jnp.float32
    )
    term_ref[...] = (scal[0] * primal - scal[1] * tangent).astype(jnp.bfloat16)
    att_ref[...] = primal.astype(jnp.bfloat16)


def head_call(kernel, scal, tables, operands, outputs):
    seq, cols = outputs[0].shape
    heads = cols // HD
    head_block = pl.BlockSpec((seq, HD), lambda h: (0, h))
    table_block = pl.BlockSpec((seq, HD), lambda h: (0, 0))
    in_specs = [pl.BlockSpec(memory_space=pltpu.SMEM), table_block, table_block]
    for operand in operands:
        if operand.ndim == 2:
            in_specs.append(head_block)
        else:
            in_specs.append(pl.BlockSpec((None, seq, HD), lambda h, s=operand.index: (s, 0, h)))
    return pl.pallas_call(
        kernel,
        grid=(heads,),
        in_specs=in_specs,
        out_specs=[head_block] * len(outputs),
        out_shape=outputs,
        compiler_params=pltpu.CompilerParams(dimension_semantics=("arbitrary",)),
    )(scal, *tables, *[o.array for o in operands])


class Operand:
    def __init__(self, array, index=None):
        self.array = array
        self.index = index
        self.ndim = 2 if index is None else 3


def local(
    t_index,
    cond_slot,
    positions,
    latent,
    teacher_query,
    teacher_key,
    teacher_value,
    student_query,
    student_key,
    student_value,
    query_tangent,
    key_tangent,
    value_tangent,
    teacher_out,
    student_out,
):
    groups = lax.axis_size("tensor")
    seq_local = latent.shape[1]
    seq_whole = seq_local * groups
    row_start = lax.axis_index("tensor") * seq_local
    time_value = 0.2 + 1.2 * (t_index[0].astype(jnp.float32) + 0.5) / STEPS
    cos_time = jnp.cos(time_value)
    sin_time = jnp.sin(time_value)
    angles_whole = rope_angles(positions[0])
    tables = rope_tables(angles_whole)
    arrived = [
        lax.all_to_all(source[0], "tensor", split_axis=1, concat_axis=0, tiled=True)
        for source in (student_query, student_key, student_value, query_tangent, key_tangent, value_tangent)
    ]
    cols = arrived[0].shape[1]
    teacher_scal = jnp.stack(
        [cos_time * cos_time * sigma_data, cond_slot[0].astype(jnp.float32)]
    )
    t_q = teacher_query.reshape((2,) + teacher_query.shape[2:])
    t_k = teacher_key.reshape((2,) + teacher_key.shape[2:])
    t_v = teacher_value.reshape((2,) + teacher_value.shape[2:])
    (teacher_term,) = head_call(
        teacher_kernel,
        teacher_scal,
        tables,
        [Operand(t_q, 0), Operand(t_k, 0), Operand(t_v, 0), Operand(t_q, 1), Operand(t_k, 1), Operand(t_v, 1)],
        [jax.ShapeDtypeStruct((seq_whole, cols), jnp.bfloat16)],
    )
    student_scal = jnp.stack(
        [-(cos_time * cos_time) * sigma_data, cos_time * sin_time * sigma_data]
    )
    student_term, attended = head_call(
        student_kernel,
        student_scal,
        tables,
        [Operand(a) for a in arrived],
        [jax.ShapeDtypeStruct((seq_whole, cols), jnp.bfloat16)] * 2,
    )
    stacked = jnp.stack([student_out, teacher_out])
    clips = lax.axis_size("dp")
    width = student_out.shape[1]
    half = width // 2
    pieces = lax.all_gather(stacked, "dp", axis=2, tiled=False)
    latent_weight = cos_time * sin_time
    attended_all = lax.all_gather(attended, "dp", axis=0, tiled=False)
    grad_scale = -2.0 / math.sqrt(clips * seq_whole)
    latent_blocks = latent[0].reshape(seq_local, clips, width)
    targets = []
    grads = []
    for part in range(2):
        chosen = slice(part * half, (part + 1) * half)
        weights = pieces[:, :, :, chosen].reshape(2, pieces.shape[1], clips * half)
        partial_value = jnp.dot(student_term, weights[0], preferred_element_type=jnp.float32) + jnp.dot(
            teacher_term, weights[1], preferred_element_type=jnp.float32
        )
        pieces_in = lax.all_to_all(
            partial_value.astype(jnp.bfloat16).reshape(groups, seq_local, clips, half),
            "tensor",
            split_axis=0,
            concat_axis=0,
            tiled=True,
        )
        velocity = jnp.sum(pieces_in.astype(jnp.float32), axis=0)
        target_part = (
            velocity - latent_weight * latent_blocks[:, :, chosen].astype(jnp.float32)
        ).astype(jnp.bfloat16)
        targets.append(target_part)
        columns = lax.all_to_all(target_part, "dp", split_axis=1, concat_axis=1, tiled=True)
        columns = lax.all_gather(columns, "tensor", axis=0, tiled=True)
        terms = jnp.einsum(
            "csi,scd->cid", attended_all, columns, preferred_element_type=jnp.float32
        )
        grads.append(jnp.sum((grad_scale * terms).astype(jnp.bfloat16).astype(jnp.float32), axis=0))
    target = jnp.concatenate(targets, axis=2).reshape(seq_local, clips * width)
    gradient = jnp.concatenate(grads, axis=1)
    return (target[None], gradient)


def solution(mesh):
    placed = (
        P("dp"),
        P("dp"),
        P("dp", None, None),
        P("dp", "tensor", None),
        P(None, "dp", None, "tensor"),
        P(None, "dp", None, "tensor"),
        P(None, "dp", None, "tensor"),
        P("dp", "tensor", None),
        P("dp", "tensor", None),
        P("dp", "tensor", None),
        P("dp", "tensor", None),
        P("dp", "tensor", None),
        P("dp", "tensor", None),
        P("tensor", "dp"),
        P("tensor", "dp"),
    )
    return jax.shard_map(
        local,
        mesh=mesh,
        in_specs=placed,
        out_specs=(P("dp", "tensor", None), P("tensor", "dp")),
        check_vma=False,
    )
```

```python
import math

import jax
import jax.numpy as jnp
from jax import lax
from jax.experimental import pallas as pl
from jax.experimental.pallas import tpu as pltpu
from jax.sharding import PartitionSpec as P

HD = 128
STEPS = 1000


sigma_data = 0.5
guidance = 5.0


def rope_angles(coords):
    half_size = HD // 2
    sixth = HD // 6
    first_pairs = half_size - 2 * sixth
    pair_index = jnp.arange(half_size)
    axis_id = (pair_index >= first_pairs).astype(jnp.int32) + (
        pair_index >= first_pairs + sixth
    ).astype(jnp.int32)
    offset = jnp.where(axis_id == 0, 0, jnp.where(axis_id == 1, first_pairs, first_pairs + sixth))
    axis_width = jnp.where(axis_id == 0, 2 * first_pairs, 2 * sixth)
    exponent = 2.0 * (pair_index - offset).astype(jnp.float32) / axis_width.astype(jnp.float32)
    frequency = jnp.exp(-exponent * math.log(10000.0))
    angles = jnp.zeros((coords.shape[1], half_size), jnp.float32)
    for which_axis in range(3):
        chosen = jnp.where(axis_id == which_axis, frequency, 0.0)
        angles = angles + coords[which_axis].astype(jnp.float32)[:, None] * chosen[None, :]
    return angles


def rotate_heads(source, angles):
    half_size = source.shape[-1] // 2
    cos_angle = jnp.cos(angles)[:, None, :]
    sin_angle = jnp.sin(angles)[:, None, :]
    front_half = source[..., :half_size]
    back_half = source[..., half_size:]
    return jnp.concatenate(
        [
            front_half * cos_angle - back_half * sin_angle,
            back_half * cos_angle + front_half * sin_angle,
        ],
        axis=-1,
    )


def split_heads(source):
    return source.reshape(source.shape[0], -1, HD)


def rotated(source, angles):
    row_count = source.shape[0]
    return (
        rotate_heads(split_heads(source).astype(jnp.float32), angles)
        .astype(jnp.bfloat16)
        .reshape(row_count, -1)
    )


def softmax_rows(scores):
    row_peak = jnp.max(scores, axis=-1, keepdims=True)
    exponent = jnp.exp(scores - row_peak)
    return exponent / jnp.sum(exponent, axis=-1, keepdims=True)


def attend_plain(queries, key_rows, value_rows):
    scores = jnp.einsum(
        "qhd,khd->hqk", queries, key_rows, preferred_element_type=jnp.float32
    ) * HD ** (-0.5)
    rounded = softmax_rows(scores).astype(jnp.bfloat16)
    return jnp.einsum("hqk,khd->qhd", rounded, value_rows, preferred_element_type=jnp.float32)


def attend_tangent(queries, key_rows, value_rows, query_dir, key_dir, value_dir):
    score_scale = HD ** (-0.5)
    scores = (
        jnp.einsum("qhd,khd->hqk", queries, key_rows, preferred_element_type=jnp.float32)
        * score_scale
    )
    weights = softmax_rows(scores)
    rounded = weights.astype(jnp.bfloat16)
    primal = jnp.einsum("hqk,khd->qhd", rounded, value_rows, preferred_element_type=jnp.float32)
    score_dir = (
        jnp.einsum("qhd,khd->hqk", query_dir, key_rows, preferred_element_type=jnp.float32)
        + jnp.einsum("qhd,khd->hqk", queries, key_dir, preferred_element_type=jnp.float32)
    ) * score_scale
    weight_dir = weights * (score_dir - jnp.sum(weights * score_dir, axis=-1, keepdims=True))
    rounded_dir = weight_dir.astype(jnp.bfloat16)
    tangent = jnp.einsum(
        "hqk,khd->qhd", rounded_dir, value_rows, preferred_element_type=jnp.float32
    ) + jnp.einsum("hqk,khd->qhd", rounded, value_dir, preferred_element_type=jnp.float32)
    return (primal, tangent)


SCORE_SCALE = HD ** (-0.5)


def rope_tables(angles):
    cos_angle = jnp.cos(angles)
    sin_angle = jnp.sin(angles)
    return (
        jnp.concatenate([cos_angle, cos_angle], axis=-1),
        jnp.concatenate([-sin_angle, sin_angle], axis=-1),
    )


def rotate_block(block, cos_ref, sin_ref):
    source = block.astype(jnp.float32)
    swapped = pltpu.roll(source, HD // 2, 1)
    return (source * cos_ref[...] + swapped * sin_ref[...]).astype(jnp.bfloat16)


def scores_of(queries, key_rows):
    return (
        lax.dot_general(
            queries, key_rows, (((1,), (1,)), ((), ())), preferred_element_type=jnp.float32
        )
        * SCORE_SCALE
    )


def softmax_block(scores):
    exponent = jnp.exp(scores - jnp.max(scores, axis=-1, keepdims=True))
    return exponent / jnp.sum(exponent, axis=-1, keepdims=True)


def teacher_kernel(scal, cos_ref, sin_ref, q0, k0, v0, q1, k1, v1, out_ref):
    def attend(q_ref, k_ref, v_ref):
        weights = softmax_block(
            scores_of(rotate_block(q_ref[...], cos_ref, sin_ref), rotate_block(k_ref[...], cos_ref, sin_ref))
        )
        return jnp.dot(weights.astype(jnp.bfloat16), v_ref[...], preferred_element_type=jnp.float32)

    first = attend(q0, k0, v0)
    second = attend(q1, k1, v1)
    pick_first = scal[1] == 0.0
    cond_out = jnp.where(pick_first, first, second)
    uncond_out = jnp.where(pick_first, second, first)
    out_ref[...] = (scal[0] * (uncond_out + guidance * (cond_out - uncond_out))).astype(jnp.bfloat16)


def student_kernel(scal, cos_ref, sin_ref, q, k, v, qt, kt, vt, term_ref, att_ref):
    queries = rotate_block(q[...], cos_ref, sin_ref)
    key_rows = rotate_block(k[...], cos_ref, sin_ref)
    query_dir = rotate_block(qt[...], cos_ref, sin_ref)
    key_dir = rotate_block(kt[...], cos_ref, sin_ref)
    weights = softmax_block(scores_of(queries, key_rows))
    rounded = weights.astype(jnp.bfloat16)
    primal = jnp.dot(rounded, v[...], preferred_element_type=jnp.float32)
    score_dir = (
        lax.dot_general(query_dir, key_rows, (((1,), (1,)), ((), ())), preferred_element_type=jnp.float32)
        + lax.dot_general(queries, key_dir, (((1,), (1,)), ((), ())), preferred_element_type=jnp.float32)
    ) * SCORE_SCALE
    weight_dir = weights * (score_dir - jnp.sum(weights * score_dir, axis=-1, keepdims=True))
    tangent = jnp.dot(weight_dir.astype(jnp.bfloat16), v[...], preferred_element_type=jnp.float32) + jnp.dot(
        rounded, vt[...], preferred_element_type=jnp.float32
    )
    term_ref[...] = (scal[0] * primal - scal[1] * tangent).astype(jnp.bfloat16)
    att_ref[...] = primal.astype(jnp.bfloat16)


def head_call(kernel, scal, tables, operands, outputs):
    seq, cols = outputs[0].shape
    heads = cols // HD
    head_block = pl.BlockSpec((seq, HD), lambda h: (0, h))
    table_block = pl.BlockSpec((seq, HD), lambda h: (0, 0))
    in_specs = [pl.BlockSpec(memory_space=pltpu.SMEM), table_block, table_block]
    for operand in operands:
        if operand.ndim == 2:
            in_specs.append(head_block)
        else:
            in_specs.append(pl.BlockSpec((None, seq, HD), lambda h, s=operand.index: (s, 0, h)))
    return pl.pallas_call(
        kernel,
        grid=(heads,),
        in_specs=in_specs,
        out_specs=[head_block] * len(outputs),
        out_shape=outputs,
        compiler_params=pltpu.CompilerParams(dimension_semantics=("arbitrary",)),
    )(scal, *tables, *[o.array for o in operands])


class Operand:
    def __init__(self, array, index=None):
        self.array = array
        self.index = index
        self.ndim = 2 if index is None else 3


def local(
    t_index,
    cond_slot,
    positions,
    latent,
    teacher_query,
    teacher_key,
    teacher_value,
    student_query,
    student_key,
    student_value,
    query_tangent,
    key_tangent,
    value_tangent,
    teacher_out,
    student_out,
):
    groups = lax.axis_size("tensor")
    seq_local = latent.shape[1]
    seq_whole = seq_local * groups
    row_start = lax.axis_index("tensor") * seq_local
    time_value = 0.2 + 1.2 * (t_index[0].astype(jnp.float32) + 0.5) / STEPS
    cos_time = jnp.cos(time_value)
    sin_time = jnp.sin(time_value)
    angles_whole = rope_angles(positions[0])
    tables = rope_tables(angles_whole)
    arrived = [
        lax.all_to_all(source[0], "tensor", split_axis=1, concat_axis=0, tiled=True)
        for source in (student_query, student_key, student_value, query_tangent, key_tangent, value_tangent)
    ]
    cols = arrived[0].shape[1]
    teacher_scal = jnp.stack(
        [cos_time * cos_time * sigma_data, cond_slot[0].astype(jnp.float32)]
    )
    t_q = teacher_query.reshape((2,) + teacher_query.shape[2:])
    t_k = teacher_key.reshape((2,) + teacher_key.shape[2:])
    t_v = teacher_value.reshape((2,) + teacher_value.shape[2:])
    (teacher_term,) = head_call(
        teacher_kernel,
        teacher_scal,
        tables,
        [Operand(t_q, 0), Operand(t_k, 0), Operand(t_v, 0), Operand(t_q, 1), Operand(t_k, 1), Operand(t_v, 1)],
        [jax.ShapeDtypeStruct((seq_whole, cols), jnp.bfloat16)],
    )
    student_scal = jnp.stack(
        [-(cos_time * cos_time) * sigma_data, cos_time * sin_time * sigma_data]
    )
    student_term, attended = head_call(
        student_kernel,
        student_scal,
        tables,
        [Operand(a) for a in arrived],
        [jax.ShapeDtypeStruct((seq_whole, cols), jnp.bfloat16)] * 2,
    )
    stacked = jnp.stack([student_out, teacher_out])
    pieces = lax.all_gather(stacked, "dp", axis=2, tiled=True)
    latent_weight = cos_time * sin_time
    span = pieces.shape[2] // 2
    target_parts = []
    for part in range(2):
        chosen = slice(part * span, (part + 1) * span)
        partial_value = jnp.dot(
            student_term, pieces[0, :, chosen], preferred_element_type=jnp.float32
        ) + jnp.dot(teacher_term, pieces[1, :, chosen], preferred_element_type=jnp.float32)
        pieces_in = lax.all_to_all(
            partial_value.astype(jnp.bfloat16).reshape(groups, seq_local, -1),
            "tensor",
            split_axis=0,
            concat_axis=0,
            tiled=True,
        )
        velocity = jnp.sum(pieces_in.astype(jnp.float32), axis=0)
        target_parts.append(
            (velocity - latent_weight * latent[0, :, chosen].astype(jnp.float32)).astype(jnp.bfloat16)
        )
    target = jnp.concatenate(target_parts, axis=1)
    clips = lax.axis_size("dp")
    width = target.shape[1] // clips
    attended_all = lax.all_gather(attended, "dp", axis=0, tiled=False)
    grad_scale = -2.0 / math.sqrt(clips * seq_whole)
    half = width // 2
    split_target = target.reshape(seq_local, clips, width)
    pieces = []
    for part in range(2):
        columns = lax.all_to_all(
            split_target[:, :, part * half : (part + 1) * half], "dp", split_axis=1, concat_axis=1, tiled=True
        )
        columns = lax.all_gather(columns, "tensor", axis=0, tiled=True)
        terms = jnp.einsum(
            "csi,scd->cid", attended_all, columns, preferred_element_type=jnp.float32
        )
        pieces.append(jnp.sum((grad_scale * terms).astype(jnp.bfloat16).astype(jnp.float32), axis=0))
    gradient = jnp.concatenate(pieces, axis=1)
    return (target[None], gradient)


def solution(mesh):
    placed = (
        P("dp"),
        P("dp"),
        P("dp", None, None),
        P("dp", "tensor", None),
        P(None, "dp", None, "tensor"),
        P(None, "dp", None, "tensor"),
        P(None, "dp", None, "tensor"),
        P("dp", "tensor", None),
        P("dp", "tensor", None),
        P("dp", "tensor", None),
        P("dp", "tensor", None),
        P("dp", "tensor", None),
        P("dp", "tensor", None),
        P("tensor", "dp"),
        P("tensor", "dp"),
    )
    return jax.shard_map(
        local,
        mesh=mesh,
        in_specs=placed,
        out_specs=(P("dp", "tensor", None), P("tensor", "dp")),
        check_vma=False,
    )
```

```python
import math

import jax
import jax.numpy as jnp
from jax import lax
from jax.experimental import pallas as pl
from jax.experimental.pallas import tpu as pltpu
from jax.sharding import PartitionSpec as P

HD = 128
STEPS = 1000


sigma_data = 0.5
guidance = 5.0


def rope_angles(coords):
    half_size = HD // 2
    sixth = HD // 6
    first_pairs = half_size - 2 * sixth
    pair_index = jnp.arange(half_size)
    axis_id = (pair_index >= first_pairs).astype(jnp.int32) + (
        pair_index >= first_pairs + sixth
    ).astype(jnp.int32)
    offset = jnp.where(axis_id == 0, 0, jnp.where(axis_id == 1, first_pairs, first_pairs + sixth))
    axis_width = jnp.where(axis_id == 0, 2 * first_pairs, 2 * sixth)
    exponent = 2.0 * (pair_index - offset).astype(jnp.float32) / axis_width.astype(jnp.float32)
    frequency = jnp.exp(-exponent * math.log(10000.0))
    angles = jnp.zeros((coords.shape[1], half_size), jnp.float32)
    for which_axis in range(3):
        chosen = jnp.where(axis_id == which_axis, frequency, 0.0)
        angles = angles + coords[which_axis].astype(jnp.float32)[:, None] * chosen[None, :]
    return angles


def rotate_heads(source, angles):
    half_size = source.shape[-1] // 2
    cos_angle = jnp.cos(angles)[:, None, :]
    sin_angle = jnp.sin(angles)[:, None, :]
    front_half = source[..., :half_size]
    back_half = source[..., half_size:]
    return jnp.concatenate(
        [
            front_half * cos_angle - back_half * sin_angle,
            back_half * cos_angle + front_half * sin_angle,
        ],
        axis=-1,
    )


def split_heads(source):
    return source.reshape(source.shape[0], -1, HD)


def rotated(source, angles):
    row_count = source.shape[0]
    return (
        rotate_heads(split_heads(source).astype(jnp.float32), angles)
        .astype(jnp.bfloat16)
        .reshape(row_count, -1)
    )


def softmax_rows(scores):
    row_peak = jnp.max(scores, axis=-1, keepdims=True)
    exponent = jnp.exp(scores - row_peak)
    return exponent / jnp.sum(exponent, axis=-1, keepdims=True)


def attend_plain(queries, key_rows, value_rows):
    scores = jnp.einsum(
        "qhd,khd->hqk", queries, key_rows, preferred_element_type=jnp.float32
    ) * HD ** (-0.5)
    rounded = softmax_rows(scores).astype(jnp.bfloat16)
    return jnp.einsum("hqk,khd->qhd", rounded, value_rows, preferred_element_type=jnp.float32)


def attend_tangent(queries, key_rows, value_rows, query_dir, key_dir, value_dir):
    score_scale = HD ** (-0.5)
    scores = (
        jnp.einsum("qhd,khd->hqk", queries, key_rows, preferred_element_type=jnp.float32)
        * score_scale
    )
    weights = softmax_rows(scores)
    rounded = weights.astype(jnp.bfloat16)
    primal = jnp.einsum("hqk,khd->qhd", rounded, value_rows, preferred_element_type=jnp.float32)
    score_dir = (
        jnp.einsum("qhd,khd->hqk", query_dir, key_rows, preferred_element_type=jnp.float32)
        + jnp.einsum("qhd,khd->hqk", queries, key_dir, preferred_element_type=jnp.float32)
    ) * score_scale
    weight_dir = weights * (score_dir - jnp.sum(weights * score_dir, axis=-1, keepdims=True))
    rounded_dir = weight_dir.astype(jnp.bfloat16)
    tangent = jnp.einsum(
        "hqk,khd->qhd", rounded_dir, value_rows, preferred_element_type=jnp.float32
    ) + jnp.einsum("hqk,khd->qhd", rounded, value_dir, preferred_element_type=jnp.float32)
    return (primal, tangent)


SCORE_SCALE = HD ** (-0.5)


def rope_tables(angles):
    cos_angle = jnp.cos(angles)
    sin_angle = jnp.sin(angles)
    return (
        jnp.concatenate([cos_angle, cos_angle], axis=-1),
        jnp.concatenate([-sin_angle, sin_angle], axis=-1),
    )


def rotate_block(block, cos_ref, sin_ref):
    source = block.astype(jnp.float32)
    swapped = pltpu.roll(source, HD // 2, 1)
    return (source * cos_ref[...] + swapped * sin_ref[...]).astype(jnp.bfloat16)


def scores_of(queries, key_rows):
    return (
        lax.dot_general(
            queries, key_rows, (((1,), (1,)), ((), ())), preferred_element_type=jnp.float32
        )
        * SCORE_SCALE
    )


def softmax_block(scores):
    exponent = jnp.exp(scores - jnp.max(scores, axis=-1, keepdims=True))
    return exponent / jnp.sum(exponent, axis=-1, keepdims=True)


def teacher_kernel(scal, cos_ref, sin_ref, q0, k0, v0, q1, k1, v1, out_ref):
    def attend(q_ref, k_ref, v_ref):
        weights = softmax_block(
            scores_of(rotate_block(q_ref[...], cos_ref, sin_ref), rotate_block(k_ref[...], cos_ref, sin_ref))
        )
        return jnp.dot(weights.astype(jnp.bfloat16), v_ref[...], preferred_element_type=jnp.float32)

    first = attend(q0, k0, v0)
    second = attend(q1, k1, v1)
    pick_first = scal[1] == 0.0
    cond_out = jnp.where(pick_first, first, second)
    uncond_out = jnp.where(pick_first, second, first)
    out_ref[...] = (scal[0] * (uncond_out + guidance * (cond_out - uncond_out))).astype(jnp.bfloat16)


def student_kernel(scal, cos_ref, sin_ref, q, k, v, qt, kt, vt, term_ref, att_ref):
    queries = rotate_block(q[...], cos_ref, sin_ref)
    key_rows = rotate_block(k[...], cos_ref, sin_ref)
    query_dir = rotate_block(qt[...], cos_ref, sin_ref)
    key_dir = rotate_block(kt[...], cos_ref, sin_ref)
    weights = softmax_block(scores_of(queries, key_rows))
    rounded = weights.astype(jnp.bfloat16)
    primal = jnp.dot(rounded, v[...], preferred_element_type=jnp.float32)
    score_dir = (
        lax.dot_general(query_dir, key_rows, (((1,), (1,)), ((), ())), preferred_element_type=jnp.float32)
        + lax.dot_general(queries, key_dir, (((1,), (1,)), ((), ())), preferred_element_type=jnp.float32)
    ) * SCORE_SCALE
    weight_dir = weights * (score_dir - jnp.sum(weights * score_dir, axis=-1, keepdims=True))
    tangent = jnp.dot(weight_dir.astype(jnp.bfloat16), v[...], preferred_element_type=jnp.float32) + jnp.dot(
        rounded, vt[...], preferred_element_type=jnp.float32
    )
    term_ref[...] = (scal[0] * primal - scal[1] * tangent).astype(jnp.bfloat16)
    att_ref[...] = primal.astype(jnp.bfloat16)


def head_call(kernel, scal, tables, operands, outputs):
    seq, cols = outputs[0].shape
    heads = cols // HD
    head_block = pl.BlockSpec((seq, HD), lambda h: (0, h))
    table_block = pl.BlockSpec((seq, HD), lambda h: (0, 0))
    in_specs = [pl.BlockSpec(memory_space=pltpu.SMEM), table_block, table_block]
    for operand in operands:
        if operand.ndim == 2:
            in_specs.append(head_block)
        else:
            in_specs.append(pl.BlockSpec((None, seq, HD), lambda h, s=operand.index: (s, 0, h)))
    return pl.pallas_call(
        kernel,
        grid=(heads,),
        in_specs=in_specs,
        out_specs=[head_block] * len(outputs),
        out_shape=outputs,
        compiler_params=pltpu.CompilerParams(dimension_semantics=("arbitrary",)),
    )(scal, *tables, *[o.array for o in operands])


class Operand:
    def __init__(self, array, index=None):
        self.array = array
        self.index = index
        self.ndim = 2 if index is None else 3


def local(
    t_index,
    cond_slot,
    positions,
    latent,
    teacher_query,
    teacher_key,
    teacher_value,
    student_query,
    student_key,
    student_value,
    query_tangent,
    key_tangent,
    value_tangent,
    teacher_out,
    student_out,
):
    groups = lax.axis_size("tensor")
    seq_local = latent.shape[1]
    seq_whole = seq_local * groups
    row_start = lax.axis_index("tensor") * seq_local
    time_value = 0.2 + 1.2 * (t_index[0].astype(jnp.float32) + 0.5) / STEPS
    cos_time = jnp.cos(time_value)
    sin_time = jnp.sin(time_value)
    angles_whole = rope_angles(positions[0])
    tables = rope_tables(angles_whole)
    arrived = [
        lax.all_to_all(source[0], "tensor", split_axis=1, concat_axis=0, tiled=True)
        for source in (student_query, student_key, student_value, query_tangent, key_tangent, value_tangent)
    ]
    cols = arrived[0].shape[1]
    teacher_scal = jnp.stack(
        [cos_time * cos_time * sigma_data, cond_slot[0].astype(jnp.float32)]
    )
    t_q = teacher_query.reshape((2,) + teacher_query.shape[2:])
    t_k = teacher_key.reshape((2,) + teacher_key.shape[2:])
    t_v = teacher_value.reshape((2,) + teacher_value.shape[2:])
    (teacher_term,) = head_call(
        teacher_kernel,
        teacher_scal,
        tables,
        [Operand(t_q, 0), Operand(t_k, 0), Operand(t_v, 0), Operand(t_q, 1), Operand(t_k, 1), Operand(t_v, 1)],
        [jax.ShapeDtypeStruct((seq_whole, cols), jnp.bfloat16)],
    )
    student_scal = jnp.stack(
        [-(cos_time * cos_time) * sigma_data, cos_time * sin_time * sigma_data]
    )
    student_term, attended = head_call(
        student_kernel,
        student_scal,
        tables,
        [Operand(a) for a in arrived],
        [jax.ShapeDtypeStruct((seq_whole, cols), jnp.bfloat16)] * 2,
    )
    stacked = jnp.stack([student_out, teacher_out])
    pieces = lax.all_gather(stacked, "dp", axis=2, tiled=True)
    latent_weight = cos_time * sin_time
    span = pieces.shape[2] // 2
    target_parts = []
    for part in range(2):
        chosen = slice(part * span, (part + 1) * span)
        partial_value = jnp.dot(
            student_term, pieces[0, :, chosen], preferred_element_type=jnp.float32
        ) + jnp.dot(teacher_term, pieces[1, :, chosen], preferred_element_type=jnp.float32)
        pieces_in = lax.all_to_all(
            partial_value.astype(jnp.bfloat16).reshape(groups, seq_local, -1),
            "tensor",
            split_axis=0,
            concat_axis=0,
            tiled=True,
        )
        velocity = jnp.sum(pieces_in.astype(jnp.float32), axis=0)
        target_parts.append(
            (velocity - latent_weight * latent[0, :, chosen].astype(jnp.float32)).astype(jnp.bfloat16)
        )
    target = jnp.concatenate(target_parts, axis=1)
    clips = lax.axis_size("dp")
    width = target.shape[1] // clips
    attended_all = lax.all_gather(attended, "dp", axis=0, tiled=False)
    grad_scale = -2.0 / math.sqrt(clips * seq_whole)
    half = width // 2
    split_target = target.reshape(seq_local, clips, width)
    pieces = []
    for part in range(2):
        columns = lax.all_to_all(
            split_target[:, :, part * half : (part + 1) * half], "dp", split_axis=1, concat_axis=1, tiled=True
        )
        if part == 0:
            columns = lax.all_gather(columns, "tensor", axis=0, tiled=True)
        else:
            copies = jnp.broadcast_to(columns[None], (groups,) + columns.shape)
            columns = lax.all_to_all(copies, "tensor", split_axis=0, concat_axis=0, tiled=True)
            columns = columns.reshape((groups * seq_local,) + columns.shape[2:])
        terms = jnp.einsum(
            "csi,scd->cid", attended_all, columns, preferred_element_type=jnp.float32
        )
        pieces.append(jnp.sum((grad_scale * terms).astype(jnp.bfloat16).astype(jnp.float32), axis=0))
    gradient = jnp.concatenate(pieces, axis=1)
    return (target[None], gradient)


def solution(mesh):
    placed = (
        P("dp"),
        P("dp"),
        P("dp", None, None),
        P("dp", "tensor", None),
        P(None, "dp", None, "tensor"),
        P(None, "dp", None, "tensor"),
        P(None, "dp", None, "tensor"),
        P("dp", "tensor", None),
        P("dp", "tensor", None),
        P("dp", "tensor", None),
        P("dp", "tensor", None),
        P("dp", "tensor", None),
        P("dp", "tensor", None),
        P("tensor", "dp"),
        P("tensor", "dp"),
    )
    return jax.shard_map(
        local,
        mesh=mesh,
        in_specs=placed,
        out_specs=(P("dp", "tensor", None), P("tensor", "dp")),
        check_vma=False,
    )
```

```python
import math

import jax
import jax.numpy as jnp
from jax import lax
from jax.experimental import pallas as pl
from jax.experimental.pallas import tpu as pltpu
from jax.sharding import PartitionSpec as P

HD = 128
STEPS = 1000


sigma_data = 0.5
guidance = 5.0


def rope_angles(coords):
    half_size = HD // 2
    sixth = HD // 6
    first_pairs = half_size - 2 * sixth
    pair_index = jnp.arange(half_size)
    axis_id = (pair_index >= first_pairs).astype(jnp.int32) + (
        pair_index >= first_pairs + sixth
    ).astype(jnp.int32)
    offset = jnp.where(axis_id == 0, 0, jnp.where(axis_id == 1, first_pairs, first_pairs + sixth))
    axis_width = jnp.where(axis_id == 0, 2 * first_pairs, 2 * sixth)
    exponent = 2.0 * (pair_index - offset).astype(jnp.float32) / axis_width.astype(jnp.float32)
    frequency = jnp.exp(-exponent * math.log(10000.0))
    angles = jnp.zeros((coords.shape[1], half_size), jnp.float32)
    for which_axis in range(3):
        chosen = jnp.where(axis_id == which_axis, frequency, 0.0)
        angles = angles + coords[which_axis].astype(jnp.float32)[:, None] * chosen[None, :]
    return angles


def rotate_heads(source, angles):
    half_size = source.shape[-1] // 2
    cos_angle = jnp.cos(angles)[:, None, :]
    sin_angle = jnp.sin(angles)[:, None, :]
    front_half = source[..., :half_size]
    back_half = source[..., half_size:]
    return jnp.concatenate(
        [
            front_half * cos_angle - back_half * sin_angle,
            back_half * cos_angle + front_half * sin_angle,
        ],
        axis=-1,
    )


def split_heads(source):
    return source.reshape(source.shape[0], -1, HD)


def rotated(source, angles):
    row_count = source.shape[0]
    return (
        rotate_heads(split_heads(source).astype(jnp.float32), angles)
        .astype(jnp.bfloat16)
        .reshape(row_count, -1)
    )


def softmax_rows(scores):
    row_peak = jnp.max(scores, axis=-1, keepdims=True)
    exponent = jnp.exp(scores - row_peak)
    return exponent / jnp.sum(exponent, axis=-1, keepdims=True)


def attend_plain(queries, key_rows, value_rows):
    scores = jnp.einsum(
        "qhd,khd->hqk", queries, key_rows, preferred_element_type=jnp.float32
    ) * HD ** (-0.5)
    rounded = softmax_rows(scores).astype(jnp.bfloat16)
    return jnp.einsum("hqk,khd->qhd", rounded, value_rows, preferred_element_type=jnp.float32)


def attend_tangent(queries, key_rows, value_rows, query_dir, key_dir, value_dir):
    score_scale = HD ** (-0.5)
    scores = (
        jnp.einsum("qhd,khd->hqk", queries, key_rows, preferred_element_type=jnp.float32)
        * score_scale
    )
    weights = softmax_rows(scores)
    rounded = weights.astype(jnp.bfloat16)
    primal = jnp.einsum("hqk,khd->qhd", rounded, value_rows, preferred_element_type=jnp.float32)
    score_dir = (
        jnp.einsum("qhd,khd->hqk", query_dir, key_rows, preferred_element_type=jnp.float32)
        + jnp.einsum("qhd,khd->hqk", queries, key_dir, preferred_element_type=jnp.float32)
    ) * score_scale
    weight_dir = weights * (score_dir - jnp.sum(weights * score_dir, axis=-1, keepdims=True))
    rounded_dir = weight_dir.astype(jnp.bfloat16)
    tangent = jnp.einsum(
        "hqk,khd->qhd", rounded_dir, value_rows, preferred_element_type=jnp.float32
    ) + jnp.einsum("hqk,khd->qhd", rounded, value_dir, preferred_element_type=jnp.float32)
    return (primal, tangent)


SCORE_SCALE = HD ** (-0.5)


def rope_tables(angles):
    cos_angle = jnp.cos(angles)
    sin_angle = jnp.sin(angles)
    return (
        jnp.concatenate([cos_angle, cos_angle], axis=-1),
        jnp.concatenate([-sin_angle, sin_angle], axis=-1),
    )


def rotate_block(block, cos_ref, sin_ref):
    source = block.astype(jnp.float32)
    swapped = pltpu.roll(source, HD // 2, 1)
    return (source * cos_ref[...] + swapped * sin_ref[...]).astype(jnp.bfloat16)


def scores_of(queries, key_rows):
    return (
        lax.dot_general(
            queries, key_rows, (((1,), (1,)), ((), ())), preferred_element_type=jnp.float32
        )
        * SCORE_SCALE
    )


def softmax_block(scores):
    exponent = jnp.exp(scores - jnp.max(scores, axis=-1, keepdims=True))
    return exponent / jnp.sum(exponent, axis=-1, keepdims=True)


def teacher_kernel(scal, cos_ref, sin_ref, q0, k0, v0, q1, k1, v1, out_ref):
    def attend(q_ref, k_ref, v_ref):
        weights = softmax_block(
            scores_of(rotate_block(q_ref[...], cos_ref, sin_ref), rotate_block(k_ref[...], cos_ref, sin_ref))
        )
        return jnp.dot(weights.astype(jnp.bfloat16), v_ref[...], preferred_element_type=jnp.float32)

    first = attend(q0, k0, v0)
    second = attend(q1, k1, v1)
    pick_first = scal[1] == 0.0
    cond_out = jnp.where(pick_first, first, second)
    uncond_out = jnp.where(pick_first, second, first)
    out_ref[...] = (scal[0] * (uncond_out + guidance * (cond_out - uncond_out))).astype(jnp.bfloat16)


def student_kernel(scal, cos_ref, sin_ref, q, k, v, qt, kt, vt, term_ref, att_ref):
    queries = rotate_block(q[...], cos_ref, sin_ref)
    key_rows = rotate_block(k[...], cos_ref, sin_ref)
    query_dir = rotate_block(qt[...], cos_ref, sin_ref)
    key_dir = rotate_block(kt[...], cos_ref, sin_ref)
    weights = softmax_block(scores_of(queries, key_rows))
    rounded = weights.astype(jnp.bfloat16)
    primal = jnp.dot(rounded, v[...], preferred_element_type=jnp.float32)
    score_dir = (
        lax.dot_general(query_dir, key_rows, (((1,), (1,)), ((), ())), preferred_element_type=jnp.float32)
        + lax.dot_general(queries, key_dir, (((1,), (1,)), ((), ())), preferred_element_type=jnp.float32)
    ) * SCORE_SCALE
    weight_dir = weights * (score_dir - jnp.sum(weights * score_dir, axis=-1, keepdims=True))
    tangent = jnp.dot(weight_dir.astype(jnp.bfloat16), v[...], preferred_element_type=jnp.float32) + jnp.dot(
        rounded, vt[...], preferred_element_type=jnp.float32
    )
    term_ref[...] = (scal[0] * primal - scal[1] * tangent).astype(jnp.bfloat16)
    att_ref[...] = primal.astype(jnp.bfloat16)


def head_call(kernel, scal, tables, operands, outputs):
    seq, cols = outputs[0].shape
    heads = cols // HD
    head_block = pl.BlockSpec((seq, HD), lambda h: (0, h))
    table_block = pl.BlockSpec((seq, HD), lambda h: (0, 0))
    in_specs = [pl.BlockSpec(memory_space=pltpu.SMEM), table_block, table_block]
    for operand in operands:
        if operand.ndim == 2:
            in_specs.append(head_block)
        else:
            in_specs.append(pl.BlockSpec((None, seq, HD), lambda h, s=operand.index: (s, 0, h)))
    return pl.pallas_call(
        kernel,
        grid=(heads,),
        in_specs=in_specs,
        out_specs=[head_block] * len(outputs),
        out_shape=outputs,
        compiler_params=pltpu.CompilerParams(dimension_semantics=("arbitrary",)),
    )(scal, *tables, *[o.array for o in operands])


class Operand:
    def __init__(self, array, index=None):
        self.array = array
        self.index = index
        self.ndim = 2 if index is None else 3


def local(
    t_index,
    cond_slot,
    positions,
    latent,
    teacher_query,
    teacher_key,
    teacher_value,
    student_query,
    student_key,
    student_value,
    query_tangent,
    key_tangent,
    value_tangent,
    teacher_out,
    student_out,
):
    groups = lax.axis_size("tensor")
    seq_local = latent.shape[1]
    seq_whole = seq_local * groups
    row_start = lax.axis_index("tensor") * seq_local
    time_value = 0.2 + 1.2 * (t_index[0].astype(jnp.float32) + 0.5) / STEPS
    cos_time = jnp.cos(time_value)
    sin_time = jnp.sin(time_value)
    angles_whole = rope_angles(positions[0])
    tables = rope_tables(angles_whole)
    arrived = [
        lax.all_to_all(source[0], "tensor", split_axis=1, concat_axis=0, tiled=True)
        for source in (student_query, student_key, student_value, query_tangent, key_tangent, value_tangent)
    ]
    cols = arrived[0].shape[1]
    teacher_scal = jnp.stack(
        [cos_time * cos_time * sigma_data, cond_slot[0].astype(jnp.float32)]
    )
    t_q = teacher_query.reshape((2,) + teacher_query.shape[2:])
    t_k = teacher_key.reshape((2,) + teacher_key.shape[2:])
    t_v = teacher_value.reshape((2,) + teacher_value.shape[2:])
    (teacher_term,) = head_call(
        teacher_kernel,
        teacher_scal,
        tables,
        [Operand(t_q, 0), Operand(t_k, 0), Operand(t_v, 0), Operand(t_q, 1), Operand(t_k, 1), Operand(t_v, 1)],
        [jax.ShapeDtypeStruct((seq_whole, cols), jnp.bfloat16)],
    )
    student_scal = jnp.stack(
        [-(cos_time * cos_time) * sigma_data, cos_time * sin_time * sigma_data]
    )
    student_term, attended = head_call(
        student_kernel,
        student_scal,
        tables,
        [Operand(a) for a in arrived],
        [jax.ShapeDtypeStruct((seq_whole, cols), jnp.bfloat16)] * 2,
    )
    clips = lax.axis_size("dp")
    rows, width = student_out.shape
    half = width // 2
    local = jnp.transpose(
        jnp.stack([student_out, teacher_out]).reshape(2, rows, 2, half), (0, 2, 1, 3)
    )
    pieces = lax.all_gather(local, "dp", axis=3, tiled=False)
    latent_weight = cos_time * sin_time
    attended_all = lax.all_gather(attended, "dp", axis=0, tiled=False)
    grad_scale = -2.0 / math.sqrt(clips * seq_whole)
    latent_blocks = latent[0].reshape(seq_local, clips, width)
    targets = []
    grads = []
    gate = None
    for part in range(2):
        partial_value = (
            jnp.einsum("si,ijd->sjd", student_term, pieces[0, part], preferred_element_type=jnp.float32)
            + jnp.einsum("si,ijd->sjd", teacher_term, pieces[1, part], preferred_element_type=jnp.float32)
        ).astype(jnp.bfloat16)
        if gate is not None:
            partial_value, columns = lax.optimization_barrier((partial_value, gate))
            columns = lax.all_gather(columns, "tensor", axis=0, tiled=True)
            terms = jnp.einsum(
                "csi,scd->cid", attended_all, columns, preferred_element_type=jnp.float32
            )
            grads.append(jnp.sum((grad_scale * terms).astype(jnp.bfloat16).astype(jnp.float32), axis=0))
        pieces_in = lax.all_to_all(
            partial_value.reshape(groups, seq_local, clips, half),
            "tensor",
            split_axis=0,
            concat_axis=0,
            tiled=True,
        )
        velocity = jnp.sum(pieces_in.astype(jnp.float32), axis=0)
        target_part = (
            velocity - latent_weight * latent_blocks[:, :, part * half : (part + 1) * half].astype(jnp.float32)
        ).astype(jnp.bfloat16)
        targets.append(target_part)
        gate = lax.all_to_all(target_part, "dp", split_axis=1, concat_axis=1, tiled=True)
    columns = lax.all_gather(gate, "tensor", axis=0, tiled=True)
    terms = jnp.einsum(
        "csi,scd->cid", attended_all, columns, preferred_element_type=jnp.float32
    )
    grads.append(jnp.sum((grad_scale * terms).astype(jnp.bfloat16).astype(jnp.float32), axis=0))
    target = jnp.concatenate(targets, axis=2).reshape(seq_local, clips * width)
    gradient = jnp.concatenate(grads, axis=1)
    return (target[None], gradient)


def solution(mesh):
    placed = (
        P("dp"),
        P("dp"),
        P("dp", None, None),
        P("dp", "tensor", None),
        P(None, "dp", None, "tensor"),
        P(None, "dp", None, "tensor"),
        P(None, "dp", None, "tensor"),
        P("dp", "tensor", None),
        P("dp", "tensor", None),
        P("dp", "tensor", None),
        P("dp", "tensor", None),
        P("dp", "tensor", None),
        P("dp", "tensor", None),
        P("tensor", "dp"),
        P("tensor", "dp"),
    )
    return jax.shard_map(
        local,
        mesh=mesh,
        in_specs=placed,
        out_specs=(P("dp", "tensor", None), P("tensor", "dp")),
        check_vma=False,
    )
```

```python
import math

import jax
import jax.numpy as jnp
from jax import lax
from jax.experimental import pallas as pl
from jax.experimental.pallas import tpu as pltpu
from jax.sharding import PartitionSpec as P

HD = 128
STEPS = 1000


sigma_data = 0.5
guidance = 5.0


def rope_angles(coords):
    half_size = HD // 2
    sixth = HD // 6
    first_pairs = half_size - 2 * sixth
    pair_index = jnp.arange(half_size)
    axis_id = (pair_index >= first_pairs).astype(jnp.int32) + (
        pair_index >= first_pairs + sixth
    ).astype(jnp.int32)
    offset = jnp.where(axis_id == 0, 0, jnp.where(axis_id == 1, first_pairs, first_pairs + sixth))
    axis_width = jnp.where(axis_id == 0, 2 * first_pairs, 2 * sixth)
    exponent = 2.0 * (pair_index - offset).astype(jnp.float32) / axis_width.astype(jnp.float32)
    frequency = jnp.exp(-exponent * math.log(10000.0))
    angles = jnp.zeros((coords.shape[1], half_size), jnp.float32)
    for which_axis in range(3):
        chosen = jnp.where(axis_id == which_axis, frequency, 0.0)
        angles = angles + coords[which_axis].astype(jnp.float32)[:, None] * chosen[None, :]
    return angles


def rotate_heads(source, angles):
    half_size = source.shape[-1] // 2
    cos_angle = jnp.cos(angles)[:, None, :]
    sin_angle = jnp.sin(angles)[:, None, :]
    front_half = source[..., :half_size]
    back_half = source[..., half_size:]
    return jnp.concatenate(
        [
            front_half * cos_angle - back_half * sin_angle,
            back_half * cos_angle + front_half * sin_angle,
        ],
        axis=-1,
    )


def split_heads(source):
    return source.reshape(source.shape[0], -1, HD)


def rotated(source, angles):
    row_count = source.shape[0]
    return (
        rotate_heads(split_heads(source).astype(jnp.float32), angles)
        .astype(jnp.bfloat16)
        .reshape(row_count, -1)
    )


def softmax_rows(scores):
    row_peak = jnp.max(scores, axis=-1, keepdims=True)
    exponent = jnp.exp(scores - row_peak)
    return exponent / jnp.sum(exponent, axis=-1, keepdims=True)


def attend_plain(queries, key_rows, value_rows):
    scores = jnp.einsum(
        "qhd,khd->hqk", queries, key_rows, preferred_element_type=jnp.float32
    ) * HD ** (-0.5)
    rounded = softmax_rows(scores).astype(jnp.bfloat16)
    return jnp.einsum("hqk,khd->qhd", rounded, value_rows, preferred_element_type=jnp.float32)


def attend_tangent(queries, key_rows, value_rows, query_dir, key_dir, value_dir):
    score_scale = HD ** (-0.5)
    scores = (
        jnp.einsum("qhd,khd->hqk", queries, key_rows, preferred_element_type=jnp.float32)
        * score_scale
    )
    weights = softmax_rows(scores)
    rounded = weights.astype(jnp.bfloat16)
    primal = jnp.einsum("hqk,khd->qhd", rounded, value_rows, preferred_element_type=jnp.float32)
    score_dir = (
        jnp.einsum("qhd,khd->hqk", query_dir, key_rows, preferred_element_type=jnp.float32)
        + jnp.einsum("qhd,khd->hqk", queries, key_dir, preferred_element_type=jnp.float32)
    ) * score_scale
    weight_dir = weights * (score_dir - jnp.sum(weights * score_dir, axis=-1, keepdims=True))
    rounded_dir = weight_dir.astype(jnp.bfloat16)
    tangent = jnp.einsum(
        "hqk,khd->qhd", rounded_dir, value_rows, preferred_element_type=jnp.float32
    ) + jnp.einsum("hqk,khd->qhd", rounded, value_dir, preferred_element_type=jnp.float32)
    return (primal, tangent)


SCORE_SCALE = HD ** (-0.5)


def rope_tables(angles):
    cos_angle = jnp.cos(angles)
    sin_angle = jnp.sin(angles)
    return (
        jnp.concatenate([cos_angle, cos_angle], axis=-1),
        jnp.concatenate([-sin_angle, sin_angle], axis=-1),
    )


def rotate_block(block, cos_ref, sin_ref):
    source = block.astype(jnp.float32)
    swapped = pltpu.roll(source, HD // 2, 1)
    return (source * cos_ref[...] + swapped * sin_ref[...]).astype(jnp.bfloat16)


def scores_of(queries, key_rows):
    return (
        lax.dot_general(
            queries, key_rows, (((1,), (1,)), ((), ())), preferred_element_type=jnp.float32
        )
        * SCORE_SCALE
    )


def softmax_block(scores):
    exponent = jnp.exp(scores - jnp.max(scores, axis=-1, keepdims=True))
    return exponent / jnp.sum(exponent, axis=-1, keepdims=True)


def teacher_kernel(scal, cos_ref, sin_ref, q0, k0, v0, q1, k1, v1, out_ref):
    def attend(q_ref, k_ref, v_ref):
        weights = softmax_block(
            scores_of(rotate_block(q_ref[...], cos_ref, sin_ref), rotate_block(k_ref[...], cos_ref, sin_ref))
        )
        return jnp.dot(weights.astype(jnp.bfloat16), v_ref[...], preferred_element_type=jnp.float32)

    first = attend(q0, k0, v0)
    second = attend(q1, k1, v1)
    pick_first = scal[1] == 0.0
    cond_out = jnp.where(pick_first, first, second)
    uncond_out = jnp.where(pick_first, second, first)
    out_ref[...] = (scal[0] * (uncond_out + guidance * (cond_out - uncond_out))).astype(jnp.bfloat16)


def student_kernel(scal, cos_ref, sin_ref, q, k, v, qt, kt, vt, term_ref, att_ref):
    queries = rotate_block(q[...], cos_ref, sin_ref)
    key_rows = rotate_block(k[...], cos_ref, sin_ref)
    query_dir = rotate_block(qt[...], cos_ref, sin_ref)
    key_dir = rotate_block(kt[...], cos_ref, sin_ref)
    weights = softmax_block(scores_of(queries, key_rows))
    rounded = weights.astype(jnp.bfloat16)
    primal = jnp.dot(rounded, v[...], preferred_element_type=jnp.float32)
    score_dir = (
        lax.dot_general(query_dir, key_rows, (((1,), (1,)), ((), ())), preferred_element_type=jnp.float32)
        + lax.dot_general(queries, key_dir, (((1,), (1,)), ((), ())), preferred_element_type=jnp.float32)
    ) * SCORE_SCALE
    weight_dir = weights * (score_dir - jnp.sum(weights * score_dir, axis=-1, keepdims=True))
    tangent = jnp.dot(weight_dir.astype(jnp.bfloat16), v[...], preferred_element_type=jnp.float32) + jnp.dot(
        rounded, vt[...], preferred_element_type=jnp.float32
    )
    term_ref[...] = (scal[0] * primal - scal[1] * tangent).astype(jnp.bfloat16)
    att_ref[...] = primal.astype(jnp.bfloat16)


def head_call(kernel, scal, tables, operands, outputs):
    seq, cols = outputs[0].shape
    heads = cols // HD
    head_block = pl.BlockSpec((seq, HD), lambda h: (0, h))
    table_block = pl.BlockSpec((seq, HD), lambda h: (0, 0))
    in_specs = [pl.BlockSpec(memory_space=pltpu.SMEM), table_block, table_block]
    for operand in operands:
        if operand.ndim == 2:
            in_specs.append(head_block)
        else:
            in_specs.append(pl.BlockSpec((None, seq, HD), lambda h, s=operand.index: (s, 0, h)))
    return pl.pallas_call(
        kernel,
        grid=(heads,),
        in_specs=in_specs,
        out_specs=[head_block] * len(outputs),
        out_shape=outputs,
        compiler_params=pltpu.CompilerParams(dimension_semantics=("arbitrary",)),
    )(scal, *tables, *[o.array for o in operands])


class Operand:
    def __init__(self, array, index=None):
        self.array = array
        self.index = index
        self.ndim = 2 if index is None else 3


def local(
    t_index,
    cond_slot,
    positions,
    latent,
    teacher_query,
    teacher_key,
    teacher_value,
    student_query,
    student_key,
    student_value,
    query_tangent,
    key_tangent,
    value_tangent,
    teacher_out,
    student_out,
):
    groups = lax.axis_size("tensor")
    seq_local = latent.shape[1]
    seq_whole = seq_local * groups
    row_start = lax.axis_index("tensor") * seq_local
    time_value = 0.2 + 1.2 * (t_index[0].astype(jnp.float32) + 0.5) / STEPS
    cos_time = jnp.cos(time_value)
    sin_time = jnp.sin(time_value)
    angles_whole = rope_angles(positions[0])
    tables = rope_tables(angles_whole)
    arrived = [
        lax.all_to_all(source[0], "tensor", split_axis=1, concat_axis=0, tiled=True)
        for source in (student_query, student_key, student_value, query_tangent, key_tangent, value_tangent)
    ]
    cols = arrived[0].shape[1]
    teacher_scal = jnp.stack(
        [cos_time * cos_time * sigma_data, cond_slot[0].astype(jnp.float32)]
    )
    t_q = teacher_query.reshape((2,) + teacher_query.shape[2:])
    t_k = teacher_key.reshape((2,) + teacher_key.shape[2:])
    t_v = teacher_value.reshape((2,) + teacher_value.shape[2:])
    (teacher_term,) = head_call(
        teacher_kernel,
        teacher_scal,
        tables,
        [Operand(t_q, 0), Operand(t_k, 0), Operand(t_v, 0), Operand(t_q, 1), Operand(t_k, 1), Operand(t_v, 1)],
        [jax.ShapeDtypeStruct((seq_whole, cols), jnp.bfloat16)],
    )
    student_scal = jnp.stack(
        [-(cos_time * cos_time) * sigma_data, cos_time * sin_time * sigma_data]
    )
    student_term, attended = head_call(
        student_kernel,
        student_scal,
        tables,
        [Operand(a) for a in arrived],
        [jax.ShapeDtypeStruct((seq_whole, cols), jnp.bfloat16)] * 2,
    )
    stacked = jnp.stack([student_out, teacher_out])
    pieces = lax.all_gather(stacked, "dp", axis=2, tiled=True)
    latent_weight = cos_time * sin_time
    bounds = (0, pieces.shape[2] // 4, pieces.shape[2])
    target_parts = []
    for part in range(2):
        chosen = slice(bounds[part], bounds[part + 1])
        partial_value = jnp.dot(
            student_term, pieces[0, :, chosen], preferred_element_type=jnp.float32
        ) + jnp.dot(teacher_term, pieces[1, :, chosen], preferred_element_type=jnp.float32)
        pieces_in = lax.all_to_all(
            partial_value.astype(jnp.bfloat16).reshape(groups, seq_local, -1),
            "tensor",
            split_axis=0,
            concat_axis=0,
            tiled=True,
        )
        velocity = jnp.sum(pieces_in.astype(jnp.float32), axis=0)
        target_parts.append(
            (velocity - latent_weight * latent[0, :, chosen].astype(jnp.float32)).astype(jnp.bfloat16)
        )
    target = jnp.concatenate(target_parts, axis=1)
    clips = lax.axis_size("dp")
    width = target.shape[1] // clips
    attended_all = lax.all_gather(attended, "dp", axis=0, tiled=False)
    grad_scale = -2.0 / math.sqrt(clips * seq_whole)
    half = width // 2
    split_target = target.reshape(seq_local, clips, width)
    pieces = []
    for part in range(2):
        columns = lax.all_to_all(
            split_target[:, :, part * half : (part + 1) * half], "dp", split_axis=1, concat_axis=1, tiled=True
        )
        columns = lax.all_gather(columns, "tensor", axis=0, tiled=True)
        terms = jnp.einsum(
            "csi,scd->cid", attended_all, columns, preferred_element_type=jnp.float32
        )
        pieces.append(jnp.sum((grad_scale * terms).astype(jnp.bfloat16).astype(jnp.float32), axis=0))
    gradient = jnp.concatenate(pieces, axis=1)
    return (target[None], gradient)


def solution(mesh):
    placed = (
        P("dp"),
        P("dp"),
        P("dp", None, None),
        P("dp", "tensor", None),
        P(None, "dp", None, "tensor"),
        P(None, "dp", None, "tensor"),
        P(None, "dp", None, "tensor"),
        P("dp", "tensor", None),
        P("dp", "tensor", None),
        P("dp", "tensor", None),
        P("dp", "tensor", None),
        P("dp", "tensor", None),
        P("dp", "tensor", None),
        P("tensor", "dp"),
        P("tensor", "dp"),
    )
    return jax.shard_map(
        local,
        mesh=mesh,
        in_specs=placed,
        out_specs=(P("dp", "tensor", None), P("tensor", "dp")),
        check_vma=False,
    )
```

```python
import math

import jax
import jax.numpy as jnp
from jax import lax
from jax.experimental import pallas as pl
from jax.experimental.pallas import tpu as pltpu
from jax.sharding import PartitionSpec as P

HD = 128
STEPS = 1000


sigma_data = 0.5
guidance = 5.0


def rope_angles(coords):
    half_size = HD // 2
    sixth = HD // 6
    first_pairs = half_size - 2 * sixth
    pair_index = jnp.arange(half_size)
    axis_id = (pair_index >= first_pairs).astype(jnp.int32) + (
        pair_index >= first_pairs + sixth
    ).astype(jnp.int32)
    offset = jnp.where(axis_id == 0, 0, jnp.where(axis_id == 1, first_pairs, first_pairs + sixth))
    axis_width = jnp.where(axis_id == 0, 2 * first_pairs, 2 * sixth)
    exponent = 2.0 * (pair_index - offset).astype(jnp.float32) / axis_width.astype(jnp.float32)
    frequency = jnp.exp(-exponent * math.log(10000.0))
    angles = jnp.zeros((coords.shape[1], half_size), jnp.float32)
    for which_axis in range(3):
        chosen = jnp.where(axis_id == which_axis, frequency, 0.0)
        angles = angles + coords[which_axis].astype(jnp.float32)[:, None] * chosen[None, :]
    return angles


def rotate_heads(source, angles):
    half_size = source.shape[-1] // 2
    cos_angle = jnp.cos(angles)[:, None, :]
    sin_angle = jnp.sin(angles)[:, None, :]
    front_half = source[..., :half_size]
    back_half = source[..., half_size:]
    return jnp.concatenate(
        [
            front_half * cos_angle - back_half * sin_angle,
            back_half * cos_angle + front_half * sin_angle,
        ],
        axis=-1,
    )


def split_heads(source):
    return source.reshape(source.shape[0], -1, HD)


def rotated(source, angles):
    row_count = source.shape[0]
    return (
        rotate_heads(split_heads(source).astype(jnp.float32), angles)
        .astype(jnp.bfloat16)
        .reshape(row_count, -1)
    )


def softmax_rows(scores):
    row_peak = jnp.max(scores, axis=-1, keepdims=True)
    exponent = jnp.exp(scores - row_peak)
    return exponent / jnp.sum(exponent, axis=-1, keepdims=True)


def attend_plain(queries, key_rows, value_rows):
    scores = jnp.einsum(
        "qhd,khd->hqk", queries, key_rows, preferred_element_type=jnp.float32
    ) * HD ** (-0.5)
    rounded = softmax_rows(scores).astype(jnp.bfloat16)
    return jnp.einsum("hqk,khd->qhd", rounded, value_rows, preferred_element_type=jnp.float32)


def attend_tangent(queries, key_rows, value_rows, query_dir, key_dir, value_dir):
    score_scale = HD ** (-0.5)
    scores = (
        jnp.einsum("qhd,khd->hqk", queries, key_rows, preferred_element_type=jnp.float32)
        * score_scale
    )
    weights = softmax_rows(scores)
    rounded = weights.astype(jnp.bfloat16)
    primal = jnp.einsum("hqk,khd->qhd", rounded, value_rows, preferred_element_type=jnp.float32)
    score_dir = (
        jnp.einsum("qhd,khd->hqk", query_dir, key_rows, preferred_element_type=jnp.float32)
        + jnp.einsum("qhd,khd->hqk", queries, key_dir, preferred_element_type=jnp.float32)
    ) * score_scale
    weight_dir = weights * (score_dir - jnp.sum(weights * score_dir, axis=-1, keepdims=True))
    rounded_dir = weight_dir.astype(jnp.bfloat16)
    tangent = jnp.einsum(
        "hqk,khd->qhd", rounded_dir, value_rows, preferred_element_type=jnp.float32
    ) + jnp.einsum("hqk,khd->qhd", rounded, value_dir, preferred_element_type=jnp.float32)
    return (primal, tangent)


SCORE_SCALE = HD ** (-0.5)


def rope_tables(angles):
    cos_angle = jnp.cos(angles)
    sin_angle = jnp.sin(angles)
    return (
        jnp.concatenate([cos_angle, cos_angle], axis=-1),
        jnp.concatenate([-sin_angle, sin_angle], axis=-1),
    )


def rotate_block(block, cos_ref, sin_ref):
    source = block.astype(jnp.float32)
    swapped = pltpu.roll(source, HD // 2, 1)
    return (source * cos_ref[...] + swapped * sin_ref[...]).astype(jnp.bfloat16)


def scores_of(queries, key_rows):
    return (
        lax.dot_general(
            queries, key_rows, (((1,), (1,)), ((), ())), preferred_element_type=jnp.float32
        )
        * SCORE_SCALE
    )


def softmax_block(scores):
    exponent = jnp.exp(scores - jnp.max(scores, axis=-1, keepdims=True))
    return exponent / jnp.sum(exponent, axis=-1, keepdims=True)


def teacher_kernel(scal, cos_ref, sin_ref, q0, k0, v0, q1, k1, v1, out_ref):
    def attend(q_ref, k_ref, v_ref):
        weights = softmax_block(
            scores_of(rotate_block(q_ref[...], cos_ref, sin_ref), rotate_block(k_ref[...], cos_ref, sin_ref))
        )
        return jnp.dot(weights.astype(jnp.bfloat16), v_ref[...], preferred_element_type=jnp.float32)

    first = attend(q0, k0, v0)
    second = attend(q1, k1, v1)
    pick_first = scal[1] == 0.0
    cond_out = jnp.where(pick_first, first, second)
    uncond_out = jnp.where(pick_first, second, first)
    out_ref[...] = (scal[0] * (uncond_out + guidance * (cond_out - uncond_out))).astype(jnp.bfloat16)


def student_kernel(scal, cos_ref, sin_ref, q, k, v, qt, kt, vt, term_ref, att_ref):
    queries = rotate_block(q[...], cos_ref, sin_ref)
    key_rows = rotate_block(k[...], cos_ref, sin_ref)
    query_dir = rotate_block(qt[...], cos_ref, sin_ref)
    key_dir = rotate_block(kt[...], cos_ref, sin_ref)
    weights = softmax_block(scores_of(queries, key_rows))
    rounded = weights.astype(jnp.bfloat16)
    primal = jnp.dot(rounded, v[...], preferred_element_type=jnp.float32)
    score_dir = (
        lax.dot_general(query_dir, key_rows, (((1,), (1,)), ((), ())), preferred_element_type=jnp.float32)
        + lax.dot_general(queries, key_dir, (((1,), (1,)), ((), ())), preferred_element_type=jnp.float32)
    ) * SCORE_SCALE
    weight_dir = weights * (score_dir - jnp.sum(weights * score_dir, axis=-1, keepdims=True))
    tangent = jnp.dot(weight_dir.astype(jnp.bfloat16), v[...], preferred_element_type=jnp.float32) + jnp.dot(
        rounded, vt[...], preferred_element_type=jnp.float32
    )
    term_ref[...] = (scal[0] * primal - scal[1] * tangent).astype(jnp.bfloat16)
    att_ref[...] = primal.astype(jnp.bfloat16)


def head_call(kernel, scal, tables, operands, outputs):
    seq, cols = outputs[0].shape
    heads = cols // HD
    head_block = pl.BlockSpec((seq, HD), lambda h: (0, h))
    table_block = pl.BlockSpec((seq, HD), lambda h: (0, 0))
    in_specs = [pl.BlockSpec(memory_space=pltpu.SMEM), table_block, table_block]
    for operand in operands:
        if operand.ndim == 2:
            in_specs.append(head_block)
        else:
            in_specs.append(pl.BlockSpec((None, seq, HD), lambda h, s=operand.index: (s, 0, h)))
    return pl.pallas_call(
        kernel,
        grid=(heads,),
        in_specs=in_specs,
        out_specs=[head_block] * len(outputs),
        out_shape=outputs,
        compiler_params=pltpu.CompilerParams(dimension_semantics=("arbitrary",)),
    )(scal, *tables, *[o.array for o in operands])


class Operand:
    def __init__(self, array, index=None):
        self.array = array
        self.index = index
        self.ndim = 2 if index is None else 3


def local(
    t_index,
    cond_slot,
    positions,
    latent,
    teacher_query,
    teacher_key,
    teacher_value,
    student_query,
    student_key,
    student_value,
    query_tangent,
    key_tangent,
    value_tangent,
    teacher_out,
    student_out,
):
    groups = lax.axis_size("tensor")
    seq_local = latent.shape[1]
    seq_whole = seq_local * groups
    row_start = lax.axis_index("tensor") * seq_local
    time_value = 0.2 + 1.2 * (t_index[0].astype(jnp.float32) + 0.5) / STEPS
    cos_time = jnp.cos(time_value)
    sin_time = jnp.sin(time_value)
    angles_whole = rope_angles(positions[0])
    tables = rope_tables(angles_whole)
    arrived = [
        lax.all_to_all(source[0], "tensor", split_axis=1, concat_axis=0, tiled=True)
        for source in (student_query, student_key, student_value, query_tangent, key_tangent, value_tangent)
    ]
    cols = arrived[0].shape[1]
    teacher_scal = jnp.stack(
        [cos_time * cos_time * sigma_data, cond_slot[0].astype(jnp.float32)]
    )
    t_q = teacher_query.reshape((2,) + teacher_query.shape[2:])
    t_k = teacher_key.reshape((2,) + teacher_key.shape[2:])
    t_v = teacher_value.reshape((2,) + teacher_value.shape[2:])
    (teacher_term,) = head_call(
        teacher_kernel,
        teacher_scal,
        tables,
        [Operand(t_q, 0), Operand(t_k, 0), Operand(t_v, 0), Operand(t_q, 1), Operand(t_k, 1), Operand(t_v, 1)],
        [jax.ShapeDtypeStruct((seq_whole, cols), jnp.bfloat16)],
    )
    student_scal = jnp.stack(
        [-(cos_time * cos_time) * sigma_data, cos_time * sin_time * sigma_data]
    )
    student_term, attended = head_call(
        student_kernel,
        student_scal,
        tables,
        [Operand(a) for a in arrived],
        [jax.ShapeDtypeStruct((seq_whole, cols), jnp.bfloat16)] * 2,
    )
    stacked = jnp.stack([student_out, teacher_out])
    pieces = lax.all_gather(stacked, "dp", axis=2, tiled=True)
    latent_weight = cos_time * sin_time
    bounds = (0, pieces.shape[2] // 4, pieces.shape[2])
    target_parts = []
    for part in range(2):
        chosen = slice(bounds[part], bounds[part + 1])
        partial_value = jnp.dot(
            student_term, pieces[0, :, chosen], preferred_element_type=jnp.float32
        ) + jnp.dot(teacher_term, pieces[1, :, chosen], preferred_element_type=jnp.float32)
        pieces_in = lax.all_to_all(
            partial_value.astype(jnp.bfloat16).reshape(groups, seq_local, -1),
            "tensor",
            split_axis=0,
            concat_axis=0,
            tiled=True,
        )
        velocity = jnp.sum(pieces_in.astype(jnp.float32), axis=0)
        target_parts.append(
            (velocity - latent_weight * latent[0, :, chosen].astype(jnp.float32)).astype(jnp.bfloat16)
        )
    target = jnp.concatenate(target_parts, axis=1)
    clips = lax.axis_size("dp")
    width = target.shape[1] // clips
    attended_all = lax.all_gather(attended, "dp", axis=0, tiled=False)
    grad_scale = -2.0 / math.sqrt(clips * seq_whole)
    edges = (0, width * 2 // 5, width)
    split_target = target.reshape(seq_local, clips, width)
    pieces = []
    for part in range(2):
        columns = lax.all_to_all(
            split_target[:, :, edges[part] : edges[part + 1]], "dp", split_axis=1, concat_axis=1, tiled=True
        )
        columns = lax.all_gather(columns, "tensor", axis=0, tiled=True)
        terms = jnp.einsum(
            "csi,scd->cid", attended_all, columns, preferred_element_type=jnp.float32
        )
        pieces.append(jnp.sum((grad_scale * terms).astype(jnp.bfloat16).astype(jnp.float32), axis=0))
    gradient = jnp.concatenate(pieces, axis=1)
    return (target[None], gradient)


def solution(mesh):
    placed = (
        P("dp"),
        P("dp"),
        P("dp", None, None),
        P("dp", "tensor", None),
        P(None, "dp", None, "tensor"),
        P(None, "dp", None, "tensor"),
        P(None, "dp", None, "tensor"),
        P("dp", "tensor", None),
        P("dp", "tensor", None),
        P("dp", "tensor", None),
        P("dp", "tensor", None),
        P("dp", "tensor", None),
        P("dp", "tensor", None),
        P("tensor", "dp"),
        P("tensor", "dp"),
    )
    return jax.shard_map(
        local,
        mesh=mesh,
        in_specs=placed,
        out_specs=(P("dp", "tensor", None), P("tensor", "dp")),
        check_vma=False,
    )
```

```python
import math

import jax
import jax.numpy as jnp
from jax import lax
from jax.experimental import pallas as pl
from jax.experimental.pallas import tpu as pltpu
from jax.sharding import PartitionSpec as P

HD = 128
STEPS = 1000


sigma_data = 0.5
guidance = 5.0


def rope_angles(coords):
    half_size = HD // 2
    sixth = HD // 6
    first_pairs = half_size - 2 * sixth
    pair_index = jnp.arange(half_size)
    axis_id = (pair_index >= first_pairs).astype(jnp.int32) + (
        pair_index >= first_pairs + sixth
    ).astype(jnp.int32)
    offset = jnp.where(axis_id == 0, 0, jnp.where(axis_id == 1, first_pairs, first_pairs + sixth))
    axis_width = jnp.where(axis_id == 0, 2 * first_pairs, 2 * sixth)
    exponent = 2.0 * (pair_index - offset).astype(jnp.float32) / axis_width.astype(jnp.float32)
    frequency = jnp.exp(-exponent * math.log(10000.0))
    angles = jnp.zeros((coords.shape[1], half_size), jnp.float32)
    for which_axis in range(3):
        chosen = jnp.where(axis_id == which_axis, frequency, 0.0)
        angles = angles + coords[which_axis].astype(jnp.float32)[:, None] * chosen[None, :]
    return angles


def rotate_heads(source, angles):
    half_size = source.shape[-1] // 2
    cos_angle = jnp.cos(angles)[:, None, :]
    sin_angle = jnp.sin(angles)[:, None, :]
    front_half = source[..., :half_size]
    back_half = source[..., half_size:]
    return jnp.concatenate(
        [
            front_half * cos_angle - back_half * sin_angle,
            back_half * cos_angle + front_half * sin_angle,
        ],
        axis=-1,
    )


def split_heads(source):
    return source.reshape(source.shape[0], -1, HD)


def rotated(source, angles):
    row_count = source.shape[0]
    return (
        rotate_heads(split_heads(source).astype(jnp.float32), angles)
        .astype(jnp.bfloat16)
        .reshape(row_count, -1)
    )


def softmax_rows(scores):
    row_peak = jnp.max(scores, axis=-1, keepdims=True)
    exponent = jnp.exp(scores - row_peak)
    return exponent / jnp.sum(exponent, axis=-1, keepdims=True)


def attend_plain(queries, key_rows, value_rows):
    scores = jnp.einsum(
        "qhd,khd->hqk", queries, key_rows, preferred_element_type=jnp.float32
    ) * HD ** (-0.5)
    rounded = softmax_rows(scores).astype(jnp.bfloat16)
    return jnp.einsum("hqk,khd->qhd", rounded, value_rows, preferred_element_type=jnp.float32)


def attend_tangent(queries, key_rows, value_rows, query_dir, key_dir, value_dir):
    score_scale = HD ** (-0.5)
    scores = (
        jnp.einsum("qhd,khd->hqk", queries, key_rows, preferred_element_type=jnp.float32)
        * score_scale
    )
    weights = softmax_rows(scores)
    rounded = weights.astype(jnp.bfloat16)
    primal = jnp.einsum("hqk,khd->qhd", rounded, value_rows, preferred_element_type=jnp.float32)
    score_dir = (
        jnp.einsum("qhd,khd->hqk", query_dir, key_rows, preferred_element_type=jnp.float32)
        + jnp.einsum("qhd,khd->hqk", queries, key_dir, preferred_element_type=jnp.float32)
    ) * score_scale
    weight_dir = weights * (score_dir - jnp.sum(weights * score_dir, axis=-1, keepdims=True))
    rounded_dir = weight_dir.astype(jnp.bfloat16)
    tangent = jnp.einsum(
        "hqk,khd->qhd", rounded_dir, value_rows, preferred_element_type=jnp.float32
    ) + jnp.einsum("hqk,khd->qhd", rounded, value_dir, preferred_element_type=jnp.float32)
    return (primal, tangent)


SCORE_SCALE = HD ** (-0.5)


def rope_tables(angles):
    cos_angle = jnp.cos(angles)
    sin_angle = jnp.sin(angles)
    return (
        jnp.concatenate([cos_angle, cos_angle], axis=-1),
        jnp.concatenate([-sin_angle, sin_angle], axis=-1),
    )


def rotate_block(block, cos_ref, sin_ref):
    source = block.astype(jnp.float32)
    swapped = pltpu.roll(source, HD // 2, 1)
    return (source * cos_ref[...] + swapped * sin_ref[...]).astype(jnp.bfloat16)


def scores_of(queries, key_rows):
    return (
        lax.dot_general(
            queries, key_rows, (((1,), (1,)), ((), ())), preferred_element_type=jnp.float32
        )
        * SCORE_SCALE
    )


def softmax_block(scores):
    exponent = jnp.exp(scores - jnp.max(scores, axis=-1, keepdims=True))
    return exponent / jnp.sum(exponent, axis=-1, keepdims=True)


def teacher_kernel(scal, cos_ref, sin_ref, q0, k0, v0, q1, k1, v1, out_ref):
    def attend(q_ref, k_ref, v_ref):
        weights = softmax_block(
            scores_of(rotate_block(q_ref[...], cos_ref, sin_ref), rotate_block(k_ref[...], cos_ref, sin_ref))
        )
        return jnp.dot(weights.astype(jnp.bfloat16), v_ref[...], preferred_element_type=jnp.float32)

    first = attend(q0, k0, v0)
    second = attend(q1, k1, v1)
    pick_first = scal[1] == 0.0
    cond_out = jnp.where(pick_first, first, second)
    uncond_out = jnp.where(pick_first, second, first)
    out_ref[...] = (scal[0] * (uncond_out + guidance * (cond_out - uncond_out))).astype(jnp.bfloat16)


def student_kernel(scal, cos_ref, sin_ref, q, k, v, qt, kt, vt, term_ref, att_ref):
    queries = rotate_block(q[...], cos_ref, sin_ref)
    key_rows = rotate_block(k[...], cos_ref, sin_ref)
    query_dir = rotate_block(qt[...], cos_ref, sin_ref)
    key_dir = rotate_block(kt[...], cos_ref, sin_ref)
    weights = softmax_block(scores_of(queries, key_rows))
    rounded = weights.astype(jnp.bfloat16)
    primal = jnp.dot(rounded, v[...], preferred_element_type=jnp.float32)
    score_dir = (
        lax.dot_general(query_dir, key_rows, (((1,), (1,)), ((), ())), preferred_element_type=jnp.float32)
        + lax.dot_general(queries, key_dir, (((1,), (1,)), ((), ())), preferred_element_type=jnp.float32)
    ) * SCORE_SCALE
    weight_dir = weights * (score_dir - jnp.sum(weights * score_dir, axis=-1, keepdims=True))
    tangent = jnp.dot(weight_dir.astype(jnp.bfloat16), v[...], preferred_element_type=jnp.float32) + jnp.dot(
        rounded, vt[...], preferred_element_type=jnp.float32
    )
    term_ref[...] = (scal[0] * primal - scal[1] * tangent).astype(jnp.bfloat16)
    att_ref[...] = primal.astype(jnp.bfloat16)


def head_call(kernel, scal, tables, operands, outputs):
    seq, cols = outputs[0].shape
    heads = cols // HD
    head_block = pl.BlockSpec((seq, HD), lambda h: (0, h))
    table_block = pl.BlockSpec((seq, HD), lambda h: (0, 0))
    in_specs = [pl.BlockSpec(memory_space=pltpu.SMEM), table_block, table_block]
    for operand in operands:
        if operand.ndim == 2:
            in_specs.append(head_block)
        else:
            in_specs.append(pl.BlockSpec((None, seq, HD), lambda h, s=operand.index: (s, 0, h)))
    return pl.pallas_call(
        kernel,
        grid=(heads,),
        in_specs=in_specs,
        out_specs=[head_block] * len(outputs),
        out_shape=outputs,
        compiler_params=pltpu.CompilerParams(dimension_semantics=("arbitrary",)),
    )(scal, *tables, *[o.array for o in operands])


class Operand:
    def __init__(self, array, index=None):
        self.array = array
        self.index = index
        self.ndim = 2 if index is None else 3


def local(
    t_index,
    cond_slot,
    positions,
    latent,
    teacher_query,
    teacher_key,
    teacher_value,
    student_query,
    student_key,
    student_value,
    query_tangent,
    key_tangent,
    value_tangent,
    teacher_out,
    student_out,
):
    groups = lax.axis_size("tensor")
    seq_local = latent.shape[1]
    seq_whole = seq_local * groups
    row_start = lax.axis_index("tensor") * seq_local
    time_value = 0.2 + 1.2 * (t_index[0].astype(jnp.float32) + 0.5) / STEPS
    cos_time = jnp.cos(time_value)
    sin_time = jnp.sin(time_value)
    angles_whole = rope_angles(positions[0])
    tables = rope_tables(angles_whole)
    arrived = [
        lax.all_to_all(source[0], "tensor", split_axis=1, concat_axis=0, tiled=True)
        for source in (student_query, student_key, student_value, query_tangent, key_tangent, value_tangent)
    ]
    cols = arrived[0].shape[1]
    teacher_scal = jnp.stack(
        [cos_time * cos_time * sigma_data, cond_slot[0].astype(jnp.float32)]
    )
    t_q = teacher_query.reshape((2,) + teacher_query.shape[2:])
    t_k = teacher_key.reshape((2,) + teacher_key.shape[2:])
    t_v = teacher_value.reshape((2,) + teacher_value.shape[2:])
    (teacher_term,) = head_call(
        teacher_kernel,
        teacher_scal,
        tables,
        [Operand(t_q, 0), Operand(t_k, 0), Operand(t_v, 0), Operand(t_q, 1), Operand(t_k, 1), Operand(t_v, 1)],
        [jax.ShapeDtypeStruct((seq_whole, cols), jnp.bfloat16)],
    )
    student_scal = jnp.stack(
        [-(cos_time * cos_time) * sigma_data, cos_time * sin_time * sigma_data]
    )
    student_term, attended = head_call(
        student_kernel,
        student_scal,
        tables,
        [Operand(a) for a in arrived],
        [jax.ShapeDtypeStruct((seq_whole, cols), jnp.bfloat16)] * 2,
    )
    stacked = jnp.stack([student_out, teacher_out])
    pieces = lax.all_gather(stacked, "dp", axis=2, tiled=True)
    latent_weight = cos_time * sin_time
    bounds = (0, pieces.shape[2] // 4, pieces.shape[2])
    target_parts = []
    for part in range(2):
        chosen = slice(bounds[part], bounds[part + 1])
        partial_value = jnp.dot(
            student_term, pieces[0, :, chosen], preferred_element_type=jnp.float32
        ) + jnp.dot(teacher_term, pieces[1, :, chosen], preferred_element_type=jnp.float32)
        pieces_in = lax.all_to_all(
            partial_value.astype(jnp.bfloat16).reshape(groups, seq_local, -1),
            "tensor",
            split_axis=0,
            concat_axis=0,
            tiled=True,
        )
        if target_parts:
            target_parts[0], pieces_in = lax.optimization_barrier((target_parts[0], pieces_in))
        velocity = jnp.sum(pieces_in.astype(jnp.float32), axis=0)
        target_parts.append(
            (velocity - latent_weight * latent[0, :, chosen].astype(jnp.float32)).astype(jnp.bfloat16)
        )
    target = jnp.concatenate(target_parts, axis=1)
    clips = lax.axis_size("dp")
    width = target.shape[1] // clips
    attended_all = lax.all_gather(attended, "dp", axis=0, tiled=False)
    grad_scale = -2.0 / math.sqrt(clips * seq_whole)
    edges = (0, width * 2 // 5, width)
    split_target = target.reshape(seq_local, clips, width)
    pieces = []
    for part in range(2):
        columns = lax.all_to_all(
            split_target[:, :, edges[part] : edges[part + 1]], "dp", split_axis=1, concat_axis=1, tiled=True
        )
        columns = lax.all_gather(columns, "tensor", axis=0, tiled=True)
        terms = jnp.einsum(
            "csi,scd->cid", attended_all, columns, preferred_element_type=jnp.float32
        )
        pieces.append(jnp.sum((grad_scale * terms).astype(jnp.bfloat16).astype(jnp.float32), axis=0))
    gradient = jnp.concatenate(pieces, axis=1)
    return (target[None], gradient)


def solution(mesh):
    placed = (
        P("dp"),
        P("dp"),
        P("dp", None, None),
        P("dp", "tensor", None),
        P(None, "dp", None, "tensor"),
        P(None, "dp", None, "tensor"),
        P(None, "dp", None, "tensor"),
        P("dp", "tensor", None),
        P("dp", "tensor", None),
        P("dp", "tensor", None),
        P("dp", "tensor", None),
        P("dp", "tensor", None),
        P("dp", "tensor", None),
        P("tensor", "dp"),
        P("tensor", "dp"),
    )
    return jax.shard_map(
        local,
        mesh=mesh,
        in_specs=placed,
        out_specs=(P("dp", "tensor", None), P("tensor", "dp")),
        check_vma=False,
    )
```

```python
import math

import jax
import jax.numpy as jnp
from jax import lax
from jax.experimental import pallas as pl
from jax.experimental.pallas import tpu as pltpu
from jax.sharding import PartitionSpec as P

HD = 128
STEPS = 1000


sigma_data = 0.5
guidance = 5.0


def rope_angles(coords):
    half_size = HD // 2
    sixth = HD // 6
    first_pairs = half_size - 2 * sixth
    pair_index = jnp.arange(half_size)
    axis_id = (pair_index >= first_pairs).astype(jnp.int32) + (
        pair_index >= first_pairs + sixth
    ).astype(jnp.int32)
    offset = jnp.where(axis_id == 0, 0, jnp.where(axis_id == 1, first_pairs, first_pairs + sixth))
    axis_width = jnp.where(axis_id == 0, 2 * first_pairs, 2 * sixth)
    exponent = 2.0 * (pair_index - offset).astype(jnp.float32) / axis_width.astype(jnp.float32)
    frequency = jnp.exp(-exponent * math.log(10000.0))
    angles = jnp.zeros((coords.shape[1], half_size), jnp.float32)
    for which_axis in range(3):
        chosen = jnp.where(axis_id == which_axis, frequency, 0.0)
        angles = angles + coords[which_axis].astype(jnp.float32)[:, None] * chosen[None, :]
    return angles


def rotate_heads(source, angles):
    half_size = source.shape[-1] // 2
    cos_angle = jnp.cos(angles)[:, None, :]
    sin_angle = jnp.sin(angles)[:, None, :]
    front_half = source[..., :half_size]
    back_half = source[..., half_size:]
    return jnp.concatenate(
        [
            front_half * cos_angle - back_half * sin_angle,
            back_half * cos_angle + front_half * sin_angle,
        ],
        axis=-1,
    )


def split_heads(source):
    return source.reshape(source.shape[0], -1, HD)


def rotated(source, angles):
    row_count = source.shape[0]
    return (
        rotate_heads(split_heads(source).astype(jnp.float32), angles)
        .astype(jnp.bfloat16)
        .reshape(row_count, -1)
    )


def softmax_rows(scores):
    row_peak = jnp.max(scores, axis=-1, keepdims=True)
    exponent = jnp.exp(scores - row_peak)
    return exponent / jnp.sum(exponent, axis=-1, keepdims=True)


def attend_plain(queries, key_rows, value_rows):
    scores = jnp.einsum(
        "qhd,khd->hqk", queries, key_rows, preferred_element_type=jnp.float32
    ) * HD ** (-0.5)
    rounded = softmax_rows(scores).astype(jnp.bfloat16)
    return jnp.einsum("hqk,khd->qhd", rounded, value_rows, preferred_element_type=jnp.float32)


def attend_tangent(queries, key_rows, value_rows, query_dir, key_dir, value_dir):
    score_scale = HD ** (-0.5)
    scores = (
        jnp.einsum("qhd,khd->hqk", queries, key_rows, preferred_element_type=jnp.float32)
        * score_scale
    )
    weights = softmax_rows(scores)
    rounded = weights.astype(jnp.bfloat16)
    primal = jnp.einsum("hqk,khd->qhd", rounded, value_rows, preferred_element_type=jnp.float32)
    score_dir = (
        jnp.einsum("qhd,khd->hqk", query_dir, key_rows, preferred_element_type=jnp.float32)
        + jnp.einsum("qhd,khd->hqk", queries, key_dir, preferred_element_type=jnp.float32)
    ) * score_scale
    weight_dir = weights * (score_dir - jnp.sum(weights * score_dir, axis=-1, keepdims=True))
    rounded_dir = weight_dir.astype(jnp.bfloat16)
    tangent = jnp.einsum(
        "hqk,khd->qhd", rounded_dir, value_rows, preferred_element_type=jnp.float32
    ) + jnp.einsum("hqk,khd->qhd", rounded, value_dir, preferred_element_type=jnp.float32)
    return (primal, tangent)


SCORE_SCALE = HD ** (-0.5)


def rope_tables(angles):
    cos_angle = jnp.cos(angles)
    sin_angle = jnp.sin(angles)
    return (
        jnp.concatenate([cos_angle, cos_angle], axis=-1),
        jnp.concatenate([-sin_angle, sin_angle], axis=-1),
    )


def rotate_block(block, cos_ref, sin_ref):
    source = block.astype(jnp.float32)
    swapped = pltpu.roll(source, HD // 2, 1)
    return (source * cos_ref[...] + swapped * sin_ref[...]).astype(jnp.bfloat16)


def scores_of(queries, key_rows):
    return (
        lax.dot_general(
            queries, key_rows, (((1,), (1,)), ((), ())), preferred_element_type=jnp.float32
        )
        * SCORE_SCALE
    )


def softmax_block(scores):
    exponent = jnp.exp(scores - jnp.max(scores, axis=-1, keepdims=True))
    return exponent / jnp.sum(exponent, axis=-1, keepdims=True)


def teacher_kernel(scal, cos_ref, sin_ref, q0, k0, v0, q1, k1, v1, out_ref):
    def attend(q_ref, k_ref, v_ref):
        weights = softmax_block(
            scores_of(rotate_block(q_ref[...], cos_ref, sin_ref), rotate_block(k_ref[...], cos_ref, sin_ref))
        )
        return jnp.dot(weights.astype(jnp.bfloat16), v_ref[...], preferred_element_type=jnp.float32)

    first = attend(q0, k0, v0)
    second = attend(q1, k1, v1)
    pick_first = scal[1] == 0.0
    cond_out = jnp.where(pick_first, first, second)
    uncond_out = jnp.where(pick_first, second, first)
    out_ref[...] = (scal[0] * (uncond_out + guidance * (cond_out - uncond_out))).astype(jnp.bfloat16)


def student_kernel(scal, cos_ref, sin_ref, q, k, v, qt, kt, vt, term_ref, att_ref):
    queries = rotate_block(q[...], cos_ref, sin_ref)
    key_rows = rotate_block(k[...], cos_ref, sin_ref)
    query_dir = rotate_block(qt[...], cos_ref, sin_ref)
    key_dir = rotate_block(kt[...], cos_ref, sin_ref)
    weights = softmax_block(scores_of(queries, key_rows))
    rounded = weights.astype(jnp.bfloat16)
    primal = jnp.dot(rounded, v[...], preferred_element_type=jnp.float32)
    score_dir = (
        lax.dot_general(query_dir, key_rows, (((1,), (1,)), ((), ())), preferred_element_type=jnp.float32)
        + lax.dot_general(queries, key_dir, (((1,), (1,)), ((), ())), preferred_element_type=jnp.float32)
    ) * SCORE_SCALE
    weight_dir = weights * (score_dir - jnp.sum(weights * score_dir, axis=-1, keepdims=True))
    tangent = jnp.dot(weight_dir.astype(jnp.bfloat16), v[...], preferred_element_type=jnp.float32) + jnp.dot(
        rounded, vt[...], preferred_element_type=jnp.float32
    )
    term_ref[...] = (scal[0] * primal - scal[1] * tangent).astype(jnp.bfloat16)
    att_ref[...] = primal.astype(jnp.bfloat16)


def head_call(kernel, scal, tables, operands, outputs):
    seq, cols = outputs[0].shape
    heads = cols // HD
    head_block = pl.BlockSpec((seq, HD), lambda h: (0, h))
    table_block = pl.BlockSpec((seq, HD), lambda h: (0, 0))
    in_specs = [pl.BlockSpec(memory_space=pltpu.SMEM), table_block, table_block]
    for operand in operands:
        if operand.ndim == 2:
            in_specs.append(head_block)
        else:
            in_specs.append(pl.BlockSpec((None, seq, HD), lambda h, s=operand.index: (s, 0, h)))
    return pl.pallas_call(
        kernel,
        grid=(heads,),
        in_specs=in_specs,
        out_specs=[head_block] * len(outputs),
        out_shape=outputs,
        compiler_params=pltpu.CompilerParams(dimension_semantics=("arbitrary",)),
    )(scal, *tables, *[o.array for o in operands])


class Operand:
    def __init__(self, array, index=None):
        self.array = array
        self.index = index
        self.ndim = 2 if index is None else 3


def local(
    t_index,
    cond_slot,
    positions,
    latent,
    teacher_query,
    teacher_key,
    teacher_value,
    student_query,
    student_key,
    student_value,
    query_tangent,
    key_tangent,
    value_tangent,
    teacher_out,
    student_out,
):
    groups = lax.axis_size("tensor")
    seq_local = latent.shape[1]
    seq_whole = seq_local * groups
    row_start = lax.axis_index("tensor") * seq_local
    time_value = 0.2 + 1.2 * (t_index[0].astype(jnp.float32) + 0.5) / STEPS
    cos_time = jnp.cos(time_value)
    sin_time = jnp.sin(time_value)
    angles_whole = rope_angles(positions[0])
    tables = rope_tables(angles_whole)
    arrived = [
        lax.all_to_all(source[0], "tensor", split_axis=1, concat_axis=0, tiled=True)
        for source in (student_query, student_key, student_value, query_tangent, key_tangent, value_tangent)
    ]
    cols = arrived[0].shape[1]
    teacher_scal = jnp.stack(
        [cos_time * cos_time * sigma_data, cond_slot[0].astype(jnp.float32)]
    )
    t_q = teacher_query.reshape((2,) + teacher_query.shape[2:])
    t_k = teacher_key.reshape((2,) + teacher_key.shape[2:])
    t_v = teacher_value.reshape((2,) + teacher_value.shape[2:])
    (teacher_term,) = head_call(
        teacher_kernel,
        teacher_scal,
        tables,
        [Operand(t_q, 0), Operand(t_k, 0), Operand(t_v, 0), Operand(t_q, 1), Operand(t_k, 1), Operand(t_v, 1)],
        [jax.ShapeDtypeStruct((seq_whole, cols), jnp.bfloat16)],
    )
    student_scal = jnp.stack(
        [-(cos_time * cos_time) * sigma_data, cos_time * sin_time * sigma_data]
    )
    student_term, attended = head_call(
        student_kernel,
        student_scal,
        tables,
        [Operand(a) for a in arrived],
        [jax.ShapeDtypeStruct((seq_whole, cols), jnp.bfloat16)] * 2,
    )
    stacked = jnp.stack([student_out, teacher_out])
    pieces = lax.all_gather(stacked, "dp", axis=2, tiled=True)
    latent_weight = cos_time * sin_time
    bounds = (0, pieces.shape[2] // 4, pieces.shape[2])
    target_parts = []
    for part in range(2):
        chosen = slice(bounds[part], bounds[part + 1])
        partial_value = jnp.dot(
            student_term, pieces[0, :, chosen], preferred_element_type=jnp.float32
        ) + jnp.dot(teacher_term, pieces[1, :, chosen], preferred_element_type=jnp.float32)
        pieces_in = lax.all_to_all(
            partial_value.astype(jnp.bfloat16).reshape(groups, seq_local, -1),
            "tensor",
            split_axis=0,
            concat_axis=0,
            tiled=True,
        )
        velocity = jnp.sum(pieces_in.astype(jnp.float32), axis=0)
        target_parts.append(
            (velocity - latent_weight * latent[0, :, chosen].astype(jnp.float32)).astype(jnp.bfloat16)
        )
    target = jnp.concatenate(target_parts, axis=1)
    clips = lax.axis_size("dp")
    width = target.shape[1] // clips
    attended_all = lax.all_gather(attended, "dp", axis=0, tiled=False)
    grad_scale = -2.0 / math.sqrt(clips * seq_whole)
    edges = (0, width * 2 // 5, width)
    split_target = target.reshape(seq_local, clips, width)
    attended_rows = jnp.swapaxes(attended_all, 1, 2)
    pieces = []
    for part in range(2):
        columns = lax.all_to_all(
            split_target[:, :, edges[part] : edges[part + 1]], "dp", split_axis=1, concat_axis=1, tiled=True
        )
        columns = lax.all_gather(columns, "tensor", axis=0, tiled=True)
        terms = jnp.einsum(
            "cis,scd->cid", attended_rows, columns, preferred_element_type=jnp.float32
        )
        pieces.append(jnp.sum((grad_scale * terms).astype(jnp.bfloat16).astype(jnp.float32), axis=0))
    gradient = jnp.concatenate(pieces, axis=1)
    return (target[None], gradient)


def solution(mesh):
    placed = (
        P("dp"),
        P("dp"),
        P("dp", None, None),
        P("dp", "tensor", None),
        P(None, "dp", None, "tensor"),
        P(None, "dp", None, "tensor"),
        P(None, "dp", None, "tensor"),
        P("dp", "tensor", None),
        P("dp", "tensor", None),
        P("dp", "tensor", None),
        P("dp", "tensor", None),
        P("dp", "tensor", None),
        P("dp", "tensor", None),
        P("tensor", "dp"),
        P("tensor", "dp"),
    )
    return jax.shard_map(
        local,
        mesh=mesh,
        in_specs=placed,
        out_specs=(P("dp", "tensor", None), P("tensor", "dp")),
        check_vma=False,
    )
```
